32 devices in a mesh: groups: 2 (over x), ctx: 8 (over z, y), heads: 2 (over core).
Axes of the slice: x: 2, y: 2, z: 4, core: 2. Of those that a mesh axis runs over, the one named last changes fastest.
Arguments:
- ssm_input: bfloat16 [4, 2048, 8192], P('groups', 'ctx', 'heads'), parts along dimension 0, may hold values from -6 to 6
- b_proj: bfloat16 [4, 2048, 512], P('groups', 'ctx', 'heads'), parts along dimension 0, may hold values from -600 to 600
- c_proj: bfloat16 [4, 2048, 512], P('groups', 'ctx', 'heads'), parts along dimension 0, may hold values from -6 to 6
- step_size: float32 [4, 128, 2048], P('groups', 'heads', 'ctx'), parts along dimension 0, may hold values from 0.01 to 0.04
- log_decay: float32 [4, 128, 2048], P('groups', 'heads', 'ctx'), parts along dimension 0, may hold values from -1 to 0
- skip_gain: float32 [128], P('heads'), may hold values from 0.5 to 1.5
- request_of_slot: int32 [16], P(('groups', 'ctx')), parts along dimension 0, may hold values from 0 to 1, as said below
- new_input: bfloat16 [16, 4, 8192], P(('groups', 'ctx'), None, 'heads'), parts along dimension 0, may hold values from -6 to 6
- new_b: bfloat16 [16, 4, 512], P(('groups', 'ctx'), None, 'heads'), parts along dimension 0, may hold values from -0.5 to 0.5
- new_c: bfloat16 [16, 4, 512], P(('groups', 'ctx'), None, 'heads'), parts along dimension 0, may hold values from -6 to 6
- new_step: float32 [16, 4, 128], P(('groups', 'ctx'), None, 'heads'), parts along dimension 0, may hold values from 0.2 to 1
- new_log_decay: float32 [16, 4, 128], P(('groups', 'ctx'), None, 'heads'), parts along dimension 0, may hold values from -0.3 to -0.02
- out_weight: bfloat16 [8192, 8192], P('heads', 'ctx'), may hold values from -0.0625 to 0.0625
Outputs:
- prefill_out: bfloat16 [4, 2048, 8192], P('groups', 'ctx', 'heads'), parts along dimension 0
- decoded: bfloat16 [16, 4, 8192], P('groups', None, 'ctx'), parts along dimension 0
The draws below stay inside these ranges and needn't reach their ends.
There are 2 independent parts, one for each index of `groups`. The reference program is written for one: setup_inputs(seed, part) draws one part's arguments, and reference() takes and returns one part's arrays. A program takes and returns all parts, laid end to end along the dimension named above; an argument that names none is the same for every part. Nothing has to cross between parts.
Inputs may be any that keep to these rules, and one draw needn't show every extreme that they name: `request_of_slot`: every prompt is named by at least one slot.
All inputs are finite; a program needn't handle non-finite values.
Results may differ from the reference program's by a relative error of at most 0.008.
Values may be sent and summed in bfloat16 or wider, within the bound.
No kernel may reach another device: no remote copies, remote signals or barrier semaphores. Data moves between devices by JAX's collectives and lax.ppermute only.
A program may use at most 320 MiB of HBM per device.

```python
import math
import jax
import jax.numpy as jnp
from jax import lax

D_MODEL = 8192
HEADS = 128
HEAD_DIM = 64
STATE = 128
GROUPS = 4
TOK_DEV = 256
PROMPT_REQUESTS = 2
STEPS = 4
PROMPT_LENGTH = 2048
SLOTS = 8


def loud_layout(key):
    layout_key = jax.random.fold_in(key, 4242)
    layout_keys = jax.random.split(layout_key, 2)
    block_count = PROMPT_LENGTH // TOK_DEV
    loud_block = jax.random.randint(layout_keys[0], (PROMPT_REQUESTS,), 0, block_count - 2).astype(jnp.int32)
    loud_group = jax.random.randint(layout_keys[1], (PROMPT_REQUESTS,), 0, GROUPS).astype(jnp.int32)
    barrier = min(6.0, 0.9 * TOK_DEV)
    position_block = jnp.arange(PROMPT_LENGTH, dtype=jnp.int32) // TOK_DEV
    in_loud = position_block[None, :] == loud_block[:, None]
    in_barrier = position_block[None, :] == loud_block[:, None] + 1
    column_group = jnp.arange(GROUPS * STATE, dtype=jnp.int32) // STATE
    column_loud = column_group[None, :] == loud_group[:, None]
    head_group = jnp.arange(HEADS, dtype=jnp.int32) // (HEADS // GROUPS)
    head_loud = head_group[None, :] == loud_group[:, None]
    return (in_loud, in_barrier, column_loud, head_loud, barrier)


def draw_log_decay(key, part):
    random_keys = jax.random.split(key, 7)
    share = 0.5
    slow_heads = jax.random.uniform(random_keys[0], (PROMPT_REQUESTS, HEADS, 1)) < share
    slow_rate = jnp.exp(jax.random.uniform(random_keys[1], (PROMPT_REQUESTS, HEADS, 1), minval=math.log(0.1), maxval=math.log(0.5))) / PROMPT_LENGTH
    fast_rate = jnp.exp(jax.random.uniform(random_keys[2], (PROMPT_REQUESTS, HEADS, 1), minval=math.log(1.0 / 50.0), maxval=math.log(1.0 / 30.0)))
    baseline_decay_rate = jnp.where(slow_heads, slow_rate, fast_rate)
    approximate_output = jnp.exp(jax.random.uniform(random_keys[3], (PROMPT_REQUESTS, HEADS, PROMPT_LENGTH), minval=math.log(0.5), maxval=math.log(2.0)))
    block_count = PROMPT_LENGTH // TOK_DEV
    block_multiplier = jnp.exp(jax.random.uniform(random_keys[4], (PROMPT_REQUESTS, HEADS, block_count), minval=math.log(0.5), maxval=math.log(2.0)))
    block_multiplier = jnp.repeat(block_multiplier, TOK_DEV, axis=2)
    spike_location = jax.random.randint(random_keys[5], (PROMPT_REQUESTS, 3, 1), 0, PROMPT_LENGTH)
    spike_decay_loss = jax.random.uniform(random_keys[6], (PROMPT_REQUESTS, 3, 1), minval=0.2, maxval=0.4)
    position_indices = jnp.arange(PROMPT_LENGTH, dtype=jnp.int32)[None, None, :]
    decay_spikes = jnp.sum(jnp.where(position_indices == spike_location, jnp.log(1.0 - spike_decay_loss), 0.0), axis=1)[:, None, :]
    decay_value = -baseline_decay_rate * approximate_output * block_multiplier + decay_spikes
    in_loud, in_barrier, column_loud, head_loud, barrier = loud_layout(key)
    loud_here = head_loud[:, :, None] & in_loud[:, None, :]
    barrier_here = head_loud[:, :, None] & in_barrier[:, None, :]
    decay_value = jnp.where(loud_here, -1.5 / TOK_DEV, decay_value)
    decay_value = jnp.where(barrier_here, -barrier / TOK_DEV, decay_value)
    return decay_value.astype(jnp.float32)


def draw_b_proj(key, part):
    draw_keys = jax.random.split(jax.random.fold_in(key, 101), 1)
    array_shape = (PROMPT_REQUESTS, PROMPT_LENGTH, GROUPS * STATE)
    base_values = jnp.clip(jax.random.normal(draw_keys[0], array_shape), -6.0, 6.0)
    in_loud, in_barrier, column_loud, head_loud, barrier = loud_layout(key)
    loud_gain = math.exp(barrier + 1.0)
    boosted = in_loud[:, :, None] & column_loud[:, None, :]
    return (base_values * jnp.where(boosted, loud_gain, 1.0) / math.sqrt(STATE)).astype(jnp.bfloat16)


def draw_c_proj(key, part):
    draw_keys = jax.random.split(jax.random.fold_in(key, 202), 1)
    array_shape = (PROMPT_REQUESTS, PROMPT_LENGTH, GROUPS * STATE)
    base_values = jnp.clip(jax.random.normal(draw_keys[0], array_shape), -6.0, 6.0)
    in_loud, in_barrier, column_loud, head_loud, barrier = loud_layout(key)
    loud_gain = math.exp(barrier + 1.0)
    quieted = (in_loud | in_barrier)[:, :, None] & column_loud[:, None, :]
    return (base_values * jnp.where(quieted, 1.0 / loud_gain, 1.0)).astype(jnp.bfloat16)


def draw_request_of_slot(key, part):
    slot_key = jax.random.fold_in(jax.random.fold_in(key, 7919), part)
    random_keys = jax.random.split(slot_key, 2)
    chosen = jax.random.randint(random_keys[0], (SLOTS,), 0, PROMPT_REQUESTS).astype(jnp.int32)
    order = jax.random.permutation(random_keys[1], jnp.arange(SLOTS, dtype=jnp.int32)).astype(jnp.int32)
    covered = chosen.at[order[:PROMPT_REQUESTS]].set(jnp.arange(PROMPT_REQUESTS, dtype=jnp.int32))
    return covered.astype(jnp.int32)


def block_scale(stream_key, dims, cuts, low, largest):
    level = 1.0
    for dim, blocks in cuts:
        heights = jax.random.uniform(jax.random.fold_in(jax.random.fold_in(stream_key, 6), dim), (blocks,), jnp.float32, low / len(cuts), largest / len(cuts))
        level = level * jnp.repeat(jnp.exp(heights), dims[dim] // blocks).reshape((-1,) + (1,) * (len(dims) - 1 - dim))
    return level


def gaussian(rng, shape, width, limit, shards=(), kind=jnp.bfloat16):
    values = jax.random.normal(rng, shape, jnp.float32) * width
    if len(shards) > 0:
        values = block_scale(rng, shape, shards, -0.22, 0.18) * values
    return jnp.clip(values, min=-limit, max=limit).astype(kind)


def setup_inputs(seed: int = 0, part: int = 0) -> dict:
    seeds = jax.random.split(jax.random.key(seed), 14)
    part_splits = jax.random.split(jax.random.fold_in(seeds[13], part), 14)
    ssm_input = gaussian(part_splits[0], (PROMPT_REQUESTS, PROMPT_LENGTH, HEADS * HEAD_DIM), 1.0, 6.0, ((1, 8), (2, 2)))
    b_proj = draw_b_proj(jax.random.fold_in(jax.random.fold_in(seeds[13], part), 71), part)
    c_proj = draw_c_proj(jax.random.fold_in(jax.random.fold_in(seeds[13], part), 71), part)
    step_size = jnp.clip(jnp.exp(math.log(0.04) - 1.3862944 * jax.random.uniform(part_splits[3], (PROMPT_REQUESTS, HEADS, PROMPT_LENGTH), jnp.float32) ** block_scale(part_splits[3], (PROMPT_REQUESTS, HEADS, PROMPT_LENGTH), ((1, 2), (2, 8)), -0.2, 0.2)), 0.01, 0.04)
    log_decay = draw_log_decay(jax.random.fold_in(jax.random.fold_in(seeds[13], part), 71), part)
    skip_gain = jnp.clip(0.5 + 1.0 * jax.random.uniform(seeds[5], (HEADS,), jnp.float32) ** block_scale(seeds[5], (HEADS,), ((0, 2),), -0.2, 0.2), 0.5, 1.5)
    request_of_slot = draw_request_of_slot(jax.random.fold_in(jax.random.fold_in(seeds[13], part), 71), part)
    new_input = gaussian(part_splits[7], (SLOTS, STEPS, HEADS * HEAD_DIM), 1.0, 6.0, ((0, 8), (2, 2)))
    new_b = gaussian(part_splits[8], (SLOTS, STEPS, GROUPS * STATE), STATE ** -0.5, 0.5, ((0, 8), (2, 2)))
    new_c = gaussian(part_splits[9], (SLOTS, STEPS, GROUPS * STATE), 1.0, 6.0, ((0, 8), (2, 2)))
    new_step = jnp.clip(jnp.exp(math.log(1.0) - 1.609438 * jax.random.uniform(part_splits[10], (SLOTS, STEPS, HEADS), jnp.float32) ** block_scale(part_splits[10], (SLOTS, STEPS, HEADS), ((0, 8), (2, 2)), -0.2, 0.2)), 0.2, 1.0)
    new_log_decay = jnp.clip(-0.3 + 0.28 * jax.random.uniform(part_splits[11], (SLOTS, STEPS, HEADS), jnp.float32) ** block_scale(part_splits[11], (SLOTS, STEPS, HEADS), ((0, 8), (2, 2)), -0.2, 0.2), -0.3, -0.02)
    out_weight = gaussian(seeds[12], (HEADS * HEAD_DIM, D_MODEL), (HEADS * HEAD_DIM) ** -0.5, 0.0625, ((0, 2), (1, 8)))
    return {"ssm_input": ssm_input, "b_proj": b_proj, "c_proj": c_proj, "step_size": step_size, "log_decay": log_decay, "skip_gain": skip_gain, "request_of_slot": request_of_slot, "new_input": new_input, "new_b": new_b, "new_c": new_c, "new_step": new_step, "new_log_decay": new_log_decay, "out_weight": out_weight}


def block_terms(block_input, block_b, block_c, block_step, block_logd):
    block_size = block_input.shape[0]
    per_group = HEADS // GROUPS
    cumulative = jnp.cumsum(block_logd, axis=1)
    block_total = cumulative[:, -1]
    inputs_head = block_input.reshape(block_size, GROUPS, per_group, HEAD_DIM).astype(jnp.float32)
    b_groups = block_b.reshape(block_size, GROUPS, STATE).astype(jnp.float32)
    c_groups = block_c.reshape(block_size, GROUPS, STATE).astype(jnp.float32)
    scores = jnp.einsum("tgn,sgn->gts", c_groups, b_groups)
    row_index = lax.broadcasted_iota(jnp.int32, (block_size, block_size), 0)
    col_index = lax.broadcasted_iota(jnp.int32, (block_size, block_size), 1)
    causal = row_index >= col_index
    log_gap = cumulative[:, :, None] - cumulative[:, None, :]
    decay_rate = jnp.where(causal, jnp.exp(jnp.where(causal, log_gap, 0.0)), 0.0) * block_step[:, None, :]
    mixing = (scores[:, None, :, :] * decay_rate.reshape(GROUPS, per_group, block_size, block_size)).astype(jnp.bfloat16)
    local_out = jnp.einsum("gkts,sgkp->tgkp", mixing.astype(jnp.float32), inputs_head)
    weighting = jnp.exp(block_total[:, None] - cumulative) * block_step
    weighted = (weighting.T.reshape(block_size, GROUPS, per_group, 1) * inputs_head).astype(jnp.bfloat16)
    block_state = jnp.einsum("sgkp,sgn->gkpn", weighted.astype(jnp.float32), b_groups)
    return cumulative, block_total.reshape(GROUPS, per_group), local_out, block_state


def finish(local_out, cumulative, block_c, entering, block_input, skip_gain):
    block_size = block_input.shape[0]
    per_group = HEADS // GROUPS
    c_groups = block_c.reshape(block_size, GROUPS, STATE).astype(jnp.float32)
    carried = jnp.einsum("tgn,gkpn->tgkp", c_groups, entering, precision=lax.Precision.HIGHEST)
    carried = carried * jnp.exp(cumulative).T.reshape(block_size, GROUPS, per_group, 1)
    inputs_head = block_input.reshape(block_size, GROUPS, per_group, HEAD_DIM).astype(jnp.float32)
    skipped = skip_gain.reshape(GROUPS, per_group, 1) * inputs_head
    return (local_out + carried + skipped).reshape(block_size, HEADS * HEAD_DIM).astype(jnp.bfloat16)


def prefill_request(request_input, request_b, request_c, request_step, request_logd, skip_gain):
    blocks = PROMPT_LENGTH // TOK_DEV
    per_group = HEADS // GROUPS
    inputs_blocks = request_input.reshape(blocks, TOK_DEV, HEADS * HEAD_DIM)
    b_blocks = request_b.reshape(blocks, TOK_DEV, GROUPS * STATE)
    c_blocks = request_c.reshape(blocks, TOK_DEV, GROUPS * STATE)
    step_blocks = request_step.reshape(HEADS, blocks, TOK_DEV).transpose(1, 0, 2)
    logd_blocks = request_logd.reshape(HEADS, blocks, TOK_DEV).transpose(1, 0, 2)

    def advance(entering, pieces):
        block_input, block_b, block_c, block_step, block_logd = pieces
        cumulative, block_total, local_out, block_state = block_terms(block_input, block_b, block_c, block_step, block_logd)
        result = finish(local_out, cumulative, block_c, entering, block_input, skip_gain)
        leaving = jnp.exp(block_total)[:, :, None, None] * entering + block_state
        return leaving, result

    start_state = jnp.zeros((GROUPS, per_group, HEAD_DIM, STATE), jnp.float32)
    final_state, results = lax.scan(advance, start_state, (inputs_blocks, b_blocks, c_blocks, step_blocks, logd_blocks))
    return final_state, results.reshape(PROMPT_LENGTH, HEADS * HEAD_DIM)


def decode_step(carry_state, row_input, row_b, row_c, row_step, row_logd, skip_gain):
    per_group = HEADS // GROUPS
    inputs_head = row_input.reshape(GROUPS, per_group, HEAD_DIM).astype(jnp.float32)
    b_groups = row_b.reshape(GROUPS, STATE).astype(jnp.float32)
    c_groups = row_c.reshape(GROUPS, STATE).astype(jnp.float32)
    scaled = row_step.reshape(GROUPS, per_group, 1) * inputs_head
    carry_state = jnp.exp(row_logd).reshape(GROUPS, per_group, 1, 1) * carry_state + scaled[:, :, :, None] * b_groups[:, None, None, :]
    output = jnp.einsum("gkpn,gn->gkp", carry_state, c_groups, precision=lax.Precision.HIGHEST)
    output = output + skip_gain.reshape(GROUPS, per_group, 1) * inputs_head
    return carry_state, output.reshape(HEADS * HEAD_DIM).astype(jnp.bfloat16)


def reference(ssm_input, b_proj, c_proj, step_size, log_decay, skip_gain, request_of_slot, new_input, new_b, new_c, new_step, new_log_decay, out_weight):
    finals = []
    prefill_rows = []
    for request in range(PROMPT_REQUESTS):
        final_state, results = prefill_request(ssm_input[request], b_proj[request], c_proj[request], step_size[request], log_decay[request], skip_gain)
        finals.append(final_state)
        prefill_rows.append(results)
    finals = jnp.stack(finals)
    prefill_out = jnp.stack(prefill_rows)
    request_numbers = jnp.arange(PROMPT_REQUESTS, dtype=jnp.int32)

    def decode_slot(pieces):
        slot_request, slot_input, slot_b, slot_c, slot_step, slot_logd = pieces
        chosen = (request_numbers == slot_request).astype(jnp.float32)
        carry_state = jnp.einsum("r,rgkpn->gkpn", chosen, finals, precision=lax.Precision.HIGHEST)
        results = []
        for position in range(STEPS):
            carry_state, output = decode_step(carry_state, slot_input[position], slot_b[position], slot_c[position], slot_step[position], slot_logd[position], skip_gain)
            results.append(output)
        return jnp.stack(results)

    new_output = lax.map(decode_slot, (request_of_slot, new_input, new_b, new_c, new_step, new_log_decay))
    decoded = jnp.dot(new_output.reshape(SLOTS * STEPS, HEADS * HEAD_DIM), out_weight, preferred_element_type=jnp.float32)
    decoded = decoded.astype(jnp.bfloat16).reshape(SLOTS, STEPS, D_MODEL)
    return (prefill_out, decoded)
```

```python
import jax
import jax.numpy as jnp
from jax import lax
from jax.sharding import PartitionSpec as P

HEADS = 128
HEAD_DIM = 64
STATE = 128
GROUPS = 4

HIGH = lax.Precision.HIGHEST


def block_terms(block_input, block_b, block_c, block_step, block_logd):
    block_size = block_input.shape[0]
    head_count = block_step.shape[0]
    per_group = HEADS // GROUPS
    group_count = head_count // per_group
    cumulative = jnp.cumsum(block_logd, axis=1)
    block_total = cumulative[:, -1]
    inputs_head = block_input.reshape(block_size, group_count, per_group, HEAD_DIM)
    b_groups = block_b.reshape(block_size, group_count, STATE)
    c_groups = block_c.reshape(block_size, group_count, STATE)
    scores = jnp.einsum("tgn,sgn->gts", c_groups, b_groups, preferred_element_type=jnp.float32)
    row_index = lax.broadcasted_iota(jnp.int32, (block_size, block_size), 0)
    col_index = lax.broadcasted_iota(jnp.int32, (block_size, block_size), 1)
    causal = row_index >= col_index
    log_gap = cumulative[:, :, None] - cumulative[:, None, :]
    decay_rate = (
        jnp.where(causal, jnp.exp(jnp.where(causal, log_gap, 0.0)), 0.0) * block_step[:, None, :]
    )
    mixing = (
        scores[:, None, :, :] * decay_rate.reshape(group_count, per_group, block_size, block_size)
    ).astype(jnp.bfloat16)
    local_out = jnp.einsum(
        "gkts,sgkp->tgkp", mixing, inputs_head, preferred_element_type=jnp.float32
    )
    weighting = jnp.exp(block_total[:, None] - cumulative) * block_step
    weighted = (weighting.T.reshape(block_size, group_count, per_group, 1) * inputs_head).astype(
        jnp.bfloat16
    )
    block_state = jnp.einsum(
        "sgkp,sgn->gkpn", weighted, b_groups, preferred_element_type=jnp.float32
    )
    return (cumulative, block_total.reshape(group_count, per_group), local_out, block_state)


def finish(local_out, cumulative, block_c, entering, block_input, skip_gain):
    block_size = block_input.shape[0]
    group_count, per_group = (entering.shape[0], entering.shape[1])
    c_groups = block_c.reshape(block_size, group_count, STATE).astype(jnp.float32)
    carried = jnp.einsum("tgn,gkpn->tgkp", c_groups, entering, precision=HIGH)
    carried = carried * jnp.exp(cumulative).T.reshape(block_size, group_count, per_group, 1)
    inputs_head = block_input.reshape(block_size, group_count, per_group, HEAD_DIM)
    skipped = skip_gain.reshape(group_count, per_group, 1) * inputs_head
    return (
        (local_out + carried + skipped)
        .reshape(block_size, group_count * per_group * HEAD_DIM)
        .astype(jnp.bfloat16)
    )


def range_decay(all_totals, low, high):
    place = lax.broadcasted_iota(jnp.int32, all_totals.shape, 0)
    keep = (place >= low) & (place <= high)
    return jnp.exp(jnp.sum(jnp.where(keep, all_totals, 0.0), axis=0))


def scale(factor, state):
    return factor[..., None, None] * state


def send(value, pairs):
    return lax.ppermute(value.astype(jnp.bfloat16), "ctx", pairs).astype(jnp.float32)


def prefix_states(states, all_totals):
    count = lax.axis_size("ctx")
    columns = count // 2
    place = lax.axis_index("ctx")
    row = place % 2
    column = place // 2
    half = states.shape[-2] // 2
    first = states[..., :half, :]
    second = states[..., half:, :]
    row_zero = row == 0
    mine = jnp.where(row_zero, first, second)
    other = jnp.where(row_zero, second, first)
    across = [(2 * m, 2 * m + 1) for m in range(columns)] + [
        (2 * m + 1, 2 * m) for m in range(columns)
    ]
    received = send(other, across)
    even_state = jnp.where(row_zero, mine, received)
    odd_state = jnp.where(row_zero, received, mine)
    odd_decay = range_decay(all_totals, 2 * column + 1, 2 * column + 1)
    window = scale(odd_decay, even_state) + odd_state
    before = jnp.zeros_like(window)
    step = 1
    while step < columns:
        pairs = [(y + 2 * m, y + 2 * (m + step)) for y in range(2) for m in range(columns - step)]
        got = send(window, pairs)
        low = 2 * (column - step) + 2
        before = scale(range_decay(all_totals, low, 2 * column - 1), got) + before
        if 2 * step < columns:
            window = scale(range_decay(all_totals, low, 2 * column + 1), got) + window
        step *= 2
    even_decay = range_decay(all_totals, 2 * column, 2 * column)
    odd_entering = scale(even_decay, before) + even_state
    outgoing = jnp.where(row_zero, odd_entering, before)
    partner = send(outgoing, across)
    own_half = jnp.where(row_zero, before, odd_entering)
    first_half = jnp.where(row_zero, own_half, partner)
    second_half = jnp.where(row_zero, partner, own_half)
    return jnp.concatenate([first_half, second_half], axis=-2)


def shards(
    ssm_input,
    b_proj,
    c_proj,
    step_size,
    log_decay,
    skip_gain,
    request_of_slot,
    new_input,
    new_b,
    new_c,
    new_step,
    new_log_decay,
    out_weight,
):
    request_count = ssm_input.shape[0]
    count = lax.axis_size("ctx")
    place = lax.axis_index("ctx")
    terms = []
    for request in range(request_count):
        terms.append(
            block_terms(
                ssm_input[request],
                b_proj[request],
                c_proj[request],
                step_size[request],
                log_decay[request],
            )
        )
    totals = jnp.stack([term[1] for term in terms])
    states = jnp.stack([term[3] for term in terms])
    group_count, per_group = totals.shape[1], totals.shape[2]

    slots, steps = new_input.shape[0], new_input.shape[1]
    pieces = [
        totals,
        request_of_slot.astype(jnp.float32),
        new_input.astype(jnp.float32),
        new_b.astype(jnp.float32),
        new_c.astype(jnp.float32),
        new_step,
        new_log_decay,
    ]
    packed = jnp.concatenate([piece.reshape(-1) for piece in pieces])
    gathered = lax.all_gather(packed, "ctx")
    unpacked = []
    offset = 0
    for piece in pieces:
        size = piece.size
        unpacked.append(
            gathered[:, offset : offset + size].reshape((count,) + piece.shape)
        )
        offset += size
    all_totals, all_request, all_input, all_b, all_c, all_step, all_logd = unpacked
    all_slots = count * slots
    all_request = all_request.reshape(all_slots)
    all_input = all_input.reshape(all_slots, steps, group_count, per_group, HEAD_DIM)
    all_b = all_b.reshape(all_slots, steps, group_count, STATE)
    all_c = all_c.reshape(all_slots, steps, group_count, STATE)
    all_step = all_step.reshape(all_slots, steps, group_count, per_group)
    all_logd = all_logd.reshape(all_slots, steps, group_count, per_group)

    later = range_decay(all_totals, place + 1, count - 1)
    weighted_states = scale(later, states)
    projected = jnp.einsum("rgkpn,jugn->rjugkp", weighted_states, all_c, precision=HIGH)
    request_numbers = lax.broadcasted_iota(jnp.int32, (request_count, 1), 0).astype(jnp.float32)
    chosen = (request_numbers == all_request[None, :]).astype(jnp.float32)
    contribution = jnp.einsum("rj,rjugkp->jugkp", chosen, projected, precision=HIGH)
    from_prompt = lax.psum(contribution, "ctx")

    cum_logd = jnp.cumsum(all_logd, axis=1)
    inner = jnp.einsum("jvgn,jugn->jvug", all_b, all_c, precision=HIGH)
    driven = all_step[..., None] * all_input
    outputs = []
    for u in range(steps):
        value = jnp.exp(cum_logd[:, u])[..., None] * from_prompt[:, u]
        for v in range(u + 1):
            gap = jnp.exp(cum_logd[:, u] - cum_logd[:, v])
            coefficient = gap * inner[:, v, u][:, :, None]
            value = value + coefficient[..., None] * driven[:, v]
        value = value + skip_gain.reshape(group_count, per_group, 1) * all_input[:, u]
        outputs.append(value.reshape(all_slots, -1).astype(jnp.bfloat16))
    new_output = jnp.stack(outputs, axis=1)
    partial_value = jnp.einsum(
        "jup,pd->jud", new_output, out_weight, preferred_element_type=jnp.float32
    )
    decoded = lax.psum(partial_value, "heads").astype(jnp.bfloat16)

    entering = prefix_states(states, all_totals)
    prefill_rows = []
    for request in range(request_count):
        prefill_rows.append(
            finish(
                terms[request][2],
                terms[request][0],
                c_proj[request],
                entering[request],
                ssm_input[request],
                skip_gain,
            )
        )
    prefill_out = jnp.stack(prefill_rows)
    return (prefill_out, decoded)


def solution(mesh):
    in_specs = (
        P("groups", "ctx", "heads"),
        P("groups", "ctx", "heads"),
        P("groups", "ctx", "heads"),
        P("groups", "heads", "ctx"),
        P("groups", "heads", "ctx"),
        P("heads"),
        P(("groups", "ctx")),
        P(("groups", "ctx"), None, "heads"),
        P(("groups", "ctx"), None, "heads"),
        P(("groups", "ctx"), None, "heads"),
        P(("groups", "ctx"), None, "heads"),
        P(("groups", "ctx"), None, "heads"),
        P("heads", "ctx"),
    )
    out_specs = (P("groups", "ctx", "heads"), P("groups", None, "ctx"))
    return jax.shard_map(shards, mesh=mesh, in_specs=in_specs, out_specs=out_specs, check_vma=False)
```

```python
import jax
import jax.numpy as jnp
from jax import lax
from jax.sharding import PartitionSpec as P

HEADS = 128
HEAD_DIM = 64
STATE = 128
GROUPS = 4

HIGH = lax.Precision.HIGHEST


def block_terms(block_input, block_b, block_c, block_step, block_logd):
    block_size = block_input.shape[0]
    head_count = block_step.shape[0]
    per_group = HEADS // GROUPS
    group_count = head_count // per_group
    cumulative = jnp.cumsum(block_logd, axis=1)
    block_total = cumulative[:, -1]
    inputs_head = block_input.reshape(block_size, group_count, per_group, HEAD_DIM)
    b_groups = block_b.reshape(block_size, group_count, STATE)
    c_groups = block_c.reshape(block_size, group_count, STATE)
    scores = jnp.einsum("tgn,sgn->gts", c_groups, b_groups, preferred_element_type=jnp.float32)
    row_index = lax.broadcasted_iota(jnp.int32, (block_size, block_size), 0)
    col_index = lax.broadcasted_iota(jnp.int32, (block_size, block_size), 1)
    causal = row_index >= col_index
    log_gap = cumulative[:, :, None] - cumulative[:, None, :]
    decay_rate = (
        jnp.where(causal, jnp.exp(jnp.where(causal, log_gap, 0.0)), 0.0) * block_step[:, None, :]
    )
    mixing = (
        scores[:, None, :, :] * decay_rate.reshape(group_count, per_group, block_size, block_size)
    ).astype(jnp.bfloat16)
    local_out = jnp.einsum(
        "gkts,sgkp->tgkp", mixing, inputs_head, preferred_element_type=jnp.float32
    )
    weighting = jnp.exp(block_total[:, None] - cumulative) * block_step
    weighted = (weighting.T.reshape(block_size, group_count, per_group, 1) * inputs_head).astype(
        jnp.bfloat16
    )
    block_state = jnp.einsum(
        "sgkp,sgn->gkpn", weighted, b_groups, preferred_element_type=jnp.float32
    )
    return (cumulative, block_total.reshape(group_count, per_group), local_out, block_state)


def finish(local_out, cumulative, block_c, entering, block_input, skip_gain):
    block_size = block_input.shape[0]
    group_count, per_group = (entering.shape[0], entering.shape[1])
    c_groups = block_c.reshape(block_size, group_count, STATE).astype(jnp.float32)
    carried = jnp.einsum("tgn,gkpn->tgkp", c_groups, entering, precision=HIGH)
    carried = carried * jnp.exp(cumulative).T.reshape(block_size, group_count, per_group, 1)
    inputs_head = block_input.reshape(block_size, group_count, per_group, HEAD_DIM)
    skipped = skip_gain.reshape(group_count, per_group, 1) * inputs_head
    return (
        (local_out + carried + skipped)
        .reshape(block_size, group_count * per_group * HEAD_DIM)
        .astype(jnp.bfloat16)
    )


def range_decay(all_totals, low, high):
    place = lax.broadcasted_iota(jnp.int32, all_totals.shape, 0)
    keep = (place >= low) & (place <= high)
    return jnp.exp(jnp.sum(jnp.where(keep, all_totals, 0.0), axis=0))


def scale(factor, state):
    return factor[..., None, None] * state


def send(value, pairs):
    return lax.ppermute(value.astype(jnp.bfloat16), "ctx", pairs).astype(jnp.float32)


def prefix_states(states, all_totals):
    count = lax.axis_size("ctx")
    columns = count // 2
    place = lax.axis_index("ctx")
    row = place % 2
    column = place // 2
    half = states.shape[-2] // 2
    first = states[..., :half, :]
    second = states[..., half:, :]
    row_zero = row == 0
    mine = jnp.where(row_zero, first, second)
    other = jnp.where(row_zero, second, first)
    across = [(2 * m, 2 * m + 1) for m in range(columns)] + [
        (2 * m + 1, 2 * m) for m in range(columns)
    ]
    received = send(other, across)
    even_state = jnp.where(row_zero, mine, received)
    odd_state = jnp.where(row_zero, received, mine)
    odd_decay = range_decay(all_totals, 2 * column + 1, 2 * column + 1)
    window = scale(odd_decay, even_state) + odd_state
    before = jnp.zeros_like(window)
    step = 1
    while step < columns:
        pairs = [(y + 2 * m, y + 2 * (m + step)) for y in range(2) for m in range(columns - step)]
        got = send(window, pairs)
        low = 2 * (column - step) + 2
        before = scale(range_decay(all_totals, low, 2 * column - 1), got) + before
        if 2 * step < columns:
            window = scale(range_decay(all_totals, low, 2 * column + 1), got) + window
        step *= 2
    even_decay = range_decay(all_totals, 2 * column, 2 * column)
    odd_entering = scale(even_decay, before) + even_state
    outgoing = jnp.where(row_zero, odd_entering, before)
    partner = send(outgoing, across)
    own_half = jnp.where(row_zero, before, odd_entering)
    first_half = jnp.where(row_zero, own_half, partner)
    second_half = jnp.where(row_zero, partner, own_half)
    return jnp.concatenate([first_half, second_half], axis=-2)


def shards(
    ssm_input,
    b_proj,
    c_proj,
    step_size,
    log_decay,
    skip_gain,
    request_of_slot,
    new_input,
    new_b,
    new_c,
    new_step,
    new_log_decay,
    out_weight,
):
    request_count = ssm_input.shape[0]
    count = lax.axis_size("ctx")
    place = lax.axis_index("ctx")
    terms = []
    for request in range(request_count):
        terms.append(
            block_terms(
                ssm_input[request],
                b_proj[request],
                c_proj[request],
                step_size[request],
                log_decay[request],
            )
        )
    totals = jnp.stack([term[1] for term in terms])
    states = jnp.stack([term[3] for term in terms])
    group_count, per_group = totals.shape[1], totals.shape[2]

    slots, steps = new_input.shape[0], new_input.shape[1]
    pieces = [totals, request_of_slot.astype(jnp.float32), new_c.astype(jnp.float32)]
    packed = jnp.concatenate([piece.reshape(-1) for piece in pieces])
    gathered = lax.all_gather(packed, "ctx")
    unpacked = []
    offset = 0
    for piece in pieces:
        size = piece.size
        unpacked.append(
            gathered[:, offset : offset + size].reshape((count,) + piece.shape)
        )
        offset += size
    all_totals, all_request, all_c = unpacked
    all_slots = count * slots
    all_request = all_request.reshape(all_slots)
    all_c = all_c.reshape(all_slots, steps, group_count, STATE)

    later = range_decay(all_totals, place + 1, count - 1)
    weighted_states = scale(later, states)
    high = weighted_states.astype(jnp.bfloat16)
    low = (weighted_states - high.astype(jnp.float32)).astype(jnp.bfloat16)
    c_rows = all_c.astype(jnp.bfloat16)
    projected = jnp.einsum(
        "rgkpn,jugn->rjugkp", high, c_rows, preferred_element_type=jnp.float32
    ) + jnp.einsum("rgkpn,jugn->rjugkp", low, c_rows, preferred_element_type=jnp.float32)
    contribution = projected[0]
    for request in range(1, request_count):
        pick = (all_request == request)[:, None, None, None, None]
        contribution = jnp.where(pick, projected[request], contribution)
    from_prompt = lax.psum_scatter(contribution, "ctx", scatter_dimension=0, tiled=True)

    row_input = new_input.reshape(slots, steps, group_count, per_group, HEAD_DIM).astype(
        jnp.float32
    )
    row_b = new_b.reshape(slots, steps, group_count, STATE).astype(jnp.float32)
    row_c = new_c.reshape(slots, steps, group_count, STATE).astype(jnp.float32)
    row_step = new_step.reshape(slots, steps, group_count, per_group)
    row_logd = new_log_decay.reshape(slots, steps, group_count, per_group)
    cum_logd = jnp.cumsum(row_logd, axis=1)
    inner = jnp.einsum("jvgn,jugn->jvug", row_b, row_c, precision=HIGH)
    order_v = lax.broadcasted_iota(jnp.int32, (steps, steps), 0)
    order_u = lax.broadcasted_iota(jnp.int32, (steps, steps), 1)
    causal = (order_v <= order_u)[None, :, :, None, None]
    gap = cum_logd[:, None, :, :, :] - cum_logd[:, :, None, :, :]
    coefficient = jnp.where(
        causal, jnp.exp(jnp.where(causal, gap, 0.0)) * inner[..., None], 0.0
    ) * row_step[:, :, None, :, :]
    local_part = jnp.sum(coefficient[..., None] * row_input[:, :, None], axis=1)
    value = (
        jnp.exp(cum_logd)[..., None] * from_prompt
        + local_part
        + skip_gain.reshape(group_count, per_group, 1) * row_input
    )
    new_output = value.reshape(slots, steps, -1).astype(jnp.bfloat16)
    partial_value = jnp.einsum(
        "jup,pd->jud",
        lax.all_gather(new_output, "ctx", axis=0, tiled=True),
        out_weight,
        preferred_element_type=jnp.float32,
    )
    decoded = lax.psum(partial_value, "heads").astype(jnp.bfloat16)

    entering = prefix_states(states, all_totals)
    prefill_rows = []
    for request in range(request_count):
        prefill_rows.append(
            finish(
                terms[request][2],
                terms[request][0],
                c_proj[request],
                entering[request],
                ssm_input[request],
                skip_gain,
            )
        )
    prefill_out = jnp.stack(prefill_rows)
    return (prefill_out, decoded)


def solution(mesh):
    in_specs = (
        P("groups", "ctx", "heads"),
        P("groups", "ctx", "heads"),
        P("groups", "ctx", "heads"),
        P("groups", "heads", "ctx"),
        P("groups", "heads", "ctx"),
        P("heads"),
        P(("groups", "ctx")),
        P(("groups", "ctx"), None, "heads"),
        P(("groups", "ctx"), None, "heads"),
        P(("groups", "ctx"), None, "heads"),
        P(("groups", "ctx"), None, "heads"),
        P(("groups", "ctx"), None, "heads"),
        P("heads", "ctx"),
    )
    out_specs = (P("groups", "ctx", "heads"), P("groups", None, "ctx"))
    return jax.shard_map(shards, mesh=mesh, in_specs=in_specs, out_specs=out_specs, check_vma=False)
```

```python
import jax
import jax.numpy as jnp
from jax import lax
from jax.sharding import PartitionSpec as P

HEADS = 128
HEAD_DIM = 64
STATE = 128
GROUPS = 4

HIGH = lax.Precision.HIGHEST


def block_terms(block_input, block_b, block_c, block_step, block_logd):
    block_size = block_input.shape[0]
    head_count = block_step.shape[0]
    per_group = HEADS // GROUPS
    group_count = head_count // per_group
    cumulative = jnp.cumsum(block_logd, axis=1)
    block_total = cumulative[:, -1]
    inputs_head = block_input.reshape(block_size, group_count, per_group, HEAD_DIM)
    b_groups = block_b.reshape(block_size, group_count, STATE)
    c_groups = block_c.reshape(block_size, group_count, STATE)
    scores = jnp.einsum("tgn,sgn->gts", c_groups, b_groups, preferred_element_type=jnp.float32)
    row_index = lax.broadcasted_iota(jnp.int32, (block_size, block_size), 0)
    col_index = lax.broadcasted_iota(jnp.int32, (block_size, block_size), 1)
    causal = row_index >= col_index
    log_gap = cumulative[:, :, None] - cumulative[:, None, :]
    decay_rate = (
        jnp.where(causal, jnp.exp(jnp.where(causal, log_gap, 0.0)), 0.0) * block_step[:, None, :]
    )
    mixing = (
        scores[:, None, :, :] * decay_rate.reshape(group_count, per_group, block_size, block_size)
    ).astype(jnp.bfloat16)
    local_out = jnp.einsum(
        "gkts,sgkp->tgkp", mixing, inputs_head, preferred_element_type=jnp.float32
    )
    weighting = jnp.exp(block_total[:, None] - cumulative) * block_step
    weighted = (weighting.T.reshape(block_size, group_count, per_group, 1) * inputs_head).astype(
        jnp.bfloat16
    )
    block_state = jnp.einsum(
        "sgkp,sgn->gkpn", weighted, b_groups, preferred_element_type=jnp.float32
    )
    return (cumulative, block_total.reshape(group_count, per_group), local_out, block_state)


def finish(local_out, cumulative, block_c, entering, block_input, skip_gain):
    block_size = block_input.shape[0]
    group_count, per_group = (entering.shape[0], entering.shape[1])
    c_groups = block_c.reshape(block_size, group_count, STATE).astype(jnp.float32)
    carried = jnp.einsum("tgn,gkpn->tgkp", c_groups, entering, precision=HIGH)
    carried = carried * jnp.exp(cumulative).T.reshape(block_size, group_count, per_group, 1)
    inputs_head = block_input.reshape(block_size, group_count, per_group, HEAD_DIM)
    skipped = skip_gain.reshape(group_count, per_group, 1) * inputs_head
    return (
        (local_out + carried + skipped)
        .reshape(block_size, group_count * per_group * HEAD_DIM)
        .astype(jnp.bfloat16)
    )


def range_decay(all_totals, low, high):
    place = lax.broadcasted_iota(jnp.int32, all_totals.shape, 0)
    keep = (place >= low) & (place <= high)
    return jnp.exp(jnp.sum(jnp.where(keep, all_totals, 0.0), axis=0))


def scale(factor, state):
    return factor[..., None, None] * state


def send(value, total, pairs):
    state, total = lax.ppermute((value.astype(jnp.bfloat16), total), "ctx", pairs)
    return state.astype(jnp.float32), total


def gather_ctx(value):
    count = lax.axis_size("ctx")
    if count & (count - 1):
        return lax.all_gather(value, "ctx", axis=0, tiled=True)
    place = lax.axis_index("ctx")
    reach = 1
    while reach < count:
        got = lax.ppermute(value, "ctx", [(i, i ^ reach) for i in range(count)])
        upper = (place & reach) != 0
        value = jnp.where(
            upper, jnp.concatenate([got, value], axis=0), jnp.concatenate([value, got], axis=0)
        )
        reach *= 2
    return value


def prefix_states(states, totals):
    count = lax.axis_size("ctx")
    columns = count // 2
    place = lax.axis_index("ctx")
    row_zero = place % 2 == 0
    half = states.shape[-2] // 2
    first = states[..., :half, :]
    second = states[..., half:, :]
    mine = jnp.where(row_zero, first, second)
    other = jnp.where(row_zero, second, first)
    across = [(2 * m, 2 * m + 1) for m in range(columns)] + [
        (2 * m + 1, 2 * m) for m in range(columns)
    ]
    received, partner_total = send(other, totals, across)
    even_state = jnp.where(row_zero, mine, received)
    odd_state = jnp.where(row_zero, received, mine)
    even_total = jnp.where(row_zero, totals, partner_total)
    odd_total = jnp.where(row_zero, partner_total, totals)
    window = scale(jnp.exp(odd_total), even_state) + odd_state
    window_total = even_total + odd_total
    before = jnp.zeros_like(window)
    before_total = jnp.zeros_like(totals)
    step = 1
    while step < columns:
        pairs = [(y + 2 * m, y + 2 * (m + step)) for y in range(2) for m in range(columns - step)]
        got, got_total = send(window, window_total, pairs)
        new_before = scale(jnp.exp(before_total), got) + before
        if 2 * step < columns:
            window = scale(jnp.exp(window_total), got) + window
            window_total = got_total + window_total
        before = new_before
        before_total = got_total + before_total
        step *= 2
    odd_entering = scale(jnp.exp(even_total), before) + even_state
    outgoing = jnp.where(row_zero, odd_entering, before)
    partner, _ = send(outgoing, totals, across)
    own_half = jnp.where(row_zero, before, odd_entering)
    first_half = jnp.where(row_zero, own_half, partner)
    second_half = jnp.where(row_zero, partner, own_half)
    return jnp.concatenate([first_half, second_half], axis=-2)


def shards(
    ssm_input,
    b_proj,
    c_proj,
    step_size,
    log_decay,
    skip_gain,
    request_of_slot,
    new_input,
    new_b,
    new_c,
    new_step,
    new_log_decay,
    out_weight,
):
    request_count = ssm_input.shape[0]
    count = lax.axis_size("ctx")
    place = lax.axis_index("ctx")
    terms = []
    for request in range(request_count):
        terms.append(
            block_terms(
                ssm_input[request],
                b_proj[request],
                c_proj[request],
                step_size[request],
                log_decay[request],
            )
        )
    totals = jnp.stack([term[1] for term in terms])
    states = jnp.stack([term[3] for term in terms])
    group_count, per_group = totals.shape[1], totals.shape[2]

    slots, steps = new_input.shape[0], new_input.shape[1]
    pieces = [totals, request_of_slot.astype(jnp.float32), new_c.astype(jnp.float32)]
    packed = jnp.concatenate([piece.reshape(-1) for piece in pieces])
    gathered = gather_ctx(packed[None])
    unpacked = []
    offset = 0
    for piece in pieces:
        size = piece.size
        unpacked.append(
            gathered[:, offset : offset + size].reshape((count,) + piece.shape)
        )
        offset += size
    all_totals, all_request, all_c = unpacked
    all_slots = count * slots
    all_request = all_request.reshape(all_slots)
    all_c = all_c.reshape(all_slots, steps, group_count, STATE)

    later = range_decay(all_totals, place + 1, count - 1)
    weighted_states = scale(later, states)
    high = weighted_states.astype(jnp.bfloat16)
    low = (weighted_states - high.astype(jnp.float32)).astype(jnp.bfloat16)
    c_rows = all_c.astype(jnp.bfloat16)
    projected = jnp.einsum(
        "rgkpn,jugn->rjugkp", high, c_rows, preferred_element_type=jnp.float32
    ) + jnp.einsum("rgkpn,jugn->rjugkp", low, c_rows, preferred_element_type=jnp.float32)
    contribution = projected[0]
    for request in range(1, request_count):
        pick = (all_request == request)[:, None, None, None, None]
        contribution = jnp.where(pick, projected[request], contribution)
    from_prompt = lax.psum_scatter(contribution, "ctx", scatter_dimension=0, tiled=True)

    row_input = new_input.reshape(slots, steps, group_count, per_group, HEAD_DIM).astype(
        jnp.float32
    )
    row_b = new_b.reshape(slots, steps, group_count, STATE).astype(jnp.float32)
    row_c = new_c.reshape(slots, steps, group_count, STATE).astype(jnp.float32)
    row_step = new_step.reshape(slots, steps, group_count, per_group)
    row_logd = new_log_decay.reshape(slots, steps, group_count, per_group)
    cum_logd = jnp.cumsum(row_logd, axis=1)
    inner = jnp.einsum("jvgn,jugn->jvug", row_b, row_c, precision=HIGH)
    order_v = lax.broadcasted_iota(jnp.int32, (steps, steps), 0)
    order_u = lax.broadcasted_iota(jnp.int32, (steps, steps), 1)
    causal = (order_v <= order_u)[None, :, :, None, None]
    gap = cum_logd[:, None, :, :, :] - cum_logd[:, :, None, :, :]
    coefficient = jnp.where(
        causal, jnp.exp(jnp.where(causal, gap, 0.0)) * inner[..., None], 0.0
    ) * row_step[:, :, None, :, :]
    local_part = jnp.sum(coefficient[..., None] * row_input[:, :, None], axis=1)
    value = (
        jnp.exp(cum_logd)[..., None] * from_prompt
        + local_part
        + skip_gain.reshape(group_count, per_group, 1) * row_input
    )
    new_output = value.reshape(slots, steps, -1).astype(jnp.bfloat16)
    partial_value = jnp.einsum(
        "jup,pd->jud",
        gather_ctx(new_output),
        out_weight,
        preferred_element_type=jnp.float32,
    )
    decoded = lax.psum(partial_value, "heads").astype(jnp.bfloat16)

    entering = prefix_states(states, totals)
    prefill_rows = []
    for request in range(request_count):
        prefill_rows.append(
            finish(
                terms[request][2],
                terms[request][0],
                c_proj[request],
                entering[request],
                ssm_input[request],
                skip_gain,
            )
        )
    prefill_out = jnp.stack(prefill_rows)
    return (prefill_out, decoded)


def solution(mesh):
    in_specs = (
        P("groups", "ctx", "heads"),
        P("groups", "ctx", "heads"),
        P("groups", "ctx", "heads"),
        P("groups", "heads", "ctx"),
        P("groups", "heads", "ctx"),
        P("heads"),
        P(("groups", "ctx")),
        P(("groups", "ctx"), None, "heads"),
        P(("groups", "ctx"), None, "heads"),
        P(("groups", "ctx"), None, "heads"),
        P(("groups", "ctx"), None, "heads"),
        P(("groups", "ctx"), None, "heads"),
        P("heads", "ctx"),
    )
    out_specs = (P("groups", "ctx", "heads"), P("groups", None, "ctx"))
    return jax.shard_map(shards, mesh=mesh, in_specs=in_specs, out_specs=out_specs, check_vma=False)
```

```python
import jax
import jax.numpy as jnp
from jax import lax
from jax.sharding import PartitionSpec as P

HEADS = 128
HEAD_DIM = 64
STATE = 128
GROUPS = 4

HIGH = lax.Precision.HIGHEST


def block_terms(block_input, block_b, block_c, block_step, block_logd):
    block_size = block_input.shape[0]
    head_count = block_step.shape[0]
    per_group = HEADS // GROUPS
    group_count = head_count // per_group
    cumulative = jnp.cumsum(block_logd, axis=1)
    block_total = cumulative[:, -1]
    inputs_head = block_input.reshape(block_size, group_count, per_group, HEAD_DIM)
    b_groups = block_b.reshape(block_size, group_count, STATE)
    c_groups = block_c.reshape(block_size, group_count, STATE)
    scores = jnp.einsum("tgn,sgn->gts", c_groups, b_groups, preferred_element_type=jnp.float32)
    row_index = lax.broadcasted_iota(jnp.int32, (block_size, block_size), 0)
    col_index = lax.broadcasted_iota(jnp.int32, (block_size, block_size), 1)
    causal = row_index >= col_index
    log_gap = cumulative[:, :, None] - cumulative[:, None, :]
    decay_rate = (
        jnp.where(causal, jnp.exp(jnp.where(causal, log_gap, 0.0)), 0.0) * block_step[:, None, :]
    )
    mixing = (
        scores[:, None, :, :] * decay_rate.reshape(group_count, per_group, block_size, block_size)
    ).astype(jnp.bfloat16)
    local_out = jnp.einsum(
        "gkts,sgkp->tgkp", mixing, inputs_head, preferred_element_type=jnp.float32
    )
    weighting = jnp.exp(block_total[:, None] - cumulative) * block_step
    weighted = (weighting.T.reshape(block_size, group_count, per_group, 1) * inputs_head).astype(
        jnp.bfloat16
    )
    block_state = jnp.einsum(
        "sgkp,sgn->gkpn", weighted, b_groups, preferred_element_type=jnp.float32
    )
    return (cumulative, block_total.reshape(group_count, per_group), local_out, block_state)


def finish(local_out, cumulative, block_c, entering, block_input, skip_gain):
    block_size = block_input.shape[0]
    group_count, per_group = (entering.shape[0], entering.shape[1])
    c_groups = block_c.reshape(block_size, group_count, STATE).astype(jnp.float32)
    carried = jnp.einsum("tgn,gkpn->tgkp", c_groups, entering, precision=HIGH)
    carried = carried * jnp.exp(cumulative).T.reshape(block_size, group_count, per_group, 1)
    inputs_head = block_input.reshape(block_size, group_count, per_group, HEAD_DIM)
    skipped = skip_gain.reshape(group_count, per_group, 1) * inputs_head
    return (
        (local_out + carried + skipped)
        .reshape(block_size, group_count * per_group * HEAD_DIM)
        .astype(jnp.bfloat16)
    )


def range_decay(all_totals, low, high):
    place = lax.broadcasted_iota(jnp.int32, all_totals.shape, 0)
    keep = (place >= low) & (place <= high)
    return jnp.exp(jnp.sum(jnp.where(keep, all_totals, 0.0), axis=0))


def scale(factor, state):
    return factor[..., None, None] * state


def send(value, total, pairs):
    state, total = lax.ppermute((value.astype(jnp.bfloat16), total), "ctx", pairs)
    return state.astype(jnp.float32), total


def gather_ctx(value):
    count = lax.axis_size("ctx")
    if count & (count - 1):
        return lax.all_gather(value, "ctx", axis=0, tiled=True)
    place = lax.axis_index("ctx")
    reach = 1
    while reach < count:
        got = lax.ppermute(value, "ctx", [(i, i ^ reach) for i in range(count)])
        upper = (place & reach) != 0
        value = jnp.where(
            upper, jnp.concatenate([got, value], axis=0), jnp.concatenate([value, got], axis=0)
        )
        reach *= 2
    return value


def reduce_scatter_ctx(value):
    count = lax.axis_size("ctx")
    if count & (count - 1):
        return lax.psum_scatter(value, "ctx", scatter_dimension=0, tiled=True)
    place = lax.axis_index("ctx")
    reach = 1
    while reach < count:
        pairs = value.reshape((value.shape[0] // 2, 2) + value.shape[1:])
        upper = (place & reach) != 0
        keep = jnp.where(upper, pairs[:, 1], pairs[:, 0])
        give = jnp.where(upper, pairs[:, 0], pairs[:, 1])
        value = keep + lax.ppermute(give, "ctx", [(i, i ^ reach) for i in range(count)])
        reach *= 2
    return value


def prefix_states(states, totals):
    count = lax.axis_size("ctx")
    columns = count // 2
    place = lax.axis_index("ctx")
    row_zero = place % 2 == 0
    half = states.shape[-2] // 2
    first = states[..., :half, :]
    second = states[..., half:, :]
    mine = jnp.where(row_zero, first, second)
    other = jnp.where(row_zero, second, first)
    across = [(2 * m, 2 * m + 1) for m in range(columns)] + [
        (2 * m + 1, 2 * m) for m in range(columns)
    ]
    received, partner_total = send(other, totals, across)
    even_state = jnp.where(row_zero, mine, received)
    odd_state = jnp.where(row_zero, received, mine)
    even_total = jnp.where(row_zero, totals, partner_total)
    odd_total = jnp.where(row_zero, partner_total, totals)
    window = scale(jnp.exp(odd_total), even_state) + odd_state
    window_total = even_total + odd_total
    before = jnp.zeros_like(window)
    before_total = jnp.zeros_like(totals)
    step = 1
    while step < columns:
        pairs = [(y + 2 * m, y + 2 * (m + step)) for y in range(2) for m in range(columns - step)]
        got, got_total = send(window, window_total, pairs)
        new_before = scale(jnp.exp(before_total), got) + before
        if 2 * step < columns:
            window = scale(jnp.exp(window_total), got) + window
            window_total = got_total + window_total
        before = new_before
        before_total = got_total + before_total
        step *= 2
    odd_entering = scale(jnp.exp(even_total), before) + even_state
    outgoing = jnp.where(row_zero, odd_entering, before)
    partner, _ = send(outgoing, totals, across)
    own_half = jnp.where(row_zero, before, odd_entering)
    first_half = jnp.where(row_zero, own_half, partner)
    second_half = jnp.where(row_zero, partner, own_half)
    return jnp.concatenate([first_half, second_half], axis=-2)


def shards(
    ssm_input,
    b_proj,
    c_proj,
    step_size,
    log_decay,
    skip_gain,
    request_of_slot,
    new_input,
    new_b,
    new_c,
    new_step,
    new_log_decay,
    out_weight,
):
    request_count = ssm_input.shape[0]
    count = lax.axis_size("ctx")
    place = lax.axis_index("ctx")
    terms = []
    for request in range(request_count):
        terms.append(
            block_terms(
                ssm_input[request],
                b_proj[request],
                c_proj[request],
                step_size[request],
                log_decay[request],
            )
        )
    totals = jnp.stack([term[1] for term in terms])
    states = jnp.stack([term[3] for term in terms])
    group_count, per_group = totals.shape[1], totals.shape[2]

    slots, steps = new_input.shape[0], new_input.shape[1]
    pieces = [totals, request_of_slot.astype(jnp.float32), new_c.astype(jnp.float32)]
    packed = jnp.concatenate([piece.reshape(-1) for piece in pieces])
    gathered = gather_ctx(packed[None])
    unpacked = []
    offset = 0
    for piece in pieces:
        size = piece.size
        unpacked.append(
            gathered[:, offset : offset + size].reshape((count,) + piece.shape)
        )
        offset += size
    all_totals, all_request, all_c = unpacked
    all_slots = count * slots
    all_request = all_request.reshape(all_slots)
    all_c = all_c.reshape(all_slots, steps, group_count, STATE)

    later = range_decay(all_totals, place + 1, count - 1)
    weighted_states = scale(later, states)
    high = weighted_states.astype(jnp.bfloat16)
    low = (weighted_states - high.astype(jnp.float32)).astype(jnp.bfloat16)
    c_rows = all_c.astype(jnp.bfloat16)
    projected = jnp.einsum(
        "rgkpn,jugn->rjugkp", high, c_rows, preferred_element_type=jnp.float32
    ) + jnp.einsum("rgkpn,jugn->rjugkp", low, c_rows, preferred_element_type=jnp.float32)
    contribution = projected[0]
    for request in range(1, request_count):
        pick = (all_request == request)[:, None, None, None, None]
        contribution = jnp.where(pick, projected[request], contribution)
    from_prompt = reduce_scatter_ctx(contribution)

    row_input = new_input.reshape(slots, steps, group_count, per_group, HEAD_DIM).astype(
        jnp.float32
    )
    row_b = new_b.reshape(slots, steps, group_count, STATE).astype(jnp.float32)
    row_c = new_c.reshape(slots, steps, group_count, STATE).astype(jnp.float32)
    row_step = new_step.reshape(slots, steps, group_count, per_group)
    row_logd = new_log_decay.reshape(slots, steps, group_count, per_group)
    cum_logd = jnp.cumsum(row_logd, axis=1)
    inner = jnp.einsum("jvgn,jugn->jvug", row_b, row_c, precision=HIGH)
    order_v = lax.broadcasted_iota(jnp.int32, (steps, steps), 0)
    order_u = lax.broadcasted_iota(jnp.int32, (steps, steps), 1)
    causal = (order_v <= order_u)[None, :, :, None, None]
    gap = cum_logd[:, None, :, :, :] - cum_logd[:, :, None, :, :]
    coefficient = jnp.where(
        causal, jnp.exp(jnp.where(causal, gap, 0.0)) * inner[..., None], 0.0
    ) * row_step[:, :, None, :, :]
    local_part = jnp.sum(coefficient[..., None] * row_input[:, :, None], axis=1)
    value = (
        jnp.exp(cum_logd)[..., None] * from_prompt
        + local_part
        + skip_gain.reshape(group_count, per_group, 1) * row_input
    )
    new_output = value.reshape(slots, steps, -1).astype(jnp.bfloat16)
    partial_value = jnp.einsum(
        "jup,pd->jud",
        gather_ctx(new_output),
        out_weight,
        preferred_element_type=jnp.float32,
    )
    decoded = lax.psum(partial_value, "heads").astype(jnp.bfloat16)

    entering = prefix_states(states, totals)
    prefill_rows = []
    for request in range(request_count):
        prefill_rows.append(
            finish(
                terms[request][2],
                terms[request][0],
                c_proj[request],
                entering[request],
                ssm_input[request],
                skip_gain,
            )
        )
    prefill_out = jnp.stack(prefill_rows)
    return (prefill_out, decoded)


def solution(mesh):
    in_specs = (
        P("groups", "ctx", "heads"),
        P("groups", "ctx", "heads"),
        P("groups", "ctx", "heads"),
        P("groups", "heads", "ctx"),
        P("groups", "heads", "ctx"),
        P("heads"),
        P(("groups", "ctx")),
        P(("groups", "ctx"), None, "heads"),
        P(("groups", "ctx"), None, "heads"),
        P(("groups", "ctx"), None, "heads"),
        P(("groups", "ctx"), None, "heads"),
        P(("groups", "ctx"), None, "heads"),
        P("heads", "ctx"),
    )
    out_specs = (P("groups", "ctx", "heads"), P("groups", None, "ctx"))
    return jax.shard_map(shards, mesh=mesh, in_specs=in_specs, out_specs=out_specs, check_vma=False)
```

```python
import jax
import jax.numpy as jnp
from jax import lax
from jax.sharding import PartitionSpec as P

HEADS = 128
HEAD_DIM = 64
STATE = 128
GROUPS = 4

HIGH = lax.Precision.HIGHEST


def block_terms(block_input, block_b, block_c, block_step, block_logd):
    block_size = block_input.shape[0]
    head_count = block_step.shape[0]
    per_group = HEADS // GROUPS
    group_count = head_count // per_group
    cumulative = jnp.cumsum(block_logd, axis=1)
    block_total = cumulative[:, -1]
    inputs_head = block_input.reshape(block_size, group_count, per_group, HEAD_DIM)
    b_groups = block_b.reshape(block_size, group_count, STATE)
    c_groups = block_c.reshape(block_size, group_count, STATE)
    scores = jnp.einsum("tgn,sgn->gts", c_groups, b_groups, preferred_element_type=jnp.float32)
    row_index = lax.broadcasted_iota(jnp.int32, (block_size, block_size), 0)
    col_index = lax.broadcasted_iota(jnp.int32, (block_size, block_size), 1)
    causal = row_index >= col_index
    log_gap = cumulative[:, :, None] - cumulative[:, None, :]
    decay_rate = (
        jnp.where(causal, jnp.exp(jnp.where(causal, log_gap, 0.0)), 0.0) * block_step[:, None, :]
    )
    mixing = (
        scores[:, None, :, :] * decay_rate.reshape(group_count, per_group, block_size, block_size)
    ).astype(jnp.bfloat16)
    local_out = jnp.einsum(
        "gkts,sgkp->tgkp", mixing, inputs_head, preferred_element_type=jnp.float32
    )
    weighting = jnp.exp(block_total[:, None] - cumulative) * block_step
    weighted = (weighting.T.reshape(block_size, group_count, per_group, 1) * inputs_head).astype(
        jnp.bfloat16
    )
    block_state = jnp.einsum(
        "sgkp,sgn->gkpn", weighted, b_groups, preferred_element_type=jnp.float32
    )
    return (cumulative, block_total.reshape(group_count, per_group), local_out, block_state)


def finish(local_out, cumulative, block_c, entering, block_input, skip_gain):
    block_size = block_input.shape[0]
    group_count, per_group = (entering.shape[0], entering.shape[1])
    c_groups = block_c.reshape(block_size, group_count, STATE).astype(jnp.float32)
    carried = jnp.einsum("tgn,gkpn->tgkp", c_groups, entering, precision=HIGH)
    carried = carried * jnp.exp(cumulative).T.reshape(block_size, group_count, per_group, 1)
    inputs_head = block_input.reshape(block_size, group_count, per_group, HEAD_DIM)
    skipped = skip_gain.reshape(group_count, per_group, 1) * inputs_head
    return (
        (local_out + carried + skipped)
        .reshape(block_size, group_count * per_group * HEAD_DIM)
        .astype(jnp.bfloat16)
    )


def range_decay(all_totals, low, high):
    place = lax.broadcasted_iota(jnp.int32, all_totals.shape, 0)
    keep = (place >= low) & (place <= high)
    return jnp.exp(jnp.sum(jnp.where(keep, all_totals, 0.0), axis=0))


def scale(factor, state):
    return factor[..., None, None] * state


def send(value, total, pairs):
    state, total = lax.ppermute((value.astype(jnp.bfloat16), total), "ctx", pairs)
    return state.astype(jnp.float32), total


def gather_ctx(value):
    count = lax.axis_size("ctx")
    if count & (count - 1):
        return lax.all_gather(value, "ctx", axis=0, tiled=True)
    place = lax.axis_index("ctx")
    reach = 1
    while reach < count:
        got = lax.ppermute(value, "ctx", [(i, i ^ reach) for i in range(count)])
        upper = (place & reach) != 0
        value = jnp.where(
            upper, jnp.concatenate([got, value], axis=0), jnp.concatenate([value, got], axis=0)
        )
        reach *= 2
    return value


def reduce_scatter_ctx(value):
    count = lax.axis_size("ctx")
    if count & (count - 1):
        return lax.psum_scatter(value, "ctx", scatter_dimension=0, tiled=True)
    place = lax.axis_index("ctx")
    reach = 1
    while reach < count:
        pairs = value.reshape((value.shape[0] // 2, 2) + value.shape[1:])
        upper = (place & reach) != 0
        keep = jnp.where(upper, pairs[:, 1], pairs[:, 0])
        give = jnp.where(upper, pairs[:, 0], pairs[:, 1])
        value = keep + lax.ppermute(give, "ctx", [(i, i ^ reach) for i in range(count)])
        reach *= 2
    return value


def prefix_states(states, totals, rider):
    count = lax.axis_size("ctx")
    columns = count // 2
    place = lax.axis_index("ctx")
    row_zero = place % 2 == 0
    half = states.shape[-2] // 2
    first = states[..., :half, :]
    second = states[..., half:, :]
    mine = jnp.where(row_zero, first, second)
    other = jnp.where(row_zero, second, first)
    across = [(2 * m, 2 * m + 1) for m in range(columns)] + [
        (2 * m + 1, 2 * m) for m in range(columns)
    ]
    received, partner_total = send(other, totals, across)
    even_state = jnp.where(row_zero, mine, received)
    odd_state = jnp.where(row_zero, received, mine)
    even_total = jnp.where(row_zero, totals, partner_total)
    odd_total = jnp.where(row_zero, partner_total, totals)
    window = scale(jnp.exp(odd_total), even_state) + odd_state
    window_total = even_total + odd_total
    before = jnp.zeros_like(window)
    before_total = jnp.zeros_like(totals)
    step = 1
    while step < columns:
        pairs = [(y + 2 * m, y + 2 * (m + step)) for y in range(2) for m in range(columns - step)]
        got, got_total = send(window, window_total, pairs)
        if step == 1:
            got, rider = lax.optimization_barrier((got, rider))
        new_before = scale(jnp.exp(before_total), got) + before
        if 2 * step < columns:
            window = scale(jnp.exp(window_total), got) + window
            window_total = got_total + window_total
        before = new_before
        before_total = got_total + before_total
        step *= 2
    odd_entering = scale(jnp.exp(even_total), before) + even_state
    outgoing = jnp.where(row_zero, odd_entering, before)
    partner, _ = send(outgoing, totals, across)
    own_half = jnp.where(row_zero, before, odd_entering)
    first_half = jnp.where(row_zero, own_half, partner)
    second_half = jnp.where(row_zero, partner, own_half)
    return jnp.concatenate([first_half, second_half], axis=-2), rider


def shards(
    ssm_input,
    b_proj,
    c_proj,
    step_size,
    log_decay,
    skip_gain,
    request_of_slot,
    new_input,
    new_b,
    new_c,
    new_step,
    new_log_decay,
    out_weight,
):
    request_count = ssm_input.shape[0]
    count = lax.axis_size("ctx")
    place = lax.axis_index("ctx")
    terms = []
    for request in range(request_count):
        terms.append(
            block_terms(
                ssm_input[request],
                b_proj[request],
                c_proj[request],
                step_size[request],
                log_decay[request],
            )
        )
    totals = jnp.stack([term[1] for term in terms])
    states = jnp.stack([term[3] for term in terms])
    group_count, per_group = totals.shape[1], totals.shape[2]

    slots, steps = new_input.shape[0], new_input.shape[1]
    pieces = [totals, request_of_slot.astype(jnp.float32), new_c.astype(jnp.float32)]
    packed = jnp.concatenate([piece.reshape(-1) for piece in pieces])
    gathered = gather_ctx(packed[None])
    unpacked = []
    offset = 0
    for piece in pieces:
        size = piece.size
        unpacked.append(
            gathered[:, offset : offset + size].reshape((count,) + piece.shape)
        )
        offset += size
    all_totals, all_request, all_c = unpacked
    all_slots = count * slots
    all_request = all_request.reshape(all_slots)
    all_c = all_c.reshape(all_slots, steps, group_count, STATE)

    later = range_decay(all_totals, place + 1, count - 1)
    weighted_states = scale(later, states)
    high = weighted_states.astype(jnp.bfloat16)
    low = (weighted_states - high.astype(jnp.float32)).astype(jnp.bfloat16)
    c_rows = all_c.astype(jnp.bfloat16)
    projected = jnp.einsum(
        "rgkpn,jugn->rjugkp", high, c_rows, preferred_element_type=jnp.float32
    ) + jnp.einsum("rgkpn,jugn->rjugkp", low, c_rows, preferred_element_type=jnp.float32)
    contribution = projected[0]
    for request in range(1, request_count):
        pick = (all_request == request)[:, None, None, None, None]
        contribution = jnp.where(pick, projected[request], contribution)
    entering, contribution = prefix_states(states, totals, contribution)
    from_prompt = reduce_scatter_ctx(contribution)

    row_input = new_input.reshape(slots, steps, group_count, per_group, HEAD_DIM).astype(
        jnp.float32
    )
    row_b = new_b.reshape(slots, steps, group_count, STATE).astype(jnp.float32)
    row_c = new_c.reshape(slots, steps, group_count, STATE).astype(jnp.float32)
    row_step = new_step.reshape(slots, steps, group_count, per_group)
    row_logd = new_log_decay.reshape(slots, steps, group_count, per_group)
    cum_logd = jnp.cumsum(row_logd, axis=1)
    inner = jnp.einsum("jvgn,jugn->jvug", row_b, row_c, precision=HIGH)
    order_v = lax.broadcasted_iota(jnp.int32, (steps, steps), 0)
    order_u = lax.broadcasted_iota(jnp.int32, (steps, steps), 1)
    causal = (order_v <= order_u)[None, :, :, None, None]
    gap = cum_logd[:, None, :, :, :] - cum_logd[:, :, None, :, :]
    coefficient = jnp.where(
        causal, jnp.exp(jnp.where(causal, gap, 0.0)) * inner[..., None], 0.0
    ) * row_step[:, :, None, :, :]
    local_part = jnp.sum(coefficient[..., None] * row_input[:, :, None], axis=1)
    value = (
        jnp.exp(cum_logd)[..., None] * from_prompt
        + local_part
        + skip_gain.reshape(group_count, per_group, 1) * row_input
    )
    new_output = value.reshape(slots, steps, -1).astype(jnp.bfloat16)
    partial_value = jnp.einsum(
        "jup,pd->jud",
        gather_ctx(new_output),
        out_weight,
        preferred_element_type=jnp.float32,
    )
    decoded = lax.psum(partial_value, "heads").astype(jnp.bfloat16)

    prefill_rows = []
    for request in range(request_count):
        prefill_rows.append(
            finish(
                terms[request][2],
                terms[request][0],
                c_proj[request],
                entering[request],
                ssm_input[request],
                skip_gain,
            )
        )
    prefill_out = jnp.stack(prefill_rows)
    return (prefill_out, decoded)


def solution(mesh):
    in_specs = (
        P("groups", "ctx", "heads"),
        P("groups", "ctx", "heads"),
        P("groups", "ctx", "heads"),
        P("groups", "heads", "ctx"),
        P("groups", "heads", "ctx"),
        P("heads"),
        P(("groups", "ctx")),
        P(("groups", "ctx"), None, "heads"),
        P(("groups", "ctx"), None, "heads"),
        P(("groups", "ctx"), None, "heads"),
        P(("groups", "ctx"), None, "heads"),
        P(("groups", "ctx"), None, "heads"),
        P("heads", "ctx"),
    )
    out_specs = (P("groups", "ctx", "heads"), P("groups", None, "ctx"))
    return jax.shard_map(shards, mesh=mesh, in_specs=in_specs, out_specs=out_specs, check_vma=False)
```

```python
import jax
import jax.numpy as jnp
from jax import lax
from jax.sharding import PartitionSpec as P

HEADS = 128
HEAD_DIM = 64
STATE = 128
GROUPS = 4

HIGH = lax.Precision.HIGHEST


def block_terms(block_input, block_b, block_c, block_step, block_logd):
    block_size = block_input.shape[0]
    head_count = block_step.shape[0]
    per_group = HEADS // GROUPS
    group_count = head_count // per_group
    cumulative = jnp.cumsum(block_logd, axis=1)
    block_total = cumulative[:, -1]
    inputs_head = block_input.reshape(block_size, group_count, per_group, HEAD_DIM)
    b_groups = block_b.reshape(block_size, group_count, STATE)
    c_groups = block_c.reshape(block_size, group_count, STATE)
    scores = jnp.einsum("tgn,sgn->gts", c_groups, b_groups, preferred_element_type=jnp.float32)
    row_index = lax.broadcasted_iota(jnp.int32, (block_size, block_size), 0)
    col_index = lax.broadcasted_iota(jnp.int32, (block_size, block_size), 1)
    causal = row_index >= col_index
    log_gap = cumulative[:, :, None] - cumulative[:, None, :]
    decay_rate = (
        jnp.where(causal, jnp.exp(jnp.where(causal, log_gap, 0.0)), 0.0) * block_step[:, None, :]
    )
    mixing = (
        scores[:, None, :, :] * decay_rate.reshape(group_count, per_group, block_size, block_size)
    ).astype(jnp.bfloat16)
    local_out = jnp.einsum(
        "gkts,sgkp->tgkp", mixing, inputs_head, preferred_element_type=jnp.float32
    )
    weighting = jnp.exp(block_total[:, None] - cumulative) * block_step
    weighted = (weighting.T.reshape(block_size, group_count, per_group, 1) * inputs_head).astype(
        jnp.bfloat16
    )
    block_state = jnp.einsum(
        "sgkp,sgn->gkpn", weighted, b_groups, preferred_element_type=jnp.float32
    )
    return (cumulative, block_total.reshape(group_count, per_group), local_out, block_state)


def finish(local_out, cumulative, block_c, entering, block_input, skip_gain):
    block_size = block_input.shape[0]
    group_count, per_group = (entering.shape[0], entering.shape[1])
    c_groups = block_c.reshape(block_size, group_count, STATE).astype(jnp.float32)
    carried = jnp.einsum("tgn,gkpn->tgkp", c_groups, entering, precision=HIGH)
    carried = carried * jnp.exp(cumulative).T.reshape(block_size, group_count, per_group, 1)
    inputs_head = block_input.reshape(block_size, group_count, per_group, HEAD_DIM)
    skipped = skip_gain.reshape(group_count, per_group, 1) * inputs_head
    return (
        (local_out + carried + skipped)
        .reshape(block_size, group_count * per_group * HEAD_DIM)
        .astype(jnp.bfloat16)
    )


def range_decay(all_totals, low, high):
    place = lax.broadcasted_iota(jnp.int32, all_totals.shape, 0)
    keep = (place >= low) & (place <= high)
    return jnp.exp(jnp.sum(jnp.where(keep, all_totals, 0.0), axis=0))


def scale(factor, state):
    return factor[..., None, None] * state


def send(value, total, pairs):
    state, total = lax.ppermute((value.astype(jnp.bfloat16), total), "ctx", pairs)
    return state.astype(jnp.float32), total


def gather_ctx(value):
    count = lax.axis_size("ctx")
    if count & (count - 1):
        return lax.all_gather(value, "ctx", axis=0, tiled=True)
    place = lax.axis_index("ctx")
    reach = 1
    while reach < count:
        got = lax.ppermute(value, "ctx", [(i, i ^ reach) for i in range(count)])
        upper = (place & reach) != 0
        value = jnp.where(
            upper, jnp.concatenate([got, value], axis=0), jnp.concatenate([value, got], axis=0)
        )
        reach *= 2
    return value


def reduce_scatter_ctx(value):
    count = lax.axis_size("ctx")
    if count & (count - 1):
        return lax.psum_scatter(value, "ctx", scatter_dimension=0, tiled=True)
    place = lax.axis_index("ctx")
    reach = 1
    while reach < count:
        pairs = value.reshape((value.shape[0] // 2, 2) + value.shape[1:])
        upper = (place & reach) != 0
        keep = jnp.where(upper, pairs[:, 1], pairs[:, 0])
        give = jnp.where(upper, pairs[:, 0], pairs[:, 1])
        value = keep + lax.ppermute(give, "ctx", [(i, i ^ reach) for i in range(count)])
        reach *= 2
    return value


def prefix_states(states, totals, rider):
    count = lax.axis_size("ctx")
    columns = count // 2
    place = lax.axis_index("ctx")
    row_zero = place % 2 == 0
    half = states.shape[-2] // 2
    first = states[..., :half, :]
    second = states[..., half:, :]
    mine = jnp.where(row_zero, first, second)
    other = jnp.where(row_zero, second, first)
    across = [(2 * m, 2 * m + 1) for m in range(columns)] + [
        (2 * m + 1, 2 * m) for m in range(columns)
    ]
    received, partner_total = send(other, totals, across)
    even_state = jnp.where(row_zero, mine, received)
    odd_state = jnp.where(row_zero, received, mine)
    even_total = jnp.where(row_zero, totals, partner_total)
    odd_total = jnp.where(row_zero, partner_total, totals)
    window = scale(jnp.exp(odd_total), even_state) + odd_state
    window_total = even_total + odd_total
    before = jnp.zeros_like(window)
    before_total = jnp.zeros_like(totals)
    step = 1
    while step < columns:
        pairs = [(y + 2 * m, y + 2 * (m + step)) for y in range(2) for m in range(columns - step)]
        got, got_total = send(window, window_total, pairs)
        new_before = scale(jnp.exp(before_total), got) + before
        if 2 * step < columns:
            window = scale(jnp.exp(window_total), got) + window
            window_total = got_total + window_total
        before = new_before
        before_total = got_total + before_total
        step *= 2
    odd_entering = scale(jnp.exp(even_total), before) + even_state
    outgoing = jnp.where(row_zero, odd_entering, before)
    partner, _ = send(outgoing, totals, across)
    own_half = jnp.where(row_zero, before, odd_entering)
    first_half = jnp.where(row_zero, own_half, partner)
    second_half = jnp.where(row_zero, partner, own_half)
    first_half, second_half, rider = lax.optimization_barrier((first_half, second_half, rider))
    return jnp.concatenate([first_half, second_half], axis=-2), rider


def shards(
    ssm_input,
    b_proj,
    c_proj,
    step_size,
    log_decay,
    skip_gain,
    request_of_slot,
    new_input,
    new_b,
    new_c,
    new_step,
    new_log_decay,
    out_weight,
):
    request_count = ssm_input.shape[0]
    count = lax.axis_size("ctx")
    place = lax.axis_index("ctx")
    terms = []
    for request in range(request_count):
        terms.append(
            block_terms(
                ssm_input[request],
                b_proj[request],
                c_proj[request],
                step_size[request],
                log_decay[request],
            )
        )
    totals = jnp.stack([term[1] for term in terms])
    states = jnp.stack([term[3] for term in terms])
    group_count, per_group = totals.shape[1], totals.shape[2]

    slots, steps = new_input.shape[0], new_input.shape[1]
    pieces = [totals, request_of_slot.astype(jnp.float32), new_c.astype(jnp.float32)]
    packed = jnp.concatenate([piece.reshape(-1) for piece in pieces])
    gathered = gather_ctx(packed[None])
    unpacked = []
    offset = 0
    for piece in pieces:
        size = piece.size
        unpacked.append(
            gathered[:, offset : offset + size].reshape((count,) + piece.shape)
        )
        offset += size
    all_totals, all_request, all_c = unpacked
    all_slots = count * slots
    all_request = all_request.reshape(all_slots)
    all_c = all_c.reshape(all_slots, steps, group_count, STATE)

    later = range_decay(all_totals, place + 1, count - 1)
    weighted_states = scale(later, states)
    high = weighted_states.astype(jnp.bfloat16)
    low = (weighted_states - high.astype(jnp.float32)).astype(jnp.bfloat16)
    c_rows = all_c.astype(jnp.bfloat16)
    projected = jnp.einsum(
        "rgkpn,jugn->rjugkp", high, c_rows, preferred_element_type=jnp.float32
    ) + jnp.einsum("rgkpn,jugn->rjugkp", low, c_rows, preferred_element_type=jnp.float32)
    contribution = projected[0]
    for request in range(1, request_count):
        pick = (all_request == request)[:, None, None, None, None]
        contribution = jnp.where(pick, projected[request], contribution)
    entering, contribution = prefix_states(states, totals, contribution)
    from_prompt = reduce_scatter_ctx(contribution)

    row_input = new_input.reshape(slots, steps, group_count, per_group, HEAD_DIM).astype(
        jnp.float32
    )
    row_b = new_b.reshape(slots, steps, group_count, STATE).astype(jnp.float32)
    row_c = new_c.reshape(slots, steps, group_count, STATE).astype(jnp.float32)
    row_step = new_step.reshape(slots, steps, group_count, per_group)
    row_logd = new_log_decay.reshape(slots, steps, group_count, per_group)
    cum_logd = jnp.cumsum(row_logd, axis=1)
    inner = jnp.einsum("jvgn,jugn->jvug", row_b, row_c, precision=HIGH)
    order_v = lax.broadcasted_iota(jnp.int32, (steps, steps), 0)
    order_u = lax.broadcasted_iota(jnp.int32, (steps, steps), 1)
    causal = (order_v <= order_u)[None, :, :, None, None]
    gap = cum_logd[:, None, :, :, :] - cum_logd[:, :, None, :, :]
    coefficient = jnp.where(
        causal, jnp.exp(jnp.where(causal, gap, 0.0)) * inner[..., None], 0.0
    ) * row_step[:, :, None, :, :]
    local_part = jnp.sum(coefficient[..., None] * row_input[:, :, None], axis=1)
    value = (
        jnp.exp(cum_logd)[..., None] * from_prompt
        + local_part
        + skip_gain.reshape(group_count, per_group, 1) * row_input
    )
    new_output = value.reshape(slots, steps, -1).astype(jnp.bfloat16)
    partial_value = jnp.einsum(
        "jup,pd->jud",
        gather_ctx(new_output),
        out_weight,
        preferred_element_type=jnp.float32,
    )
    decoded = lax.psum(partial_value, "heads").astype(jnp.bfloat16)

    prefill_rows = []
    for request in range(request_count):
        prefill_rows.append(
            finish(
                terms[request][2],
                terms[request][0],
                c_proj[request],
                entering[request],
                ssm_input[request],
                skip_gain,
            )
        )
    prefill_out = jnp.stack(prefill_rows)
    return (prefill_out, decoded)


def solution(mesh):
    in_specs = (
        P("groups", "ctx", "heads"),
        P("groups", "ctx", "heads"),
        P("groups", "ctx", "heads"),
        P("groups", "heads", "ctx"),
        P("groups", "heads", "ctx"),
        P("heads"),
        P(("groups", "ctx")),
        P(("groups", "ctx"), None, "heads"),
        P(("groups", "ctx"), None, "heads"),
        P(("groups", "ctx"), None, "heads"),
        P(("groups", "ctx"), None, "heads"),
        P(("groups", "ctx"), None, "heads"),
        P("heads", "ctx"),
    )
    out_specs = (P("groups", "ctx", "heads"), P("groups", None, "ctx"))
    return jax.shard_map(shards, mesh=mesh, in_specs=in_specs, out_specs=out_specs, check_vma=False)
```

```python
import jax
import jax.numpy as jnp
from jax import lax
from jax.sharding import PartitionSpec as P

HEADS = 128
HEAD_DIM = 64
STATE = 128
GROUPS = 4

HIGH = lax.Precision.HIGHEST


def block_terms(block_input, block_b, block_c, block_step, block_logd):
    block_size = block_input.shape[0]
    head_count = block_step.shape[0]
    per_group = HEADS // GROUPS
    group_count = head_count // per_group
    cumulative = jnp.cumsum(block_logd, axis=1)
    block_total = cumulative[:, -1]
    inputs_head = block_input.reshape(block_size, group_count, per_group, HEAD_DIM)
    b_groups = block_b.reshape(block_size, group_count, STATE)
    c_groups = block_c.reshape(block_size, group_count, STATE)
    scores = jnp.einsum("tgn,sgn->gts", c_groups, b_groups, preferred_element_type=jnp.float32)
    row_index = lax.broadcasted_iota(jnp.int32, (block_size, block_size), 0)
    col_index = lax.broadcasted_iota(jnp.int32, (block_size, block_size), 1)
    causal = row_index >= col_index
    log_gap = cumulative[:, :, None] - cumulative[:, None, :]
    decay_rate = (
        jnp.where(causal, jnp.exp(jnp.where(causal, log_gap, 0.0)), 0.0) * block_step[:, None, :]
    )
    mixing = (
        scores[:, None, :, :] * decay_rate.reshape(group_count, per_group, block_size, block_size)
    ).astype(jnp.bfloat16)
    local_out = jnp.einsum(
        "gkts,sgkp->gktp", mixing, inputs_head, preferred_element_type=jnp.float32
    )
    weighting = jnp.exp(block_total[:, None] - cumulative) * block_step
    weighted = (weighting.T.reshape(block_size, group_count, per_group, 1) * inputs_head).astype(
        jnp.bfloat16
    )
    block_state = jnp.einsum(
        "sgkp,sgn->gkpn", weighted, b_groups, preferred_element_type=jnp.float32
    )
    return (cumulative, block_total.reshape(group_count, per_group), local_out, block_state)


def finish(local_out, cumulative, c_proj, entering, ssm_input, skip_gain):
    request_count, group_count, per_group, block_size = local_out.shape[:4]
    c_groups = c_proj.reshape(request_count, block_size, group_count, STATE)
    flat = entering.reshape(request_count, group_count, per_group * HEAD_DIM, STATE)
    high = flat.astype(jnp.bfloat16)
    low = (flat - high.astype(jnp.float32)).astype(jnp.bfloat16)
    numbers = (((3,), (3,)), ((0, 2), (0, 1)))
    carried = lax.dot_general(
        c_groups, high, numbers, preferred_element_type=jnp.float32
    ) + lax.dot_general(c_groups, low, numbers, preferred_element_type=jnp.float32)
    carried = carried.reshape(request_count, group_count, block_size, per_group, HEAD_DIM)
    growth = jnp.exp(cumulative).reshape(request_count, group_count, per_group, block_size)
    carried = carried * growth.transpose(0, 1, 3, 2)[..., None]
    inputs_head = ssm_input.reshape(
        request_count, block_size, group_count, per_group, HEAD_DIM
    ).astype(jnp.float32)
    skipped = skip_gain.reshape(group_count, per_group, 1) * inputs_head
    total = carried.transpose(0, 2, 1, 3, 4) + local_out.transpose(0, 3, 1, 2, 4) + skipped
    return total.reshape(request_count, block_size, -1).astype(jnp.bfloat16)


def range_decay(all_totals, low, high):
    place = lax.broadcasted_iota(jnp.int32, all_totals.shape, 0)
    keep = (place >= low) & (place <= high)
    return jnp.exp(jnp.sum(jnp.where(keep, all_totals, 0.0), axis=0))


def scale(factor, state):
    return factor[..., None, None] * state


def send(value, total, pairs):
    state, total = lax.ppermute((value.astype(jnp.bfloat16), total), "ctx", pairs)
    return state.astype(jnp.float32), total


def gather_ctx(value):
    count = lax.axis_size("ctx")
    if count & (count - 1):
        return lax.all_gather(value, "ctx", axis=0, tiled=True)
    place = lax.axis_index("ctx")
    reach = 1
    while reach < count:
        got = lax.ppermute(value, "ctx", [(i, i ^ reach) for i in range(count)])
        upper = (place & reach) != 0
        value = jnp.where(
            upper, jnp.concatenate([got, value], axis=0), jnp.concatenate([value, got], axis=0)
        )
        reach *= 2
    return value


def reduce_scatter_ctx(value):
    count = lax.axis_size("ctx")
    if count & (count - 1):
        return lax.psum_scatter(value, "ctx", scatter_dimension=0, tiled=True)
    place = lax.axis_index("ctx")
    reach = 1
    while reach < count:
        pairs = value.reshape((value.shape[0] // 2, 2) + value.shape[1:])
        upper = (place & reach) != 0
        keep = jnp.where(upper, pairs[:, 1], pairs[:, 0])
        give = jnp.where(upper, pairs[:, 0], pairs[:, 1])
        value = keep + lax.ppermute(give, "ctx", [(i, i ^ reach) for i in range(count)])
        reach *= 2
    return value


def prefix_states(states, totals):
    count = lax.axis_size("ctx")
    columns = count // 2
    place = lax.axis_index("ctx")
    row_zero = place % 2 == 0
    half = states.shape[-2] // 2
    first = states[..., :half, :]
    second = states[..., half:, :]
    mine = jnp.where(row_zero, first, second)
    other = jnp.where(row_zero, second, first)
    across = [(2 * m, 2 * m + 1) for m in range(columns)] + [
        (2 * m + 1, 2 * m) for m in range(columns)
    ]
    received, partner_total = send(other, totals, across)
    even_state = jnp.where(row_zero, mine, received)
    odd_state = jnp.where(row_zero, received, mine)
    even_total = jnp.where(row_zero, totals, partner_total)
    odd_total = jnp.where(row_zero, partner_total, totals)
    window = scale(jnp.exp(odd_total), even_state) + odd_state
    window_total = even_total + odd_total
    before = jnp.zeros_like(window)
    before_total = jnp.zeros_like(totals)
    step = 1
    while step < columns:
        pairs = [(y + 2 * m, y + 2 * (m + step)) for y in range(2) for m in range(columns - step)]
        got, got_total = send(window, window_total, pairs)
        new_before = scale(jnp.exp(before_total), got) + before
        if 2 * step < columns:
            window = scale(jnp.exp(window_total), got) + window
            window_total = got_total + window_total
        before = new_before
        before_total = got_total + before_total
        step *= 2
    odd_entering = scale(jnp.exp(even_total), before) + even_state
    outgoing = jnp.where(row_zero, odd_entering, before)
    partner, _ = send(outgoing, totals, across)
    own_half = jnp.where(row_zero, before, odd_entering)
    first_half = jnp.where(row_zero, own_half, partner)
    second_half = jnp.where(row_zero, partner, own_half)
    return jnp.concatenate([first_half, second_half], axis=-2)


def shards(
    ssm_input,
    b_proj,
    c_proj,
    step_size,
    log_decay,
    skip_gain,
    request_of_slot,
    new_input,
    new_b,
    new_c,
    new_step,
    new_log_decay,
    out_weight,
):
    request_count = ssm_input.shape[0]
    count = lax.axis_size("ctx")
    place = lax.axis_index("ctx")
    terms = []
    for request in range(request_count):
        terms.append(
            block_terms(
                ssm_input[request],
                b_proj[request],
                c_proj[request],
                step_size[request],
                log_decay[request],
            )
        )
    totals = jnp.stack([term[1] for term in terms])
    states = jnp.stack([term[3] for term in terms])
    group_count, per_group = totals.shape[1], totals.shape[2]

    slots, steps = new_input.shape[0], new_input.shape[1]
    pieces = [totals, request_of_slot.astype(jnp.float32), new_c.astype(jnp.float32)]
    packed = jnp.concatenate([piece.reshape(-1) for piece in pieces])
    gathered = gather_ctx(packed[None])
    unpacked = []
    offset = 0
    for piece in pieces:
        size = piece.size
        unpacked.append(
            gathered[:, offset : offset + size].reshape((count,) + piece.shape)
        )
        offset += size
    all_totals, all_request, all_c = unpacked
    all_slots = count * slots
    all_request = all_request.reshape(all_slots)
    all_c = all_c.reshape(all_slots, steps, group_count, STATE)

    later = range_decay(all_totals, place + 1, count - 1)
    weighted_states = scale(later, states)
    high = weighted_states.astype(jnp.bfloat16)
    low = (weighted_states - high.astype(jnp.float32)).astype(jnp.bfloat16)
    c_rows = all_c.astype(jnp.bfloat16)
    projected = jnp.einsum(
        "rgkpn,jugn->rjugkp", high, c_rows, preferred_element_type=jnp.float32
    ) + jnp.einsum("rgkpn,jugn->rjugkp", low, c_rows, preferred_element_type=jnp.float32)
    contribution = projected[0]
    for request in range(1, request_count):
        pick = (all_request == request)[:, None, None, None, None]
        contribution = jnp.where(pick, projected[request], contribution)
    from_prompt = reduce_scatter_ctx(contribution)

    row_input = new_input.reshape(slots, steps, group_count, per_group, HEAD_DIM).astype(
        jnp.float32
    )
    row_b = new_b.reshape(slots, steps, group_count, STATE).astype(jnp.float32)
    row_c = new_c.reshape(slots, steps, group_count, STATE).astype(jnp.float32)
    row_step = new_step.reshape(slots, steps, group_count, per_group)
    row_logd = new_log_decay.reshape(slots, steps, group_count, per_group)
    cum_logd = jnp.cumsum(row_logd, axis=1)
    inner = jnp.einsum("jvgn,jugn->jvug", row_b, row_c, precision=HIGH)
    order_v = lax.broadcasted_iota(jnp.int32, (steps, steps), 0)
    order_u = lax.broadcasted_iota(jnp.int32, (steps, steps), 1)
    causal = (order_v <= order_u)[None, :, :, None, None]
    gap = cum_logd[:, None, :, :, :] - cum_logd[:, :, None, :, :]
    coefficient = jnp.where(
        causal, jnp.exp(jnp.where(causal, gap, 0.0)) * inner[..., None], 0.0
    ) * row_step[:, :, None, :, :]
    local_part = jnp.sum(coefficient[..., None] * row_input[:, :, None], axis=1)
    value = (
        jnp.exp(cum_logd)[..., None] * from_prompt
        + local_part
        + skip_gain.reshape(group_count, per_group, 1) * row_input
    )
    new_output = value.reshape(slots, steps, -1).astype(jnp.bfloat16)
    partial_value = jnp.einsum(
        "jup,pd->jud",
        gather_ctx(new_output),
        out_weight,
        preferred_element_type=jnp.float32,
    )
    decoded = lax.psum(partial_value, "heads").astype(jnp.bfloat16)

    entering = prefix_states(states, totals)
    prefill_out = finish(
        jnp.stack([term[2] for term in terms]),
        jnp.stack([term[0] for term in terms]),
        c_proj,
        entering,
        ssm_input,
        skip_gain,
    )
    return (prefill_out, decoded)


def solution(mesh):
    in_specs = (
        P("groups", "ctx", "heads"),
        P("groups", "ctx", "heads"),
        P("groups", "ctx", "heads"),
        P("groups", "heads", "ctx"),
        P("groups", "heads", "ctx"),
        P("heads"),
        P(("groups", "ctx")),
        P(("groups", "ctx"), None, "heads"),
        P(("groups", "ctx"), None, "heads"),
        P(("groups", "ctx"), None, "heads"),
        P(("groups", "ctx"), None, "heads"),
        P(("groups", "ctx"), None, "heads"),
        P("heads", "ctx"),
    )
    out_specs = (P("groups", "ctx", "heads"), P("groups", None, "ctx"))
    return jax.shard_map(shards, mesh=mesh, in_specs=in_specs, out_specs=out_specs, check_vma=False)
```

```python
import jax
import jax.numpy as jnp
from jax import lax
from jax.sharding import PartitionSpec as P

HEADS = 128
HEAD_DIM = 64
STATE = 128
GROUPS = 4

HIGH = lax.Precision.HIGHEST


def block_terms(block_input, block_b, block_c, block_step, block_logd):
    block_size = block_input.shape[0]
    head_count = block_step.shape[0]
    per_group = HEADS // GROUPS
    group_count = head_count // per_group
    cumulative = jnp.cumsum(block_logd, axis=1)
    block_total = cumulative[:, -1]
    inputs_head = block_input.reshape(block_size, group_count, per_group, HEAD_DIM)
    b_groups = block_b.reshape(block_size, group_count, STATE)
    c_groups = block_c.reshape(block_size, group_count, STATE)
    scores = jnp.einsum("tgn,sgn->gts", c_groups, b_groups, preferred_element_type=jnp.float32)
    row_index = lax.broadcasted_iota(jnp.int32, (block_size, block_size), 0)
    col_index = lax.broadcasted_iota(jnp.int32, (block_size, block_size), 1)
    causal = row_index >= col_index
    log_gap = cumulative[:, :, None] - cumulative[:, None, :]
    decay_rate = (
        jnp.where(causal, jnp.exp(jnp.where(causal, log_gap, 0.0)), 0.0) * block_step[:, None, :]
    )
    mixing = (
        scores[:, None, :, :] * decay_rate.reshape(group_count, per_group, block_size, block_size)
    ).astype(jnp.bfloat16)
    local_out = jnp.einsum(
        "gkts,sgkp->gktp", mixing, inputs_head, preferred_element_type=jnp.float32
    )
    weighting = jnp.exp(block_total[:, None] - cumulative) * block_step
    weighted = (weighting.T.reshape(block_size, group_count, per_group, 1) * inputs_head).astype(
        jnp.bfloat16
    )
    block_state = jnp.einsum(
        "sgkp,sgn->gkpn", weighted, b_groups, preferred_element_type=jnp.float32
    )
    return (cumulative, block_total.reshape(group_count, per_group), local_out, block_state)


def finish(local_out, cumulative, c_proj, entering, ssm_input, skip_gain):
    request_count, group_count, per_group, block_size = local_out.shape[:4]
    c_groups = c_proj.reshape(request_count, block_size, group_count, STATE)
    flat = entering.reshape(request_count, group_count, per_group * HEAD_DIM, STATE)
    high = flat.astype(jnp.bfloat16)
    low = (flat - high.astype(jnp.float32)).astype(jnp.bfloat16)
    numbers = (((3,), (3,)), ((0, 2), (0, 1)))
    carried = lax.dot_general(
        c_groups, high, numbers, preferred_element_type=jnp.float32
    ) + lax.dot_general(c_groups, low, numbers, preferred_element_type=jnp.float32)
    carried = carried.reshape(request_count, group_count, block_size, per_group, HEAD_DIM)
    growth = jnp.exp(cumulative).reshape(request_count, group_count, per_group, block_size)
    carried = carried * growth.transpose(0, 1, 3, 2)[..., None]
    inputs_head = ssm_input.reshape(
        request_count, block_size, group_count, per_group, HEAD_DIM
    ).astype(jnp.float32)
    skipped = skip_gain.reshape(group_count, per_group, 1) * inputs_head
    total = carried.transpose(0, 2, 1, 3, 4) + local_out.transpose(0, 3, 1, 2, 4) + skipped
    return total.reshape(request_count, block_size, -1).astype(jnp.bfloat16)


def range_decay(all_totals, low, high):
    place = lax.broadcasted_iota(jnp.int32, all_totals.shape, 0)
    keep = (place >= low) & (place <= high)
    return jnp.exp(jnp.sum(jnp.where(keep, all_totals, 0.0), axis=0))


def scale(factor, state):
    return factor[..., None, None] * state


def send(value, total, pairs):
    state, total = lax.ppermute((value.astype(jnp.bfloat16), total), "ctx", pairs)
    return state.astype(jnp.float32), total


def gather_ctx(value):
    count = lax.axis_size("ctx")
    if count & (count - 1):
        return lax.all_gather(value, "ctx", axis=0, tiled=True)
    place = lax.axis_index("ctx")
    reach = 1
    while reach < count:
        got = lax.ppermute(value, "ctx", [(i, i ^ reach) for i in range(count)])
        upper = (place & reach) != 0
        value = jnp.where(
            upper, jnp.concatenate([got, value], axis=0), jnp.concatenate([value, got], axis=0)
        )
        reach *= 2
    return value


def reduce_scatter_ctx(value):
    count = lax.axis_size("ctx")
    if count & (count - 1):
        return lax.psum_scatter(value, "ctx", scatter_dimension=0, tiled=True)
    place = lax.axis_index("ctx")
    reach = 1
    while reach < count:
        pairs = value.reshape((value.shape[0] // 2, 2) + value.shape[1:])
        upper = (place & reach) != 0
        keep = jnp.where(upper, pairs[:, 1], pairs[:, 0])
        give = jnp.where(upper, pairs[:, 0], pairs[:, 1])
        value = keep + lax.ppermute(give, "ctx", [(i, i ^ reach) for i in range(count)])
        reach *= 2
    return value


def exchange_ctx(value, total):
    count = lax.axis_size("ctx")
    got = lax.all_to_all(value, "ctx", 0, 0, tiled=True)
    got = got.reshape((count, value.shape[0] // count) + value.shape[1:])
    return jnp.sum(got, axis=0) if total else got.reshape(value.shape)


def prefix_states(states, totals):
    count = lax.axis_size("ctx")
    columns = count // 2
    place = lax.axis_index("ctx")
    row_zero = place % 2 == 0
    half = states.shape[-2] // 2
    first = states[..., :half, :]
    second = states[..., half:, :]
    mine = jnp.where(row_zero, first, second)
    other = jnp.where(row_zero, second, first)
    across = [(2 * m, 2 * m + 1) for m in range(columns)] + [
        (2 * m + 1, 2 * m) for m in range(columns)
    ]
    received, partner_total = send(other, totals, across)
    even_state = jnp.where(row_zero, mine, received)
    odd_state = jnp.where(row_zero, received, mine)
    even_total = jnp.where(row_zero, totals, partner_total)
    odd_total = jnp.where(row_zero, partner_total, totals)
    window = scale(jnp.exp(odd_total), even_state) + odd_state
    window_total = even_total + odd_total
    before = jnp.zeros_like(window)
    before_total = jnp.zeros_like(totals)
    step = 1
    while step < columns:
        pairs = [(y + 2 * m, y + 2 * (m + step)) for y in range(2) for m in range(columns - step)]
        got, got_total = send(window, window_total, pairs)
        new_before = scale(jnp.exp(before_total), got) + before
        if 2 * step < columns:
            window = scale(jnp.exp(window_total), got) + window
            window_total = got_total + window_total
        before = new_before
        before_total = got_total + before_total
        step *= 2
    odd_entering = scale(jnp.exp(even_total), before) + even_state
    outgoing = jnp.where(row_zero, odd_entering, before)
    partner, _ = send(outgoing, totals, across)
    own_half = jnp.where(row_zero, before, odd_entering)
    first_half = jnp.where(row_zero, own_half, partner)
    second_half = jnp.where(row_zero, partner, own_half)
    return jnp.concatenate([first_half, second_half], axis=-2)


def shards(
    ssm_input,
    b_proj,
    c_proj,
    step_size,
    log_decay,
    skip_gain,
    request_of_slot,
    new_input,
    new_b,
    new_c,
    new_step,
    new_log_decay,
    out_weight,
):
    request_count = ssm_input.shape[0]
    count = lax.axis_size("ctx")
    place = lax.axis_index("ctx")
    terms = []
    for request in range(request_count):
        terms.append(
            block_terms(
                ssm_input[request],
                b_proj[request],
                c_proj[request],
                step_size[request],
                log_decay[request],
            )
        )
    totals = jnp.stack([term[1] for term in terms])
    states = jnp.stack([term[3] for term in terms])
    group_count, per_group = totals.shape[1], totals.shape[2]

    slots, steps = new_input.shape[0], new_input.shape[1]
    pieces = [totals, request_of_slot.astype(jnp.float32), new_c.astype(jnp.float32)]
    packed = jnp.concatenate([piece.reshape(-1) for piece in pieces])
    gathered = gather_ctx(packed[None])
    unpacked = []
    offset = 0
    for piece in pieces:
        size = piece.size
        unpacked.append(
            gathered[:, offset : offset + size].reshape((count,) + piece.shape)
        )
        offset += size
    all_totals, all_request, all_c = unpacked
    all_slots = count * slots
    all_request = all_request.reshape(all_slots)
    all_c = all_c.reshape(all_slots, steps, group_count, STATE)

    later = range_decay(all_totals, place + 1, count - 1)
    weighted_states = scale(later, states)
    high = weighted_states.astype(jnp.bfloat16)
    low = (weighted_states - high.astype(jnp.float32)).astype(jnp.bfloat16)
    c_rows = all_c.astype(jnp.bfloat16)
    projected = jnp.einsum(
        "rgkpn,jugn->rjugkp", high, c_rows, preferred_element_type=jnp.float32
    ) + jnp.einsum("rgkpn,jugn->rjugkp", low, c_rows, preferred_element_type=jnp.float32)
    contribution = projected[0]
    for request in range(1, request_count):
        pick = (all_request == request)[:, None, None, None, None]
        contribution = jnp.where(pick, projected[request], contribution)
    from_prompt = exchange_ctx(contribution, True)

    row_input = new_input.reshape(slots, steps, group_count, per_group, HEAD_DIM).astype(
        jnp.float32
    )
    row_b = new_b.reshape(slots, steps, group_count, STATE).astype(jnp.float32)
    row_c = new_c.reshape(slots, steps, group_count, STATE).astype(jnp.float32)
    row_step = new_step.reshape(slots, steps, group_count, per_group)
    row_logd = new_log_decay.reshape(slots, steps, group_count, per_group)
    cum_logd = jnp.cumsum(row_logd, axis=1)
    inner = jnp.einsum("jvgn,jugn->jvug", row_b, row_c, precision=HIGH)
    order_v = lax.broadcasted_iota(jnp.int32, (steps, steps), 0)
    order_u = lax.broadcasted_iota(jnp.int32, (steps, steps), 1)
    causal = (order_v <= order_u)[None, :, :, None, None]
    gap = cum_logd[:, None, :, :, :] - cum_logd[:, :, None, :, :]
    coefficient = jnp.where(
        causal, jnp.exp(jnp.where(causal, gap, 0.0)) * inner[..., None], 0.0
    ) * row_step[:, :, None, :, :]
    local_part = jnp.sum(coefficient[..., None] * row_input[:, :, None], axis=1)
    value = (
        jnp.exp(cum_logd)[..., None] * from_prompt
        + local_part
        + skip_gain.reshape(group_count, per_group, 1) * row_input
    )
    new_output = value.reshape(slots, steps, -1).astype(jnp.bfloat16)
    partial_value = jnp.einsum(
        "jup,pd->jud",
        exchange_ctx(jnp.concatenate([new_output] * count, axis=0), False),
        out_weight,
        preferred_element_type=jnp.float32,
    )
    decoded = lax.psum(partial_value, "heads").astype(jnp.bfloat16)

    entering = prefix_states(states, totals)
    prefill_out = finish(
        jnp.stack([term[2] for term in terms]),
        jnp.stack([term[0] for term in terms]),
        c_proj,
        entering,
        ssm_input,
        skip_gain,
    )
    return (prefill_out, decoded)


def solution(mesh):
    in_specs = (
        P("groups", "ctx", "heads"),
        P("groups", "ctx", "heads"),
        P("groups", "ctx", "heads"),
        P("groups", "heads", "ctx"),
        P("groups", "heads", "ctx"),
        P("heads"),
        P(("groups", "ctx")),
        P(("groups", "ctx"), None, "heads"),
        P(("groups", "ctx"), None, "heads"),
        P(("groups", "ctx"), None, "heads"),
        P(("groups", "ctx"), None, "heads"),
        P(("groups", "ctx"), None, "heads"),
        P("heads", "ctx"),
    )
    out_specs = (P("groups", "ctx", "heads"), P("groups", None, "ctx"))
    return jax.shard_map(shards, mesh=mesh, in_specs=in_specs, out_specs=out_specs, check_vma=False)
```

```python
import jax
import jax.numpy as jnp
from jax import lax
from jax.sharding import PartitionSpec as P

HEADS = 128
HEAD_DIM = 64
STATE = 128
GROUPS = 4

HIGH = lax.Precision.HIGHEST


def block_terms(block_input, block_b, block_c, block_step, block_logd):
    block_size = block_input.shape[0]
    head_count = block_step.shape[0]
    per_group = HEADS // GROUPS
    group_count = head_count // per_group
    cumulative = jnp.cumsum(block_logd, axis=1)
    block_total = cumulative[:, -1]
    inputs_head = block_input.reshape(block_size, group_count, per_group, HEAD_DIM)
    b_groups = block_b.reshape(block_size, group_count, STATE)
    c_groups = block_c.reshape(block_size, group_count, STATE)
    scores = jnp.einsum("tgn,sgn->gts", c_groups, b_groups, preferred_element_type=jnp.float32)
    row_index = lax.broadcasted_iota(jnp.int32, (block_size, block_size), 0)
    col_index = lax.broadcasted_iota(jnp.int32, (block_size, block_size), 1)
    causal = row_index >= col_index
    log_gap = cumulative[:, :, None] - cumulative[:, None, :]
    decay_rate = (
        jnp.where(causal, jnp.exp(jnp.where(causal, log_gap, 0.0)), 0.0) * block_step[:, None, :]
    )
    mixing = (
        scores[:, None, :, :] * decay_rate.reshape(group_count, per_group, block_size, block_size)
    ).astype(jnp.bfloat16)
    local_out = jnp.einsum(
        "gkts,sgkp->gktp", mixing, inputs_head, preferred_element_type=jnp.float32
    )
    weighting = jnp.exp(block_total[:, None] - cumulative) * block_step
    weighted = (weighting.T.reshape(block_size, group_count, per_group, 1) * inputs_head).astype(
        jnp.bfloat16
    )
    block_state = jnp.einsum(
        "sgkp,sgn->gkpn", weighted, b_groups, preferred_element_type=jnp.float32
    )
    return (cumulative, block_total.reshape(group_count, per_group), local_out, block_state)


def finish(local_out, cumulative, c_proj, entering, ssm_input, skip_gain):
    request_count, group_count, per_group, block_size = local_out.shape[:4]
    c_groups = c_proj.reshape(request_count, block_size, group_count, STATE)
    flat = entering.reshape(request_count, group_count, per_group * HEAD_DIM, STATE)
    high = flat.astype(jnp.bfloat16)
    low = (flat - high.astype(jnp.float32)).astype(jnp.bfloat16)
    numbers = (((3,), (3,)), ((0, 2), (0, 1)))
    carried = lax.dot_general(
        c_groups, high, numbers, preferred_element_type=jnp.float32
    ) + lax.dot_general(c_groups, low, numbers, preferred_element_type=jnp.float32)
    carried = carried.reshape(request_count, group_count, block_size, per_group, HEAD_DIM)
    growth = jnp.exp(cumulative).reshape(request_count, group_count, per_group, block_size)
    carried = carried * growth.transpose(0, 1, 3, 2)[..., None]
    inputs_head = ssm_input.reshape(
        request_count, block_size, group_count, per_group, HEAD_DIM
    ).astype(jnp.float32)
    skipped = skip_gain.reshape(group_count, per_group, 1) * inputs_head
    total = carried.transpose(0, 2, 1, 3, 4) + local_out.transpose(0, 3, 1, 2, 4) + skipped
    return total.reshape(request_count, block_size, -1).astype(jnp.bfloat16)


def range_decay(all_totals, low, high):
    place = lax.broadcasted_iota(jnp.int32, all_totals.shape, 0)
    keep = (place >= low) & (place <= high)
    return jnp.exp(jnp.sum(jnp.where(keep, all_totals, 0.0), axis=0))


def scale(factor, state):
    return factor[..., None, None] * state


def send(value, total, pairs):
    state, total = lax.ppermute((value.astype(jnp.bfloat16), total), "ctx", pairs)
    return state.astype(jnp.float32), total


def gather_ctx(value):
    count = lax.axis_size("ctx")
    if count & (count - 1):
        return lax.all_gather(value, "ctx", axis=0, tiled=True)
    place = lax.axis_index("ctx")
    reach = 1
    while reach < count:
        got = lax.ppermute(value, "ctx", [(i, i ^ reach) for i in range(count)])
        upper = (place & reach) != 0
        value = jnp.where(
            upper, jnp.concatenate([got, value], axis=0), jnp.concatenate([value, got], axis=0)
        )
        reach *= 2
    return value


def reduce_scatter_ctx(value):
    count = lax.axis_size("ctx")
    if count & (count - 1):
        return lax.psum_scatter(value, "ctx", scatter_dimension=0, tiled=True)
    place = lax.axis_index("ctx")
    reach = 1
    while reach < count:
        pairs = value.reshape((value.shape[0] // 2, 2) + value.shape[1:])
        upper = (place & reach) != 0
        keep = jnp.where(upper, pairs[:, 1], pairs[:, 0])
        give = jnp.where(upper, pairs[:, 0], pairs[:, 1])
        value = keep + lax.ppermute(give, "ctx", [(i, i ^ reach) for i in range(count)])
        reach *= 2
    return value


def chain_columns(window, window_total, column, columns):
    chunks = window.shape[0]
    growth = jnp.exp(window_total)
    entering = [jnp.zeros_like(window[k]) for k in range(chunks)]
    for stage in range(columns - 1 + chunks - 1):
        senders = [m for m in range(columns - 1) if 0 <= stage - m < chunks]
        pairs = [(y + 2 * m, y + 2 * (m + 1)) for y in range(2) for m in senders]
        outgoing = jnp.zeros_like(window[0])
        for k in range(chunks):
            leaving = scale(growth[k], entering[k]) + window[k]
            outgoing = jnp.where(stage - column == k, leaving, outgoing)
        got = lax.ppermute(outgoing.astype(jnp.bfloat16), "ctx", pairs).astype(jnp.float32)
        for k in range(chunks):
            entering[k] = jnp.where(stage - column + 1 == k, got, entering[k])
    return jnp.stack(entering)


def prefix_states(states, totals):
    count = lax.axis_size("ctx")
    columns = count // 2
    place = lax.axis_index("ctx")
    row_zero = place % 2 == 0
    column = place // 2
    half = states.shape[-2] // 2
    first = states[..., :half, :]
    second = states[..., half:, :]
    mine = jnp.where(row_zero, first, second)
    other = jnp.where(row_zero, second, first)
    across = [(2 * m, 2 * m + 1) for m in range(columns)] + [
        (2 * m + 1, 2 * m) for m in range(columns)
    ]
    received, partner_total = send(other, totals, across)
    even_state = jnp.where(row_zero, mine, received)
    odd_state = jnp.where(row_zero, received, mine)
    even_total = jnp.where(row_zero, totals, partner_total)
    odd_total = jnp.where(row_zero, partner_total, totals)
    window = scale(jnp.exp(odd_total), even_state) + odd_state
    window_total = even_total + odd_total
    if columns <= 4:
        before = chain_columns(window, window_total, column, columns)
    else:
        before = jnp.zeros_like(window)
        before_total = jnp.zeros_like(totals)
        step = 1
        while step < columns:
            pairs = [
                (y + 2 * m, y + 2 * (m + step)) for y in range(2) for m in range(columns - step)
            ]
            got, got_total = send(window, window_total, pairs)
            new_before = scale(jnp.exp(before_total), got) + before
            if 2 * step < columns:
                window = scale(jnp.exp(window_total), got) + window
                window_total = got_total + window_total
            before = new_before
            before_total = got_total + before_total
            step *= 2
    odd_entering = scale(jnp.exp(even_total), before) + even_state
    outgoing = jnp.where(row_zero, odd_entering, before)
    partner, _ = send(outgoing, totals, across)
    own_half = jnp.where(row_zero, before, odd_entering)
    first_half = jnp.where(row_zero, own_half, partner)
    second_half = jnp.where(row_zero, partner, own_half)
    return jnp.concatenate([first_half, second_half], axis=-2)


def shards(
    ssm_input,
    b_proj,
    c_proj,
    step_size,
    log_decay,
    skip_gain,
    request_of_slot,
    new_input,
    new_b,
    new_c,
    new_step,
    new_log_decay,
    out_weight,
):
    request_count = ssm_input.shape[0]
    count = lax.axis_size("ctx")
    place = lax.axis_index("ctx")
    terms = []
    for request in range(request_count):
        terms.append(
            block_terms(
                ssm_input[request],
                b_proj[request],
                c_proj[request],
                step_size[request],
                log_decay[request],
            )
        )
    totals = jnp.stack([term[1] for term in terms])
    states = jnp.stack([term[3] for term in terms])
    group_count, per_group = totals.shape[1], totals.shape[2]

    slots, steps = new_input.shape[0], new_input.shape[1]
    pieces = [totals, request_of_slot.astype(jnp.float32), new_c.astype(jnp.float32)]
    packed = jnp.concatenate([piece.reshape(-1) for piece in pieces])
    gathered = gather_ctx(packed[None])
    unpacked = []
    offset = 0
    for piece in pieces:
        size = piece.size
        unpacked.append(
            gathered[:, offset : offset + size].reshape((count,) + piece.shape)
        )
        offset += size
    all_totals, all_request, all_c = unpacked
    all_slots = count * slots
    all_request = all_request.reshape(all_slots)
    all_c = all_c.reshape(all_slots, steps, group_count, STATE)

    later = range_decay(all_totals, place + 1, count - 1)
    weighted_states = scale(later, states)
    high = weighted_states.astype(jnp.bfloat16)
    low = (weighted_states - high.astype(jnp.float32)).astype(jnp.bfloat16)
    c_rows = all_c.astype(jnp.bfloat16)
    projected = jnp.einsum(
        "rgkpn,jugn->rjugkp", high, c_rows, preferred_element_type=jnp.float32
    ) + jnp.einsum("rgkpn,jugn->rjugkp", low, c_rows, preferred_element_type=jnp.float32)
    contribution = projected[0]
    for request in range(1, request_count):
        pick = (all_request == request)[:, None, None, None, None]
        contribution = jnp.where(pick, projected[request], contribution)
    from_prompt = reduce_scatter_ctx(contribution)

    row_input = new_input.reshape(slots, steps, group_count, per_group, HEAD_DIM).astype(
        jnp.float32
    )
    row_b = new_b.reshape(slots, steps, group_count, STATE).astype(jnp.float32)
    row_c = new_c.reshape(slots, steps, group_count, STATE).astype(jnp.float32)
    row_step = new_step.reshape(slots, steps, group_count, per_group)
    row_logd = new_log_decay.reshape(slots, steps, group_count, per_group)
    cum_logd = jnp.cumsum(row_logd, axis=1)
    inner = jnp.einsum("jvgn,jugn->jvug", row_b, row_c, precision=HIGH)
    order_v = lax.broadcasted_iota(jnp.int32, (steps, steps), 0)
    order_u = lax.broadcasted_iota(jnp.int32, (steps, steps), 1)
    causal = (order_v <= order_u)[None, :, :, None, None]
    gap = cum_logd[:, None, :, :, :] - cum_logd[:, :, None, :, :]
    coefficient = jnp.where(
        causal, jnp.exp(jnp.where(causal, gap, 0.0)) * inner[..., None], 0.0
    ) * row_step[:, :, None, :, :]
    local_part = jnp.sum(coefficient[..., None] * row_input[:, :, None], axis=1)
    value = (
        jnp.exp(cum_logd)[..., None] * from_prompt
        + local_part
        + skip_gain.reshape(group_count, per_group, 1) * row_input
    )
    new_output = value.reshape(slots, steps, -1).astype(jnp.bfloat16)
    partial_value = jnp.einsum(
        "jup,pd->jud",
        gather_ctx(new_output),
        out_weight,
        preferred_element_type=jnp.float32,
    )
    decoded = lax.psum(partial_value, "heads").astype(jnp.bfloat16)

    entering = prefix_states(states, totals)
    prefill_out = finish(
        jnp.stack([term[2] for term in terms]),
        jnp.stack([term[0] for term in terms]),
        c_proj,
        entering,
        ssm_input,
        skip_gain,
    )
    return (prefill_out, decoded)


def solution(mesh):
    in_specs = (
        P("groups", "ctx", "heads"),
        P("groups", "ctx", "heads"),
        P("groups", "ctx", "heads"),
        P("groups", "heads", "ctx"),
        P("groups", "heads", "ctx"),
        P("heads"),
        P(("groups", "ctx")),
        P(("groups", "ctx"), None, "heads"),
        P(("groups", "ctx"), None, "heads"),
        P(("groups", "ctx"), None, "heads"),
        P(("groups", "ctx"), None, "heads"),
        P(("groups", "ctx"), None, "heads"),
        P("heads", "ctx"),
    )
    out_specs = (P("groups", "ctx", "heads"), P("groups", None, "ctx"))
    return jax.shard_map(shards, mesh=mesh, in_specs=in_specs, out_specs=out_specs, check_vma=False)
```

```python
import jax
import jax.numpy as jnp
from jax import lax
from jax.sharding import PartitionSpec as P

HEADS = 128
HEAD_DIM = 64
STATE = 128
GROUPS = 4

HIGH = lax.Precision.HIGHEST


def block_terms(block_input, block_b, block_c, block_step, block_logd):
    block_size = block_input.shape[0]
    head_count = block_step.shape[0]
    per_group = HEADS // GROUPS
    group_count = head_count // per_group
    cumulative = jnp.cumsum(block_logd, axis=1)
    block_total = cumulative[:, -1]
    inputs_head = block_input.reshape(block_size, group_count, per_group, HEAD_DIM)
    b_groups = block_b.reshape(block_size, group_count, STATE)
    c_groups = block_c.reshape(block_size, group_count, STATE)
    scores = jnp.einsum("tgn,sgn->gts", c_groups, b_groups, preferred_element_type=jnp.float32)
    row_index = lax.broadcasted_iota(jnp.int32, (block_size, block_size), 0)
    col_index = lax.broadcasted_iota(jnp.int32, (block_size, block_size), 1)
    causal = row_index >= col_index
    log_gap = cumulative[:, :, None] - cumulative[:, None, :]
    decay_rate = (
        jnp.where(causal, jnp.exp(jnp.where(causal, log_gap, 0.0)), 0.0) * block_step[:, None, :]
    )
    mixing = (
        scores[:, None, :, :] * decay_rate.reshape(group_count, per_group, block_size, block_size)
    ).astype(jnp.bfloat16)
    local_out = jnp.einsum(
        "gkts,sgkp->gktp", mixing, inputs_head, preferred_element_type=jnp.float32
    )
    weighting = jnp.exp(block_total[:, None] - cumulative) * block_step
    weighted = (weighting.T.reshape(block_size, group_count, per_group, 1) * inputs_head).astype(
        jnp.bfloat16
    )
    block_state = jnp.einsum(
        "sgkp,sgn->gkpn", weighted, b_groups, preferred_element_type=jnp.float32
    )
    return (cumulative, block_total.reshape(group_count, per_group), local_out, block_state)


def finish(local_out, cumulative, c_proj, entering, ssm_input, skip_gain):
    request_count, group_count, per_group, block_size = local_out.shape[:4]
    c_groups = c_proj.reshape(request_count, block_size, group_count, STATE)
    flat = entering.reshape(request_count, group_count, per_group * HEAD_DIM, STATE)
    high = flat.astype(jnp.bfloat16)
    low = (flat - high.astype(jnp.float32)).astype(jnp.bfloat16)
    numbers = (((3,), (3,)), ((0, 2), (0, 1)))
    carried = lax.dot_general(
        c_groups, high, numbers, preferred_element_type=jnp.float32
    ) + lax.dot_general(c_groups, low, numbers, preferred_element_type=jnp.float32)
    carried = carried.reshape(request_count, group_count, block_size, per_group, HEAD_DIM)
    growth = jnp.exp(cumulative).reshape(request_count, group_count, per_group, block_size)
    carried = carried * growth.transpose(0, 1, 3, 2)[..., None]
    inputs_head = ssm_input.reshape(
        request_count, block_size, group_count, per_group, HEAD_DIM
    ).astype(jnp.float32)
    skipped = skip_gain.reshape(group_count, per_group, 1) * inputs_head
    total = carried.transpose(0, 2, 1, 3, 4) + local_out.transpose(0, 3, 1, 2, 4) + skipped
    return total.reshape(request_count, block_size, -1).astype(jnp.bfloat16)


def range_decay(all_totals, low, high):
    place = lax.broadcasted_iota(jnp.int32, all_totals.shape, 0)
    keep = (place >= low) & (place <= high)
    return jnp.exp(jnp.sum(jnp.where(keep, all_totals, 0.0), axis=0))


def scale(factor, state):
    return factor[..., None, None] * state


def send(value, total, pairs):
    state, total = lax.ppermute((value.astype(jnp.bfloat16), total), "ctx", pairs)
    return state.astype(jnp.float32), total


def gather_ctx(value):
    count = lax.axis_size("ctx")
    if count & (count - 1):
        return lax.all_gather(value, "ctx", axis=0, tiled=True)
    place = lax.axis_index("ctx")
    reach = 1
    while reach < count:
        got = lax.ppermute(value, "ctx", [(i, i ^ reach) for i in range(count)])
        upper = (place & reach) != 0
        value = jnp.where(
            upper, jnp.concatenate([got, value], axis=0), jnp.concatenate([value, got], axis=0)
        )
        reach *= 2
    return value


def reduce_scatter_ctx(value):
    count = lax.axis_size("ctx")
    if count & (count - 1):
        return lax.psum_scatter(value, "ctx", scatter_dimension=0, tiled=True)
    place = lax.axis_index("ctx")
    reach = count // 2
    while reach >= 1:
        pairs = value.reshape((2, value.shape[0] // 2) + value.shape[1:])
        upper = (place & reach) != 0
        keep = jnp.where(upper, pairs[1], pairs[0])
        give = jnp.where(upper, pairs[0], pairs[1])
        value = keep + lax.ppermute(give, "ctx", [(i, i ^ reach) for i in range(count)])
        reach //= 2
    return value


def chain_columns(window, window_total, column, columns):
    chunks = window.shape[0]
    growth = jnp.exp(window_total)
    entering = [jnp.zeros_like(window[k]) for k in range(chunks)]
    for stage in range(columns - 1 + chunks - 1):
        senders = [m for m in range(columns - 1) if 0 <= stage - m < chunks]
        pairs = [(y + 2 * m, y + 2 * (m + 1)) for y in range(2) for m in senders]
        outgoing = jnp.zeros_like(window[0])
        for k in range(chunks):
            leaving = scale(growth[k], entering[k]) + window[k]
            outgoing = jnp.where(stage - column == k, leaving, outgoing)
        got = lax.ppermute(outgoing.astype(jnp.bfloat16), "ctx", pairs).astype(jnp.float32)
        for k in range(chunks):
            entering[k] = jnp.where(stage - column + 1 == k, got, entering[k])
    return jnp.stack(entering)


def prefix_states(states, totals):
    count = lax.axis_size("ctx")
    columns = count // 2
    place = lax.axis_index("ctx")
    row_zero = place % 2 == 0
    column = place // 2
    half = states.shape[-2] // 2
    first = states[..., :half, :]
    second = states[..., half:, :]
    mine = jnp.where(row_zero, first, second)
    other = jnp.where(row_zero, second, first)
    across = [(2 * m, 2 * m + 1) for m in range(columns)] + [
        (2 * m + 1, 2 * m) for m in range(columns)
    ]
    received, partner_total = send(other, totals, across)
    even_state = jnp.where(row_zero, mine, received)
    odd_state = jnp.where(row_zero, received, mine)
    even_total = jnp.where(row_zero, totals, partner_total)
    odd_total = jnp.where(row_zero, partner_total, totals)
    window = scale(jnp.exp(odd_total), even_state) + odd_state
    window_total = even_total + odd_total
    if columns <= 4:
        before = chain_columns(window, window_total, column, columns)
    else:
        before = jnp.zeros_like(window)
        before_total = jnp.zeros_like(totals)
        step = 1
        while step < columns:
            pairs = [
                (y + 2 * m, y + 2 * (m + step)) for y in range(2) for m in range(columns - step)
            ]
            got, got_total = send(window, window_total, pairs)
            new_before = scale(jnp.exp(before_total), got) + before
            if 2 * step < columns:
                window = scale(jnp.exp(window_total), got) + window
                window_total = got_total + window_total
            before = new_before
            before_total = got_total + before_total
            step *= 2
    odd_entering = scale(jnp.exp(even_total), before) + even_state
    outgoing = jnp.where(row_zero, odd_entering, before)
    partner, _ = send(outgoing, totals, across)
    own_half = jnp.where(row_zero, before, odd_entering)
    first_half = jnp.where(row_zero, own_half, partner)
    second_half = jnp.where(row_zero, partner, own_half)
    return jnp.concatenate([first_half, second_half], axis=-2)


def shards(
    ssm_input,
    b_proj,
    c_proj,
    step_size,
    log_decay,
    skip_gain,
    request_of_slot,
    new_input,
    new_b,
    new_c,
    new_step,
    new_log_decay,
    out_weight,
):
    request_count = ssm_input.shape[0]
    count = lax.axis_size("ctx")
    place = lax.axis_index("ctx")
    terms = []
    for request in range(request_count):
        terms.append(
            block_terms(
                ssm_input[request],
                b_proj[request],
                c_proj[request],
                step_size[request],
                log_decay[request],
            )
        )
    totals = jnp.stack([term[1] for term in terms])
    states = jnp.stack([term[3] for term in terms])
    group_count, per_group = totals.shape[1], totals.shape[2]

    slots, steps = new_input.shape[0], new_input.shape[1]
    pieces = [totals, request_of_slot.astype(jnp.float32), new_c.astype(jnp.float32)]
    packed = jnp.concatenate([piece.reshape(-1) for piece in pieces])
    gathered = gather_ctx(packed[None])
    unpacked = []
    offset = 0
    for piece in pieces:
        size = piece.size
        unpacked.append(
            gathered[:, offset : offset + size].reshape((count,) + piece.shape)
        )
        offset += size
    all_totals, all_request, all_c = unpacked
    all_slots = count * slots
    all_request = all_request.reshape(all_slots)
    all_c = all_c.reshape(all_slots, steps, group_count, STATE)

    later = range_decay(all_totals, place + 1, count - 1)
    weighted_states = scale(later, states)
    high = weighted_states.astype(jnp.bfloat16)
    low = (weighted_states - high.astype(jnp.float32)).astype(jnp.bfloat16)
    c_rows = all_c.astype(jnp.bfloat16)
    projected = jnp.einsum(
        "rgkpn,jugn->rjugkp", high, c_rows, preferred_element_type=jnp.float32
    ) + jnp.einsum("rgkpn,jugn->rjugkp", low, c_rows, preferred_element_type=jnp.float32)
    contribution = projected[0]
    for request in range(1, request_count):
        pick = (all_request == request)[:, None, None, None, None]
        contribution = jnp.where(pick, projected[request], contribution)
    from_prompt = reduce_scatter_ctx(contribution)

    row_input = new_input.reshape(slots, steps, group_count, per_group, HEAD_DIM).astype(
        jnp.float32
    )
    row_b = new_b.reshape(slots, steps, group_count, STATE).astype(jnp.float32)
    row_c = new_c.reshape(slots, steps, group_count, STATE).astype(jnp.float32)
    row_step = new_step.reshape(slots, steps, group_count, per_group)
    row_logd = new_log_decay.reshape(slots, steps, group_count, per_group)
    cum_logd = jnp.cumsum(row_logd, axis=1)
    inner = jnp.einsum("jvgn,jugn->jvug", row_b, row_c, precision=HIGH)
    order_v = lax.broadcasted_iota(jnp.int32, (steps, steps), 0)
    order_u = lax.broadcasted_iota(jnp.int32, (steps, steps), 1)
    causal = (order_v <= order_u)[None, :, :, None, None]
    gap = cum_logd[:, None, :, :, :] - cum_logd[:, :, None, :, :]
    coefficient = jnp.where(
        causal, jnp.exp(jnp.where(causal, gap, 0.0)) * inner[..., None], 0.0
    ) * row_step[:, :, None, :, :]
    local_part = jnp.sum(coefficient[..., None] * row_input[:, :, None], axis=1)
    value = (
        jnp.exp(cum_logd)[..., None] * from_prompt
        + local_part
        + skip_gain.reshape(group_count, per_group, 1) * row_input
    )
    new_output = value.reshape(slots, steps, -1).astype(jnp.bfloat16)
    partial_value = jnp.einsum(
        "jup,pd->jud",
        gather_ctx(new_output),
        out_weight,
        preferred_element_type=jnp.float32,
    )
    decoded = lax.psum(partial_value, "heads").astype(jnp.bfloat16)

    entering = prefix_states(states, totals)
    prefill_out = finish(
        jnp.stack([term[2] for term in terms]),
        jnp.stack([term[0] for term in terms]),
        c_proj,
        entering,
        ssm_input,
        skip_gain,
    )
    return (prefill_out, decoded)


def solution(mesh):
    in_specs = (
        P("groups", "ctx", "heads"),
        P("groups", "ctx", "heads"),
        P("groups", "ctx", "heads"),
        P("groups", "heads", "ctx"),
        P("groups", "heads", "ctx"),
        P("heads"),
        P(("groups", "ctx")),
        P(("groups", "ctx"), None, "heads"),
        P(("groups", "ctx"), None, "heads"),
        P(("groups", "ctx"), None, "heads"),
        P(("groups", "ctx"), None, "heads"),
        P(("groups", "ctx"), None, "heads"),
        P("heads", "ctx"),
    )
    out_specs = (P("groups", "ctx", "heads"), P("groups", None, "ctx"))
    return jax.shard_map(shards, mesh=mesh, in_specs=in_specs, out_specs=out_specs, check_vma=False)
```

```python
import jax
import jax.numpy as jnp
from jax import lax
from jax.sharding import PartitionSpec as P

HEADS = 128
HEAD_DIM = 64
STATE = 128
GROUPS = 4

HIGH = lax.Precision.HIGHEST


def block_terms(block_input, block_b, block_c, block_step, block_logd):
    block_size = block_input.shape[0]
    head_count = block_step.shape[0]
    per_group = HEADS // GROUPS
    group_count = head_count // per_group
    cumulative = jnp.cumsum(block_logd, axis=1)
    block_total = cumulative[:, -1]
    inputs_head = block_input.reshape(block_size, group_count, per_group, HEAD_DIM)
    b_groups = block_b.reshape(block_size, group_count, STATE)
    c_groups = block_c.reshape(block_size, group_count, STATE)
    scores = jnp.einsum("tgn,sgn->gts", c_groups, b_groups, preferred_element_type=jnp.float32)
    row_index = lax.broadcasted_iota(jnp.int32, (block_size, block_size), 0)
    col_index = lax.broadcasted_iota(jnp.int32, (block_size, block_size), 1)
    causal = row_index >= col_index
    log_gap = cumulative[:, :, None] - cumulative[:, None, :]
    decay_rate = (
        jnp.where(causal, jnp.exp(jnp.where(causal, log_gap, 0.0)), 0.0) * block_step[:, None, :]
    )
    mixing = (
        scores[:, None, :, :] * decay_rate.reshape(group_count, per_group, block_size, block_size)
    ).astype(jnp.bfloat16)
    local_out = jnp.einsum(
        "gkts,sgkp->gktp", mixing, inputs_head, preferred_element_type=jnp.float32
    )
    weighting = jnp.exp(block_total[:, None] - cumulative) * block_step
    weighted = (weighting.T.reshape(block_size, group_count, per_group, 1) * inputs_head).astype(
        jnp.bfloat16
    )
    block_state = jnp.einsum(
        "sgkp,sgn->gkpn", weighted, b_groups, preferred_element_type=jnp.float32
    )
    return (cumulative, block_total.reshape(group_count, per_group), local_out, block_state)


def finish(local_out, cumulative, c_proj, entering, ssm_input, skip_gain):
    request_count, group_count, per_group, block_size = local_out.shape[:4]
    c_groups = c_proj.reshape(request_count, block_size, group_count, STATE)
    flat = entering.reshape(request_count, group_count, per_group * HEAD_DIM, STATE)
    high = flat.astype(jnp.bfloat16)
    low = (flat - high.astype(jnp.float32)).astype(jnp.bfloat16)
    numbers = (((3,), (3,)), ((0, 2), (0, 1)))
    carried = lax.dot_general(
        c_groups, high, numbers, preferred_element_type=jnp.float32
    ) + lax.dot_general(c_groups, low, numbers, preferred_element_type=jnp.float32)
    carried = carried.reshape(request_count, group_count, block_size, per_group, HEAD_DIM)
    growth = jnp.exp(cumulative).reshape(request_count, group_count, per_group, block_size)
    carried = carried * growth.transpose(0, 1, 3, 2)[..., None]
    inputs_head = ssm_input.reshape(
        request_count, block_size, group_count, per_group, HEAD_DIM
    ).astype(jnp.float32)
    skipped = skip_gain.reshape(group_count, per_group, 1) * inputs_head
    total = carried.transpose(0, 2, 1, 3, 4) + local_out.transpose(0, 3, 1, 2, 4) + skipped
    return total.reshape(request_count, block_size, -1).astype(jnp.bfloat16)


def range_decay(all_totals, low, high):
    place = lax.broadcasted_iota(jnp.int32, all_totals.shape, 0)
    keep = (place >= low) & (place <= high)
    return jnp.exp(jnp.sum(jnp.where(keep, all_totals, 0.0), axis=0))


def scale(factor, state):
    return factor[..., None, None] * state


def send(value, total, pairs):
    state, total = lax.ppermute((value.astype(jnp.bfloat16), total), "ctx", pairs)
    return state.astype(jnp.float32), total


def gather_ctx(value):
    count = lax.axis_size("ctx")
    if count & (count - 1):
        return lax.all_gather(value, "ctx", axis=0, tiled=True)
    place = lax.axis_index("ctx")
    reach = 1
    while reach < count:
        got = lax.ppermute(value, "ctx", [(i, i ^ reach) for i in range(count)])
        upper = (place & reach) != 0
        value = jnp.where(
            upper, jnp.concatenate([got, value], axis=0), jnp.concatenate([value, got], axis=0)
        )
        reach *= 2
    return value


def reduce_scatter_ctx(value):
    count = lax.axis_size("ctx")
    if count & (count - 1):
        return lax.psum_scatter(value, "ctx", scatter_dimension=0, tiled=True)
    place = lax.axis_index("ctx")
    reach = 1
    while reach < count:
        pairs = value.reshape((value.shape[0] // 2, 2) + value.shape[1:])
        upper = (place & reach) != 0
        keep = jnp.where(upper, pairs[:, 1], pairs[:, 0])
        give = jnp.where(upper, pairs[:, 0], pairs[:, 1])
        value = keep + lax.ppermute(give, "ctx", [(i, i ^ reach) for i in range(count)])
        reach *= 2
    return value


def chain_columns(window, window_total, column, columns):
    chunks = window.shape[0]
    growth = jnp.exp(window_total)
    entering = [jnp.zeros_like(window[k]) for k in range(chunks)]
    for stage in range(columns - 1 + chunks - 1):
        senders = [m for m in range(columns - 1) if 0 <= stage - m < chunks]
        pairs = [(y + 2 * m, y + 2 * (m + 1)) for y in range(2) for m in senders]
        outgoing = jnp.zeros_like(window[0])
        for k in range(chunks):
            leaving = scale(growth[k], entering[k]) + window[k]
            outgoing = jnp.where(stage - column == k, leaving, outgoing)
        got = lax.ppermute(outgoing.astype(jnp.bfloat16), "ctx", pairs).astype(jnp.float32)
        for k in range(chunks):
            entering[k] = jnp.where(stage - column + 1 == k, got, entering[k])
    return jnp.stack(entering)


def prefix_chunked(states, totals):
    count = lax.axis_size("ctx")
    columns = count // 2
    place = lax.axis_index("ctx")
    row_zero = place % 2 == 0
    column = place // 2
    half = states.shape[-2] // 2
    first = states[..., :half, :]
    second = states[..., half:, :]
    mine = jnp.where(row_zero, first, second)
    other = jnp.where(row_zero, second, first)
    across = [(2 * m, 2 * m + 1) for m in range(columns)] + [
        (2 * m + 1, 2 * m) for m in range(columns)
    ]
    chunks = states.shape[0]
    even_state, even_total, window, growth = [], [], [], []
    for k in range(chunks):
        received, partner_total = send(other[k], totals[k], across)
        even_state.append(jnp.where(row_zero, mine[k], received))
        odd_state = jnp.where(row_zero, received, mine[k])
        even_total.append(jnp.where(row_zero, totals[k], partner_total))
        odd_total = jnp.where(row_zero, partner_total, totals[k])
        window.append(scale(jnp.exp(odd_total), even_state[k]) + odd_state)
        growth.append(jnp.exp(even_total[k] + odd_total))
    entering = [jnp.zeros_like(window[k]) for k in range(chunks)]
    for stage in range(columns - 1 + chunks - 1):
        senders = [m for m in range(columns - 1) if 0 <= stage - m < chunks]
        pairs = [(y + 2 * m, y + 2 * (m + 1)) for y in range(2) for m in senders]
        sent = sorted({stage - m for m in senders})
        outgoing = jnp.zeros_like(window[0])
        for k in sent:
            leaving = scale(growth[k], entering[k]) + window[k]
            outgoing = jnp.where(stage - column == k, leaving, outgoing)
        got = lax.ppermute(outgoing.astype(jnp.bfloat16), "ctx", pairs).astype(jnp.float32)
        for k in sent:
            entering[k] = jnp.where(stage - column + 1 == k, got, entering[k])
    results = []
    for k in range(chunks):
        odd_entering = scale(jnp.exp(even_total[k]), entering[k]) + even_state[k]
        outgoing = jnp.where(row_zero, odd_entering, entering[k])
        partner, _ = send(outgoing, totals[k], across)
        own_half = jnp.where(row_zero, entering[k], odd_entering)
        first_half = jnp.where(row_zero, own_half, partner)
        second_half = jnp.where(row_zero, partner, own_half)
        results.append(jnp.concatenate([first_half, second_half], axis=-2))
    return jnp.stack(results)


def prefix_states(states, totals):
    count = lax.axis_size("ctx")
    columns = count // 2
    place = lax.axis_index("ctx")
    row_zero = place % 2 == 0
    column = place // 2
    half = states.shape[-2] // 2
    first = states[..., :half, :]
    second = states[..., half:, :]
    mine = jnp.where(row_zero, first, second)
    other = jnp.where(row_zero, second, first)
    across = [(2 * m, 2 * m + 1) for m in range(columns)] + [
        (2 * m + 1, 2 * m) for m in range(columns)
    ]
    received, partner_total = send(other, totals, across)
    even_state = jnp.where(row_zero, mine, received)
    odd_state = jnp.where(row_zero, received, mine)
    even_total = jnp.where(row_zero, totals, partner_total)
    odd_total = jnp.where(row_zero, partner_total, totals)
    window = scale(jnp.exp(odd_total), even_state) + odd_state
    window_total = even_total + odd_total
    if columns <= 4:
        before = chain_columns(window, window_total, column, columns)
    else:
        before = jnp.zeros_like(window)
        before_total = jnp.zeros_like(totals)
        step = 1
        while step < columns:
            pairs = [
                (y + 2 * m, y + 2 * (m + step)) for y in range(2) for m in range(columns - step)
            ]
            got, got_total = send(window, window_total, pairs)
            new_before = scale(jnp.exp(before_total), got) + before
            if 2 * step < columns:
                window = scale(jnp.exp(window_total), got) + window
                window_total = got_total + window_total
            before = new_before
            before_total = got_total + before_total
            step *= 2
    odd_entering = scale(jnp.exp(even_total), before) + even_state
    outgoing = jnp.where(row_zero, odd_entering, before)
    partner, _ = send(outgoing, totals, across)
    own_half = jnp.where(row_zero, before, odd_entering)
    first_half = jnp.where(row_zero, own_half, partner)
    second_half = jnp.where(row_zero, partner, own_half)
    return jnp.concatenate([first_half, second_half], axis=-2)


def shards(
    ssm_input,
    b_proj,
    c_proj,
    step_size,
    log_decay,
    skip_gain,
    request_of_slot,
    new_input,
    new_b,
    new_c,
    new_step,
    new_log_decay,
    out_weight,
):
    request_count = ssm_input.shape[0]
    count = lax.axis_size("ctx")
    place = lax.axis_index("ctx")
    terms = []
    for request in range(request_count):
        terms.append(
            block_terms(
                ssm_input[request],
                b_proj[request],
                c_proj[request],
                step_size[request],
                log_decay[request],
            )
        )
    totals = jnp.stack([term[1] for term in terms])
    states = jnp.stack([term[3] for term in terms])
    group_count, per_group = totals.shape[1], totals.shape[2]

    slots, steps = new_input.shape[0], new_input.shape[1]
    pieces = [totals, request_of_slot.astype(jnp.float32), new_c.astype(jnp.float32)]
    packed = jnp.concatenate([piece.reshape(-1) for piece in pieces])
    gathered = gather_ctx(packed[None])
    unpacked = []
    offset = 0
    for piece in pieces:
        size = piece.size
        unpacked.append(
            gathered[:, offset : offset + size].reshape((count,) + piece.shape)
        )
        offset += size
    all_totals, all_request, all_c = unpacked
    all_slots = count * slots
    all_request = all_request.reshape(all_slots)
    all_c = all_c.reshape(all_slots, steps, group_count, STATE)

    later = range_decay(all_totals, place + 1, count - 1)
    weighted_states = scale(later, states)
    high = weighted_states.astype(jnp.bfloat16)
    low = (weighted_states - high.astype(jnp.float32)).astype(jnp.bfloat16)
    c_rows = all_c.astype(jnp.bfloat16)
    projected = jnp.einsum(
        "rgkpn,jugn->rjugkp", high, c_rows, preferred_element_type=jnp.float32
    ) + jnp.einsum("rgkpn,jugn->rjugkp", low, c_rows, preferred_element_type=jnp.float32)
    contribution = projected[0]
    for request in range(1, request_count):
        pick = (all_request == request)[:, None, None, None, None]
        contribution = jnp.where(pick, projected[request], contribution)
    from_prompt = reduce_scatter_ctx(contribution)

    row_input = new_input.reshape(slots, steps, group_count, per_group, HEAD_DIM).astype(
        jnp.float32
    )
    row_b = new_b.reshape(slots, steps, group_count, STATE).astype(jnp.float32)
    row_c = new_c.reshape(slots, steps, group_count, STATE).astype(jnp.float32)
    row_step = new_step.reshape(slots, steps, group_count, per_group)
    row_logd = new_log_decay.reshape(slots, steps, group_count, per_group)
    cum_logd = jnp.cumsum(row_logd, axis=1)
    inner = jnp.einsum("jvgn,jugn->jvug", row_b, row_c, precision=HIGH)
    order_v = lax.broadcasted_iota(jnp.int32, (steps, steps), 0)
    order_u = lax.broadcasted_iota(jnp.int32, (steps, steps), 1)
    causal = (order_v <= order_u)[None, :, :, None, None]
    gap = cum_logd[:, None, :, :, :] - cum_logd[:, :, None, :, :]
    coefficient = jnp.where(
        causal, jnp.exp(jnp.where(causal, gap, 0.0)) * inner[..., None], 0.0
    ) * row_step[:, :, None, :, :]
    local_part = jnp.sum(coefficient[..., None] * row_input[:, :, None], axis=1)
    value = (
        jnp.exp(cum_logd)[..., None] * from_prompt
        + local_part
        + skip_gain.reshape(group_count, per_group, 1) * row_input
    )
    new_output = value.reshape(slots, steps, -1).astype(jnp.bfloat16)
    partial_value = jnp.einsum(
        "jup,pd->jud",
        gather_ctx(new_output),
        out_weight,
        preferred_element_type=jnp.float32,
    )
    decoded = lax.psum(partial_value, "heads").astype(jnp.bfloat16)

    if lax.axis_size("ctx") <= 8:
        entering = prefix_chunked(states, totals)
    else:
        entering = prefix_states(states, totals)
    prefill_out = finish(
        jnp.stack([term[2] for term in terms]),
        jnp.stack([term[0] for term in terms]),
        c_proj,
        entering,
        ssm_input,
        skip_gain,
    )
    return (prefill_out, decoded)


def solution(mesh):
    in_specs = (
        P("groups", "ctx", "heads"),
        P("groups", "ctx", "heads"),
        P("groups", "ctx", "heads"),
        P("groups", "heads", "ctx"),
        P("groups", "heads", "ctx"),
        P("heads"),
        P(("groups", "ctx")),
        P(("groups", "ctx"), None, "heads"),
        P(("groups", "ctx"), None, "heads"),
        P(("groups", "ctx"), None, "heads"),
        P(("groups", "ctx"), None, "heads"),
        P(("groups", "ctx"), None, "heads"),
        P("heads", "ctx"),
    )
    out_specs = (P("groups", "ctx", "heads"), P("groups", None, "ctx"))
    return jax.shard_map(shards, mesh=mesh, in_specs=in_specs, out_specs=out_specs, check_vma=False)
```

```python
import jax
import jax.numpy as jnp
from jax import lax
from jax.sharding import PartitionSpec as P

HEADS = 128
HEAD_DIM = 64
STATE = 128
GROUPS = 4

HIGH = lax.Precision.HIGHEST


def block_terms(block_input, block_b, block_c, block_step, block_logd):
    block_size = block_input.shape[0]
    head_count = block_step.shape[0]
    per_group = HEADS // GROUPS
    group_count = head_count // per_group
    cumulative = jnp.cumsum(block_logd, axis=1)
    block_total = cumulative[:, -1]
    inputs_head = block_input.reshape(block_size, group_count, per_group, HEAD_DIM)
    b_groups = block_b.reshape(block_size, group_count, STATE)
    c_groups = block_c.reshape(block_size, group_count, STATE)
    scores = jnp.einsum("tgn,sgn->gts", c_groups, b_groups, preferred_element_type=jnp.float32)
    row_index = lax.broadcasted_iota(jnp.int32, (block_size, block_size), 0)
    col_index = lax.broadcasted_iota(jnp.int32, (block_size, block_size), 1)
    causal = row_index >= col_index
    log_gap = cumulative[:, :, None] - cumulative[:, None, :]
    decay_rate = (
        jnp.where(causal, jnp.exp(jnp.where(causal, log_gap, 0.0)), 0.0) * block_step[:, None, :]
    )
    mixing = (
        scores[:, None, :, :] * decay_rate.reshape(group_count, per_group, block_size, block_size)
    ).astype(jnp.bfloat16)
    local_out = jnp.einsum(
        "gkts,sgkp->gktp", mixing, inputs_head, preferred_element_type=jnp.float32
    )
    weighting = jnp.exp(block_total[:, None] - cumulative) * block_step
    weighted = (weighting.T.reshape(block_size, group_count, per_group, 1) * inputs_head).astype(
        jnp.bfloat16
    )
    block_state = jnp.einsum(
        "sgkp,sgn->gkpn", weighted, b_groups, preferred_element_type=jnp.float32
    )
    return (cumulative, block_total.reshape(group_count, per_group), local_out, block_state)


def finish(local_out, cumulative, c_proj, entering, ssm_input, skip_gain):
    request_count, group_count, per_group, block_size = local_out.shape[:4]
    c_groups = c_proj.reshape(request_count, block_size, group_count, STATE)
    flat = entering.reshape(request_count, group_count, per_group * HEAD_DIM, STATE)
    high = flat.astype(jnp.bfloat16)
    low = (flat - high.astype(jnp.float32)).astype(jnp.bfloat16)
    numbers = (((3,), (3,)), ((0, 2), (0, 1)))
    carried = lax.dot_general(
        c_groups, high, numbers, preferred_element_type=jnp.float32
    ) + lax.dot_general(c_groups, low, numbers, preferred_element_type=jnp.float32)
    carried = carried.reshape(request_count, group_count, block_size, per_group, HEAD_DIM)
    growth = jnp.exp(cumulative).reshape(request_count, group_count, per_group, block_size)
    carried = carried * growth.transpose(0, 1, 3, 2)[..., None]
    inputs_head = ssm_input.reshape(
        request_count, block_size, group_count, per_group, HEAD_DIM
    ).astype(jnp.float32)
    skipped = skip_gain.reshape(group_count, per_group, 1) * inputs_head
    total = carried.transpose(0, 2, 1, 3, 4) + local_out.transpose(0, 3, 1, 2, 4) + skipped
    return total.reshape(request_count, block_size, -1).astype(jnp.bfloat16)


def range_decay(all_totals, low, high):
    place = lax.broadcasted_iota(jnp.int32, all_totals.shape, 0)
    keep = (place >= low) & (place <= high)
    return jnp.exp(jnp.sum(jnp.where(keep, all_totals, 0.0), axis=0))


def scale(factor, state):
    return factor[..., None, None] * state


def send(value, total, pairs):
    state, total = lax.ppermute((value.astype(jnp.bfloat16), total), "ctx", pairs)
    return state.astype(jnp.float32), total


def gather_ctx(value):
    count = lax.axis_size("ctx")
    if count & (count - 1):
        return lax.all_gather(value, "ctx", axis=0, tiled=True)
    place = lax.axis_index("ctx")
    reach = 1
    while reach < count:
        got = lax.ppermute(value, "ctx", [(i, i ^ reach) for i in range(count)])
        upper = (place & reach) != 0
        value = jnp.where(
            upper, jnp.concatenate([got, value], axis=0), jnp.concatenate([value, got], axis=0)
        )
        reach *= 2
    return value


def reduce_scatter_ctx(value):
    count = lax.axis_size("ctx")
    if count & (count - 1):
        return lax.psum_scatter(value, "ctx", scatter_dimension=0, tiled=True)
    place = lax.axis_index("ctx")
    reach = 1
    while reach < count:
        pairs = value.reshape((value.shape[0] // 2, 2) + value.shape[1:])
        upper = (place & reach) != 0
        keep = jnp.where(upper, pairs[:, 1], pairs[:, 0])
        give = jnp.where(upper, pairs[:, 0], pairs[:, 1])
        value = keep + lax.ppermute(give, "ctx", [(i, i ^ reach) for i in range(count)])
        reach *= 2
    return value


def exchange_ctx(value, total):
    count = lax.axis_size("ctx")
    got = lax.all_to_all(value, "ctx", 0, 0, tiled=True)
    got = got.reshape((count, value.shape[0] // count) + value.shape[1:])
    return jnp.sum(got, axis=0) if total else got.reshape(value.shape)


def chain_columns(window, window_total, column, columns):
    chunks = window.shape[0]
    growth = jnp.exp(window_total)
    entering = [jnp.zeros_like(window[k]) for k in range(chunks)]
    for stage in range(columns - 1 + chunks - 1):
        senders = [m for m in range(columns - 1) if 0 <= stage - m < chunks]
        pairs = [(y + 2 * m, y + 2 * (m + 1)) for y in range(2) for m in senders]
        outgoing = jnp.zeros_like(window[0])
        for k in range(chunks):
            leaving = scale(growth[k], entering[k]) + window[k]
            outgoing = jnp.where(stage - column == k, leaving, outgoing)
        got = lax.ppermute(outgoing.astype(jnp.bfloat16), "ctx", pairs).astype(jnp.float32)
        for k in range(chunks):
            entering[k] = jnp.where(stage - column + 1 == k, got, entering[k])
    return jnp.stack(entering)


def prefix_states(states, totals):
    count = lax.axis_size("ctx")
    columns = count // 2
    place = lax.axis_index("ctx")
    row_zero = place % 2 == 0
    column = place // 2
    half = states.shape[-2] // 2
    first = states[..., :half, :]
    second = states[..., half:, :]
    mine = jnp.where(row_zero, first, second)
    other = jnp.where(row_zero, second, first)
    across = [(2 * m, 2 * m + 1) for m in range(columns)] + [
        (2 * m + 1, 2 * m) for m in range(columns)
    ]
    received, partner_total = send(other, totals, across)
    even_state = jnp.where(row_zero, mine, received)
    odd_state = jnp.where(row_zero, received, mine)
    even_total = jnp.where(row_zero, totals, partner_total)
    odd_total = jnp.where(row_zero, partner_total, totals)
    window = scale(jnp.exp(odd_total), even_state) + odd_state
    window_total = even_total + odd_total
    if columns <= 4:
        before = chain_columns(window, window_total, column, columns)
    else:
        before = jnp.zeros_like(window)
        before_total = jnp.zeros_like(totals)
        step = 1
        while step < columns:
            pairs = [
                (y + 2 * m, y + 2 * (m + step)) for y in range(2) for m in range(columns - step)
            ]
            got, got_total = send(window, window_total, pairs)
            new_before = scale(jnp.exp(before_total), got) + before
            if 2 * step < columns:
                window = scale(jnp.exp(window_total), got) + window
                window_total = got_total + window_total
            before = new_before
            before_total = got_total + before_total
            step *= 2
    odd_entering = scale(jnp.exp(even_total), before) + even_state
    outgoing = jnp.where(row_zero, odd_entering, before)
    partner, _ = send(outgoing, totals, across)
    own_half = jnp.where(row_zero, before, odd_entering)
    first_half = jnp.where(row_zero, own_half, partner)
    second_half = jnp.where(row_zero, partner, own_half)
    return jnp.concatenate([first_half, second_half], axis=-2)


def shards(
    ssm_input,
    b_proj,
    c_proj,
    step_size,
    log_decay,
    skip_gain,
    request_of_slot,
    new_input,
    new_b,
    new_c,
    new_step,
    new_log_decay,
    out_weight,
):
    request_count = ssm_input.shape[0]
    count = lax.axis_size("ctx")
    place = lax.axis_index("ctx")
    terms = []
    for request in range(request_count):
        terms.append(
            block_terms(
                ssm_input[request],
                b_proj[request],
                c_proj[request],
                step_size[request],
                log_decay[request],
            )
        )
    totals = jnp.stack([term[1] for term in terms])
    states = jnp.stack([term[3] for term in terms])
    group_count, per_group = totals.shape[1], totals.shape[2]

    slots, steps = new_input.shape[0], new_input.shape[1]
    pieces = [totals, request_of_slot.astype(jnp.float32), new_c.astype(jnp.float32)]
    packed = jnp.concatenate([piece.reshape(-1) for piece in pieces])
    gathered = gather_ctx(packed[None])
    unpacked = []
    offset = 0
    for piece in pieces:
        size = piece.size
        unpacked.append(
            gathered[:, offset : offset + size].reshape((count,) + piece.shape)
        )
        offset += size
    all_totals, all_request, all_c = unpacked
    all_slots = count * slots
    all_request = all_request.reshape(all_slots)
    all_c = all_c.reshape(all_slots, steps, group_count, STATE)

    later = range_decay(all_totals, place + 1, count - 1)
    weighted_states = scale(later, states)
    high = weighted_states.astype(jnp.bfloat16)
    low = (weighted_states - high.astype(jnp.float32)).astype(jnp.bfloat16)
    c_rows = all_c.astype(jnp.bfloat16)
    projected = jnp.einsum(
        "rgkpn,jugn->rjugkp", high, c_rows, preferred_element_type=jnp.float32
    ) + jnp.einsum("rgkpn,jugn->rjugkp", low, c_rows, preferred_element_type=jnp.float32)
    contribution = projected[0]
    for request in range(1, request_count):
        pick = (all_request == request)[:, None, None, None, None]
        contribution = jnp.where(pick, projected[request], contribution)
    from_prompt = exchange_ctx(contribution, True)

    row_input = new_input.reshape(slots, steps, group_count, per_group, HEAD_DIM).astype(
        jnp.float32
    )
    row_b = new_b.reshape(slots, steps, group_count, STATE).astype(jnp.float32)
    row_c = new_c.reshape(slots, steps, group_count, STATE).astype(jnp.float32)
    row_step = new_step.reshape(slots, steps, group_count, per_group)
    row_logd = new_log_decay.reshape(slots, steps, group_count, per_group)
    cum_logd = jnp.cumsum(row_logd, axis=1)
    inner = jnp.einsum("jvgn,jugn->jvug", row_b, row_c, precision=HIGH)
    order_v = lax.broadcasted_iota(jnp.int32, (steps, steps), 0)
    order_u = lax.broadcasted_iota(jnp.int32, (steps, steps), 1)
    causal = (order_v <= order_u)[None, :, :, None, None]
    gap = cum_logd[:, None, :, :, :] - cum_logd[:, :, None, :, :]
    coefficient = jnp.where(
        causal, jnp.exp(jnp.where(causal, gap, 0.0)) * inner[..., None], 0.0
    ) * row_step[:, :, None, :, :]
    local_part = jnp.sum(coefficient[..., None] * row_input[:, :, None], axis=1)
    value = (
        jnp.exp(cum_logd)[..., None] * from_prompt
        + local_part
        + skip_gain.reshape(group_count, per_group, 1) * row_input
    )
    new_output = value.reshape(slots, steps, -1).astype(jnp.bfloat16)
    partial_value = jnp.einsum(
        "jup,pd->jud",
        exchange_ctx(jnp.concatenate([new_output] * count, axis=0), False),
        out_weight,
        preferred_element_type=jnp.float32,
    )
    decoded = lax.psum(partial_value, "heads").astype(jnp.bfloat16)

    entering = prefix_states(states, totals)
    prefill_out = finish(
        jnp.stack([term[2] for term in terms]),
        jnp.stack([term[0] for term in terms]),
        c_proj,
        entering,
        ssm_input,
        skip_gain,
    )
    return (prefill_out, decoded)


def solution(mesh):
    in_specs = (
        P("groups", "ctx", "heads"),
        P("groups", "ctx", "heads"),
        P("groups", "ctx", "heads"),
        P("groups", "heads", "ctx"),
        P("groups", "heads", "ctx"),
        P("heads"),
        P(("groups", "ctx")),
        P(("groups", "ctx"), None, "heads"),
        P(("groups", "ctx"), None, "heads"),
        P(("groups", "ctx"), None, "heads"),
        P(("groups", "ctx"), None, "heads"),
        P(("groups", "ctx"), None, "heads"),
        P("heads", "ctx"),
    )
    out_specs = (P("groups", "ctx", "heads"), P("groups", None, "ctx"))
    return jax.shard_map(shards, mesh=mesh, in_specs=in_specs, out_specs=out_specs, check_vma=False)
```

```python
import jax
import jax.numpy as jnp
from jax import lax
from jax.sharding import PartitionSpec as P

HEADS = 128
HEAD_DIM = 64
STATE = 128
GROUPS = 4

HIGH = lax.Precision.HIGHEST


def block_terms(block_input, block_b, block_c, block_step, block_logd):
    block_size = block_input.shape[0]
    head_count = block_step.shape[0]
    per_group = HEADS // GROUPS
    group_count = head_count // per_group
    cumulative = jnp.cumsum(block_logd, axis=1)
    block_total = cumulative[:, -1]
    inputs_head = block_input.reshape(block_size, group_count, per_group, HEAD_DIM)
    b_groups = block_b.reshape(block_size, group_count, STATE)
    c_groups = block_c.reshape(block_size, group_count, STATE)
    scores = jnp.einsum("tgn,sgn->gts", c_groups, b_groups, preferred_element_type=jnp.float32)
    row_index = lax.broadcasted_iota(jnp.int32, (block_size, block_size), 0)
    col_index = lax.broadcasted_iota(jnp.int32, (block_size, block_size), 1)
    causal = row_index >= col_index
    log_gap = cumulative[:, :, None] - cumulative[:, None, :]
    decay_rate = (
        jnp.where(causal, jnp.exp(jnp.where(causal, log_gap, 0.0)), 0.0) * block_step[:, None, :]
    )
    mixing = (
        scores[:, None, :, :] * decay_rate.reshape(group_count, per_group, block_size, block_size)
    ).astype(jnp.bfloat16)
    local_out = jnp.einsum(
        "gkts,sgkp->gktp", mixing, inputs_head, preferred_element_type=jnp.float32
    )
    weighting = jnp.exp(block_total[:, None] - cumulative) * block_step
    weighted = (weighting.T.reshape(block_size, group_count, per_group, 1) * inputs_head).astype(
        jnp.bfloat16
    )
    block_state = jnp.einsum(
        "sgkp,sgn->gkpn", weighted, b_groups, preferred_element_type=jnp.float32
    )
    return (cumulative, block_total.reshape(group_count, per_group), local_out, block_state)


def finish(local_out, cumulative, c_proj, entering, ssm_input, skip_gain):
    request_count, group_count, per_group, block_size = local_out.shape[:4]
    c_groups = c_proj.reshape(request_count, block_size, group_count, STATE)
    flat = entering.reshape(request_count, group_count, per_group * HEAD_DIM, STATE)
    high = flat.astype(jnp.bfloat16)
    low = (flat - high.astype(jnp.float32)).astype(jnp.bfloat16)
    numbers = (((3,), (3,)), ((0, 2), (0, 1)))
    carried = lax.dot_general(
        c_groups, high, numbers, preferred_element_type=jnp.float32
    ) + lax.dot_general(c_groups, low, numbers, preferred_element_type=jnp.float32)
    carried = carried.reshape(request_count, group_count, block_size, per_group, HEAD_DIM)
    growth = jnp.exp(cumulative).reshape(request_count, group_count, per_group, block_size)
    carried = carried * growth.transpose(0, 1, 3, 2)[..., None]
    inputs_head = ssm_input.reshape(
        request_count, block_size, group_count, per_group, HEAD_DIM
    ).astype(jnp.float32)
    skipped = skip_gain.reshape(group_count, per_group, 1) * inputs_head
    total = carried.transpose(0, 2, 1, 3, 4) + local_out.transpose(0, 3, 1, 2, 4) + skipped
    return total.reshape(request_count, block_size, -1).astype(jnp.bfloat16)


def range_decay(all_totals, low, high):
    place = lax.broadcasted_iota(jnp.int32, all_totals.shape, 0)
    keep = (place >= low) & (place <= high)
    return jnp.exp(jnp.sum(jnp.where(keep, all_totals, 0.0), axis=0))


def scale(factor, state):
    return factor[..., None, None] * state


def send(value, total, pairs):
    state, total = lax.ppermute((value.astype(jnp.bfloat16), total), "ctx", pairs)
    return state.astype(jnp.float32), total


def gather_ctx(value):
    count = lax.axis_size("ctx")
    if count & (count - 1):
        return lax.all_gather(value, "ctx", axis=0, tiled=True)
    place = lax.axis_index("ctx")
    reach = 1
    while reach < count:
        got = lax.ppermute(value, "ctx", [(i, i ^ reach) for i in range(count)])
        upper = (place & reach) != 0
        value = jnp.where(
            upper, jnp.concatenate([got, value], axis=0), jnp.concatenate([value, got], axis=0)
        )
        reach *= 2
    return value


def reduce_scatter_ctx(value):
    count = lax.axis_size("ctx")
    if count & (count - 1):
        return lax.psum_scatter(value, "ctx", scatter_dimension=0, tiled=True)
    place = lax.axis_index("ctx")
    reach = 1
    while reach < count:
        pairs = value.reshape((value.shape[0] // 2, 2) + value.shape[1:])
        upper = (place & reach) != 0
        keep = jnp.where(upper, pairs[:, 1], pairs[:, 0])
        give = jnp.where(upper, pairs[:, 0], pairs[:, 1])
        value = keep + lax.ppermute(give, "ctx", [(i, i ^ reach) for i in range(count)])
        reach *= 2
    return value


def exchange_ctx(value, total):
    count = lax.axis_size("ctx")
    got = lax.all_to_all(value, "ctx", 0, 0, tiled=True)
    got = got.reshape((count, value.shape[0] // count) + value.shape[1:])
    return jnp.sum(got, axis=0) if total else got.reshape(value.shape)


def chain_columns(window, window_total, column, columns):
    chunks = window.shape[0]
    growth = jnp.exp(window_total)
    entering = [jnp.zeros_like(window[k]) for k in range(chunks)]
    for stage in range(columns - 1 + chunks - 1):
        senders = [m for m in range(columns - 1) if 0 <= stage - m < chunks]
        pairs = [(y + 2 * m, y + 2 * (m + 1)) for y in range(2) for m in senders]
        outgoing = jnp.zeros_like(window[0])
        for k in range(chunks):
            leaving = scale(growth[k], entering[k]) + window[k]
            outgoing = jnp.where(stage - column == k, leaving, outgoing)
        got = lax.ppermute(outgoing.astype(jnp.bfloat16), "ctx", pairs).astype(jnp.float32)
        for k in range(chunks):
            entering[k] = jnp.where(stage - column + 1 == k, got, entering[k])
    return jnp.stack(entering)


def prefix_states(states, totals):
    count = lax.axis_size("ctx")
    columns = count // 2
    place = lax.axis_index("ctx")
    row_zero = place % 2 == 0
    column = place // 2
    half = states.shape[-2] // 2
    first = states[..., :half, :]
    second = states[..., half:, :]
    mine = jnp.where(row_zero, first, second)
    other = jnp.where(row_zero, second, first)
    across = [(2 * m, 2 * m + 1) for m in range(columns)] + [
        (2 * m + 1, 2 * m) for m in range(columns)
    ]
    received, partner_total = send(other, totals, across)
    even_state = jnp.where(row_zero, mine, received)
    odd_state = jnp.where(row_zero, received, mine)
    even_total = jnp.where(row_zero, totals, partner_total)
    odd_total = jnp.where(row_zero, partner_total, totals)
    window = scale(jnp.exp(odd_total), even_state) + odd_state
    window_total = even_total + odd_total
    if columns <= 4:
        before = chain_columns(window, window_total, column, columns)
    else:
        before = jnp.zeros_like(window)
        before_total = jnp.zeros_like(totals)
        step = 1
        while step < columns:
            pairs = [
                (y + 2 * m, y + 2 * (m + step)) for y in range(2) for m in range(columns - step)
            ]
            got, got_total = send(window, window_total, pairs)
            new_before = scale(jnp.exp(before_total), got) + before
            if 2 * step < columns:
                window = scale(jnp.exp(window_total), got) + window
                window_total = got_total + window_total
            before = new_before
            before_total = got_total + before_total
            step *= 2
    odd_entering = scale(jnp.exp(even_total), before) + even_state
    outgoing = jnp.where(row_zero, odd_entering, before)
    partner, _ = send(outgoing, totals, across)
    own_half = jnp.where(row_zero, before, odd_entering)
    first_half = jnp.where(row_zero, own_half, partner)
    second_half = jnp.where(row_zero, partner, own_half)
    return jnp.concatenate([first_half, second_half], axis=-2)


def shards(
    ssm_input,
    b_proj,
    c_proj,
    step_size,
    log_decay,
    skip_gain,
    request_of_slot,
    new_input,
    new_b,
    new_c,
    new_step,
    new_log_decay,
    out_weight,
):
    request_count = ssm_input.shape[0]
    count = lax.axis_size("ctx")
    place = lax.axis_index("ctx")
    terms = []
    for request in range(request_count):
        terms.append(
            block_terms(
                ssm_input[request],
                b_proj[request],
                c_proj[request],
                step_size[request],
                log_decay[request],
            )
        )
    totals = jnp.stack([term[1] for term in terms])
    states = jnp.stack([term[3] for term in terms])
    group_count, per_group = totals.shape[1], totals.shape[2]

    slots, steps = new_input.shape[0], new_input.shape[1]
    pieces = [totals, request_of_slot.astype(jnp.float32), new_c.astype(jnp.float32)]
    packed = jnp.concatenate([piece.reshape(-1) for piece in pieces])
    gathered = gather_ctx(packed[None])
    unpacked = []
    offset = 0
    for piece in pieces:
        size = piece.size
        unpacked.append(
            gathered[:, offset : offset + size].reshape((count,) + piece.shape)
        )
        offset += size
    all_totals, all_request, all_c = unpacked
    all_slots = count * slots
    all_request = all_request.reshape(all_slots)
    all_c = all_c.reshape(all_slots, steps, group_count, STATE)

    later = range_decay(all_totals, place + 1, count - 1)
    weighted_states = scale(later, states)
    high = weighted_states.astype(jnp.bfloat16)
    low = (weighted_states - high.astype(jnp.float32)).astype(jnp.bfloat16)
    c_rows = all_c.astype(jnp.bfloat16)
    projected = jnp.einsum(
        "rgkpn,jugn->rjugkp", high, c_rows, preferred_element_type=jnp.float32
    ) + jnp.einsum("rgkpn,jugn->rjugkp", low, c_rows, preferred_element_type=jnp.float32)
    contribution = projected[0]
    for request in range(1, request_count):
        pick = (all_request == request)[:, None, None, None, None]
        contribution = jnp.where(pick, projected[request], contribution)
    from_prompt = exchange_ctx(contribution, True)

    row_input = new_input.reshape(slots, steps, group_count, per_group, HEAD_DIM).astype(
        jnp.float32
    )
    row_b = new_b.reshape(slots, steps, group_count, STATE).astype(jnp.float32)
    row_c = new_c.reshape(slots, steps, group_count, STATE).astype(jnp.float32)
    row_step = new_step.reshape(slots, steps, group_count, per_group)
    row_logd = new_log_decay.reshape(slots, steps, group_count, per_group)
    cum_logd = jnp.cumsum(row_logd, axis=1)
    inner = jnp.einsum("jvgn,jugn->jvug", row_b, row_c, precision=HIGH)
    order_v = lax.broadcasted_iota(jnp.int32, (steps, steps), 0)
    order_u = lax.broadcasted_iota(jnp.int32, (steps, steps), 1)
    causal = (order_v <= order_u)[None, :, :, None, None]
    gap = cum_logd[:, None, :, :, :] - cum_logd[:, :, None, :, :]
    coefficient = jnp.where(
        causal, jnp.exp(jnp.where(causal, gap, 0.0)) * inner[..., None], 0.0
    ) * row_step[:, :, None, :, :]
    local_part = jnp.sum(coefficient[..., None] * row_input[:, :, None], axis=1)
    value = (
        jnp.exp(cum_logd)[..., None] * from_prompt
        + local_part
        + skip_gain.reshape(group_count, per_group, 1) * row_input
    )
    new_output = value.reshape(slots, steps, -1).astype(jnp.bfloat16)
    partial_value = jnp.einsum(
        "jup,pd->jud",
        exchange_ctx(jnp.concatenate([new_output] * count, axis=0), False),
        out_weight,
        preferred_element_type=jnp.float32,
    )
    if lax.axis_size("heads") == 2:
        other_half = lax.ppermute(partial_value, "heads", [(0, 1), (1, 0)])
        decoded = (partial_value + other_half).astype(jnp.bfloat16)
    else:
        decoded = lax.psum(partial_value, "heads").astype(jnp.bfloat16)

    entering = prefix_states(states, totals)
    prefill_out = finish(
        jnp.stack([term[2] for term in terms]),
        jnp.stack([term[0] for term in terms]),
        c_proj,
        entering,
        ssm_input,
        skip_gain,
    )
    return (prefill_out, decoded)


def solution(mesh):
    in_specs = (
        P("groups", "ctx", "heads"),
        P("groups", "ctx", "heads"),
        P("groups", "ctx", "heads"),
        P("groups", "heads", "ctx"),
        P("groups", "heads", "ctx"),
        P("heads"),
        P(("groups", "ctx")),
        P(("groups", "ctx"), None, "heads"),
        P(("groups", "ctx"), None, "heads"),
        P(("groups", "ctx"), None, "heads"),
        P(("groups", "ctx"), None, "heads"),
        P(("groups", "ctx"), None, "heads"),
        P("heads", "ctx"),
    )
    out_specs = (P("groups", "ctx", "heads"), P("groups", None, "ctx"))
    return jax.shard_map(shards, mesh=mesh, in_specs=in_specs, out_specs=out_specs, check_vma=False)
```

```python
import jax
import jax.numpy as jnp
from jax import lax
from jax.sharding import PartitionSpec as P

HEADS = 128
HEAD_DIM = 64
STATE = 128
GROUPS = 4

HIGH = lax.Precision.HIGHEST


def block_terms(block_input, block_b, block_c, block_step, block_logd):
    block_size = block_input.shape[0]
    head_count = block_step.shape[0]
    per_group = HEADS // GROUPS
    group_count = head_count // per_group
    cumulative = jnp.cumsum(block_logd, axis=1)
    block_total = cumulative[:, -1]
    inputs_head = block_input.reshape(block_size, group_count, per_group, HEAD_DIM)
    b_groups = block_b.reshape(block_size, group_count, STATE)
    c_groups = block_c.reshape(block_size, group_count, STATE)
    scores = jnp.einsum("tgn,sgn->gts", c_groups, b_groups, preferred_element_type=jnp.float32)
    row_index = lax.broadcasted_iota(jnp.int32, (block_size, block_size), 0)
    col_index = lax.broadcasted_iota(jnp.int32, (block_size, block_size), 1)
    causal = row_index >= col_index
    log_gap = cumulative[:, :, None] - cumulative[:, None, :]
    decay_rate = (
        jnp.where(causal, jnp.exp(jnp.where(causal, log_gap, 0.0)), 0.0) * block_step[:, None, :]
    )
    mixing = (
        scores[:, None, :, :] * decay_rate.reshape(group_count, per_group, block_size, block_size)
    ).astype(jnp.bfloat16)
    local_out = jnp.einsum(
        "gkts,sgkp->gktp", mixing, inputs_head, preferred_element_type=jnp.float32
    )
    weighting = jnp.exp(block_total[:, None] - cumulative) * block_step
    weighted = (weighting.T.reshape(block_size, group_count, per_group, 1) * inputs_head).astype(
        jnp.bfloat16
    )
    block_state = jnp.einsum(
        "sgkp,sgn->gkpn", weighted, b_groups, preferred_element_type=jnp.float32
    )
    return (cumulative, block_total.reshape(group_count, per_group), local_out, block_state)


def finish(local_out, cumulative, c_proj, entering, ssm_input, skip_gain):
    request_count, group_count, per_group, block_size = local_out.shape[:4]
    c_groups = c_proj.reshape(request_count, block_size, group_count, STATE)
    flat = entering.reshape(request_count, group_count, per_group * HEAD_DIM, STATE)
    high = flat.astype(jnp.bfloat16)
    low = (flat - high.astype(jnp.float32)).astype(jnp.bfloat16)
    numbers = (((3,), (3,)), ((0, 2), (0, 1)))
    carried = lax.dot_general(
        c_groups, high, numbers, preferred_element_type=jnp.float32
    ) + lax.dot_general(c_groups, low, numbers, preferred_element_type=jnp.float32)
    carried = carried.reshape(request_count, group_count, block_size, per_group, HEAD_DIM)
    growth = jnp.exp(cumulative).reshape(request_count, group_count, per_group, block_size)
    carried = carried * growth.transpose(0, 1, 3, 2)[..., None]
    inputs_head = ssm_input.reshape(
        request_count, block_size, group_count, per_group, HEAD_DIM
    ).astype(jnp.float32)
    skipped = skip_gain.reshape(group_count, per_group, 1) * inputs_head
    total = carried.transpose(0, 2, 1, 3, 4) + local_out.transpose(0, 3, 1, 2, 4) + skipped
    return total.reshape(request_count, block_size, -1).astype(jnp.bfloat16)


def range_decay(all_totals, low, high):
    place = lax.broadcasted_iota(jnp.int32, all_totals.shape, 0)
    keep = (place >= low) & (place <= high)
    return jnp.exp(jnp.sum(jnp.where(keep, all_totals, 0.0), axis=0))


def scale(factor, state):
    return factor[..., None, None] * state


def send(value, total, pairs):
    state, total = lax.ppermute((value.astype(jnp.bfloat16), total), "ctx", pairs)
    return state.astype(jnp.float32), total


def gather_ctx(value):
    count = lax.axis_size("ctx")
    if count & (count - 1):
        return lax.all_gather(value, "ctx", axis=0, tiled=True)
    place = lax.axis_index("ctx")
    reach = 1
    while reach < count:
        got = lax.ppermute(value, "ctx", [(i, i ^ reach) for i in range(count)])
        upper = (place & reach) != 0
        value = jnp.where(
            upper, jnp.concatenate([got, value], axis=0), jnp.concatenate([value, got], axis=0)
        )
        reach *= 2
    return value


def reduce_scatter_ctx(value):
    count = lax.axis_size("ctx")
    if count & (count - 1):
        return lax.psum_scatter(value, "ctx", scatter_dimension=0, tiled=True)
    place = lax.axis_index("ctx")
    reach = 1
    while reach < count:
        pairs = value.reshape((value.shape[0] // 2, 2) + value.shape[1:])
        upper = (place & reach) != 0
        keep = jnp.where(upper, pairs[:, 1], pairs[:, 0])
        give = jnp.where(upper, pairs[:, 0], pairs[:, 1])
        value = keep + lax.ppermute(give, "ctx", [(i, i ^ reach) for i in range(count)])
        reach *= 2
    return value


def exchange_ctx(value, total):
    count = lax.axis_size("ctx")
    got = lax.all_to_all(value, "ctx", 0, 0, tiled=True)
    got = got.reshape((count, value.shape[0] // count) + value.shape[1:])
    return jnp.sum(got, axis=0) if total else got.reshape(value.shape)


def chain_columns(window, window_total, column, columns):
    chunks = window.shape[0]
    growth = jnp.exp(window_total)
    entering = [jnp.zeros_like(window[k]) for k in range(chunks)]
    for stage in range(columns - 1 + chunks - 1):
        senders = [m for m in range(columns - 1) if 0 <= stage - m < chunks]
        pairs = [(y + 2 * m, y + 2 * (m + 1)) for y in range(2) for m in senders]
        outgoing = jnp.zeros_like(window[0])
        for k in range(chunks):
            leaving = scale(growth[k], entering[k]) + window[k]
            outgoing = jnp.where(stage - column == k, leaving, outgoing)
        got = lax.ppermute(outgoing.astype(jnp.bfloat16), "ctx", pairs).astype(jnp.float32)
        for k in range(chunks):
            entering[k] = jnp.where(stage - column + 1 == k, got, entering[k])
    return jnp.stack(entering)


def prefix_states(states, totals):
    count = lax.axis_size("ctx")
    columns = count // 2
    place = lax.axis_index("ctx")
    row_zero = place % 2 == 0
    column = place // 2
    half = states.shape[-2] // 2
    first = states[..., :half, :]
    second = states[..., half:, :]
    mine = jnp.where(row_zero, first, second)
    other = jnp.where(row_zero, second, first)
    across = [(2 * m, 2 * m + 1) for m in range(columns)] + [
        (2 * m + 1, 2 * m) for m in range(columns)
    ]
    received, partner_total = send(other, totals, across)
    even_state = jnp.where(row_zero, mine, received)
    odd_state = jnp.where(row_zero, received, mine)
    even_total = jnp.where(row_zero, totals, partner_total)
    odd_total = jnp.where(row_zero, partner_total, totals)
    window = scale(jnp.exp(odd_total), even_state) + odd_state
    window_total = even_total + odd_total
    if columns <= 4:
        before = chain_columns(window, window_total, column, columns)
    else:
        before = jnp.zeros_like(window)
        before_total = jnp.zeros_like(totals)
        step = 1
        while step < columns:
            pairs = [
                (y + 2 * m, y + 2 * (m + step)) for y in range(2) for m in range(columns - step)
            ]
            got, got_total = send(window, window_total, pairs)
            new_before = scale(jnp.exp(before_total), got) + before
            if 2 * step < columns:
                window = scale(jnp.exp(window_total), got) + window
                window_total = got_total + window_total
            before = new_before
            before_total = got_total + before_total
            step *= 2
    odd_entering = scale(jnp.exp(even_total), before) + even_state
    outgoing = jnp.where(row_zero, odd_entering, before)
    partner, _ = send(outgoing, totals, across)
    own_half = jnp.where(row_zero, before, odd_entering)
    first_half = jnp.where(row_zero, own_half, partner)
    second_half = jnp.where(row_zero, partner, own_half)
    return jnp.concatenate([first_half, second_half], axis=-2)


def shards(
    ssm_input,
    b_proj,
    c_proj,
    step_size,
    log_decay,
    skip_gain,
    request_of_slot,
    new_input,
    new_b,
    new_c,
    new_step,
    new_log_decay,
    out_weight,
):
    request_count = ssm_input.shape[0]
    count = lax.axis_size("ctx")
    place = lax.axis_index("ctx")
    terms = []
    for request in range(request_count):
        terms.append(
            block_terms(
                ssm_input[request],
                b_proj[request],
                c_proj[request],
                step_size[request],
                log_decay[request],
            )
        )
    totals = jnp.stack([term[1] for term in terms])
    states = jnp.stack([term[3] for term in terms])
    group_count, per_group = totals.shape[1], totals.shape[2]

    slots, steps = new_input.shape[0], new_input.shape[1]
    pieces = [totals, request_of_slot.astype(jnp.float32), new_c.astype(jnp.float32)]
    packed = jnp.concatenate([piece.reshape(-1) for piece in pieces])
    gathered = exchange_ctx(jnp.concatenate([packed[None]] * count, axis=0), False)
    unpacked = []
    offset = 0
    for piece in pieces:
        size = piece.size
        unpacked.append(
            gathered[:, offset : offset + size].reshape((count,) + piece.shape)
        )
        offset += size
    all_totals, all_request, all_c = unpacked
    all_slots = count * slots
    all_request = all_request.reshape(all_slots)
    all_c = all_c.reshape(all_slots, steps, group_count, STATE)

    later = range_decay(all_totals, place + 1, count - 1)
    weighted_states = scale(later, states)
    high = weighted_states.astype(jnp.bfloat16)
    low = (weighted_states - high.astype(jnp.float32)).astype(jnp.bfloat16)
    c_rows = all_c.astype(jnp.bfloat16)
    projected = jnp.einsum(
        "rgkpn,jugn->rjugkp", high, c_rows, preferred_element_type=jnp.float32
    ) + jnp.einsum("rgkpn,jugn->rjugkp", low, c_rows, preferred_element_type=jnp.float32)
    contribution = projected[0]
    for request in range(1, request_count):
        pick = (all_request == request)[:, None, None, None, None]
        contribution = jnp.where(pick, projected[request], contribution)
    from_prompt = exchange_ctx(contribution, True)

    row_input = new_input.reshape(slots, steps, group_count, per_group, HEAD_DIM).astype(
        jnp.float32
    )
    row_b = new_b.reshape(slots, steps, group_count, STATE).astype(jnp.float32)
    row_c = new_c.reshape(slots, steps, group_count, STATE).astype(jnp.float32)
    row_step = new_step.reshape(slots, steps, group_count, per_group)
    row_logd = new_log_decay.reshape(slots, steps, group_count, per_group)
    cum_logd = jnp.cumsum(row_logd, axis=1)
    inner = jnp.einsum("jvgn,jugn->jvug", row_b, row_c, precision=HIGH)
    order_v = lax.broadcasted_iota(jnp.int32, (steps, steps), 0)
    order_u = lax.broadcasted_iota(jnp.int32, (steps, steps), 1)
    causal = (order_v <= order_u)[None, :, :, None, None]
    gap = cum_logd[:, None, :, :, :] - cum_logd[:, :, None, :, :]
    coefficient = jnp.where(
        causal, jnp.exp(jnp.where(causal, gap, 0.0)) * inner[..., None], 0.0
    ) * row_step[:, :, None, :, :]
    local_part = jnp.sum(coefficient[..., None] * row_input[:, :, None], axis=1)
    value = (
        jnp.exp(cum_logd)[..., None] * from_prompt
        + local_part
        + skip_gain.reshape(group_count, per_group, 1) * row_input
    )
    new_output = value.reshape(slots, steps, -1).astype(jnp.bfloat16)
    partial_value = jnp.einsum(
        "jup,pd->jud",
        exchange_ctx(jnp.concatenate([new_output] * count, axis=0), False),
        out_weight,
        preferred_element_type=jnp.float32,
    )
    if lax.axis_size("heads") == 2:
        other_half = lax.ppermute(partial_value, "heads", [(0, 1), (1, 0)])
        decoded = (partial_value + other_half).astype(jnp.bfloat16)
    else:
        decoded = lax.psum(partial_value, "heads").astype(jnp.bfloat16)

    entering = prefix_states(states, totals)
    prefill_out = finish(
        jnp.stack([term[2] for term in terms]),
        jnp.stack([term[0] for term in terms]),
        c_proj,
        entering,
        ssm_input,
        skip_gain,
    )
    return (prefill_out, decoded)


def solution(mesh):
    in_specs = (
        P("groups", "ctx", "heads"),
        P("groups", "ctx", "heads"),
        P("groups", "ctx", "heads"),
        P("groups", "heads", "ctx"),
        P("groups", "heads", "ctx"),
        P("heads"),
        P(("groups", "ctx")),
        P(("groups", "ctx"), None, "heads"),
        P(("groups", "ctx"), None, "heads"),
        P(("groups", "ctx"), None, "heads"),
        P(("groups", "ctx"), None, "heads"),
        P(("groups", "ctx"), None, "heads"),
        P("heads", "ctx"),
    )
    out_specs = (P("groups", "ctx", "heads"), P("groups", None, "ctx"))
    return jax.shard_map(shards, mesh=mesh, in_specs=in_specs, out_specs=out_specs, check_vma=False)
```

```python
import jax
import jax.numpy as jnp
from jax import lax
from jax.sharding import PartitionSpec as P

HEADS = 128
HEAD_DIM = 64
STATE = 128
GROUPS = 4

HIGH = lax.Precision.HIGHEST


def block_terms(block_input, block_b, block_c, block_step, block_logd):
    block_size = block_input.shape[0]
    head_count = block_step.shape[0]
    per_group = HEADS // GROUPS
    group_count = head_count // per_group
    cumulative = jnp.cumsum(block_logd, axis=1)
    block_total = cumulative[:, -1]
    inputs_head = block_input.reshape(block_size, group_count, per_group, HEAD_DIM)
    b_groups = block_b.reshape(block_size, group_count, STATE)
    c_groups = block_c.reshape(block_size, group_count, STATE)
    scores = jnp.einsum("tgn,sgn->gts", c_groups, b_groups, preferred_element_type=jnp.float32)
    row_index = lax.broadcasted_iota(jnp.int32, (block_size, block_size), 0)
    col_index = lax.broadcasted_iota(jnp.int32, (block_size, block_size), 1)
    causal = row_index >= col_index
    log_gap = cumulative[:, :, None] - cumulative[:, None, :]
    decay_rate = (
        jnp.where(causal, jnp.exp(jnp.where(causal, log_gap, 0.0)), 0.0) * block_step[:, None, :]
    )
    mixing = (
        scores[:, None, :, :] * decay_rate.reshape(group_count, per_group, block_size, block_size)
    ).astype(jnp.bfloat16)
    local_out = jnp.einsum(
        "gkts,sgkp->gktp", mixing, inputs_head, preferred_element_type=jnp.float32
    )
    weighting = jnp.exp(block_total[:, None] - cumulative) * block_step
    weighted = (weighting.T.reshape(block_size, group_count, per_group, 1) * inputs_head).astype(
        jnp.bfloat16
    )
    block_state = jnp.einsum(
        "sgkp,sgn->gkpn", weighted, b_groups, preferred_element_type=jnp.float32
    )
    return (cumulative, block_total.reshape(group_count, per_group), local_out, block_state)


def finish(local_out, cumulative, c_proj, entering, ssm_input, skip_gain):
    request_count, group_count, per_group, block_size = local_out.shape[:4]
    c_groups = c_proj.reshape(request_count, block_size, group_count, STATE)
    flat = entering.reshape(request_count, group_count, per_group * HEAD_DIM, STATE)
    high = flat.astype(jnp.bfloat16)
    low = (flat - high.astype(jnp.float32)).astype(jnp.bfloat16)
    numbers = (((3,), (3,)), ((0, 2), (0, 1)))
    carried = lax.dot_general(
        c_groups, high, numbers, preferred_element_type=jnp.float32
    ) + lax.dot_general(c_groups, low, numbers, preferred_element_type=jnp.float32)
    carried = carried.reshape(request_count, group_count, block_size, per_group, HEAD_DIM)
    growth = jnp.exp(cumulative).reshape(request_count, group_count, per_group, block_size)
    carried = carried * growth.transpose(0, 1, 3, 2)[..., None]
    total = carried.transpose(0, 2, 1, 3, 4) + local_out.transpose(0, 3, 1, 2, 4)
    return total.reshape(request_count, block_size, -1).astype(jnp.bfloat16)


def range_decay(all_totals, low, high):
    place = lax.broadcasted_iota(jnp.int32, all_totals.shape, 0)
    keep = (place >= low) & (place <= high)
    return jnp.exp(jnp.sum(jnp.where(keep, all_totals, 0.0), axis=0))


def scale(factor, state):
    return factor[..., None, None] * state


def send(value, total, pairs):
    state, total = lax.ppermute((value.astype(jnp.bfloat16), total), "ctx", pairs)
    return state.astype(jnp.float32), total


def gather_ctx(value):
    count = lax.axis_size("ctx")
    if count & (count - 1):
        return lax.all_gather(value, "ctx", axis=0, tiled=True)
    place = lax.axis_index("ctx")
    reach = 1
    while reach < count:
        got = lax.ppermute(value, "ctx", [(i, i ^ reach) for i in range(count)])
        upper = (place & reach) != 0
        value = jnp.where(
            upper, jnp.concatenate([got, value], axis=0), jnp.concatenate([value, got], axis=0)
        )
        reach *= 2
    return value


def reduce_scatter_ctx(value):
    count = lax.axis_size("ctx")
    if count & (count - 1):
        return lax.psum_scatter(value, "ctx", scatter_dimension=0, tiled=True)
    place = lax.axis_index("ctx")
    reach = 1
    while reach < count:
        pairs = value.reshape((value.shape[0] // 2, 2) + value.shape[1:])
        upper = (place & reach) != 0
        keep = jnp.where(upper, pairs[:, 1], pairs[:, 0])
        give = jnp.where(upper, pairs[:, 0], pairs[:, 1])
        value = keep + lax.ppermute(give, "ctx", [(i, i ^ reach) for i in range(count)])
        reach *= 2
    return value


def exchange_ctx(value, total):
    count = lax.axis_size("ctx")
    got = lax.all_to_all(value, "ctx", 0, 0, tiled=True)
    got = got.reshape((count, value.shape[0] // count) + value.shape[1:])
    return jnp.sum(got, axis=0) if total else got.reshape(value.shape)


def chain_columns(window, window_total, column, columns):
    chunks = window.shape[0]
    growth = jnp.exp(window_total)
    entering = [jnp.zeros_like(window[k]) for k in range(chunks)]
    for stage in range(columns - 1 + chunks - 1):
        senders = [m for m in range(columns - 1) if 0 <= stage - m < chunks]
        pairs = [(y + 2 * m, y + 2 * (m + 1)) for y in range(2) for m in senders]
        outgoing = jnp.zeros_like(window[0])
        for k in range(chunks):
            leaving = scale(growth[k], entering[k]) + window[k]
            outgoing = jnp.where(stage - column == k, leaving, outgoing)
        got = lax.ppermute(outgoing.astype(jnp.bfloat16), "ctx", pairs).astype(jnp.float32)
        for k in range(chunks):
            entering[k] = jnp.where(stage - column + 1 == k, got, entering[k])
    return jnp.stack(entering)


def prefix_states(states, totals):
    count = lax.axis_size("ctx")
    columns = count // 2
    place = lax.axis_index("ctx")
    row_zero = place % 2 == 0
    column = place // 2
    half = states.shape[-2] // 2
    first = states[..., :half, :]
    second = states[..., half:, :]
    mine = jnp.where(row_zero, first, second)
    other = jnp.where(row_zero, second, first)
    across = [(2 * m, 2 * m + 1) for m in range(columns)] + [
        (2 * m + 1, 2 * m) for m in range(columns)
    ]
    received, partner_total = send(other, totals, across)
    even_state = jnp.where(row_zero, mine, received)
    odd_state = jnp.where(row_zero, received, mine)
    even_total = jnp.where(row_zero, totals, partner_total)
    odd_total = jnp.where(row_zero, partner_total, totals)
    window = scale(jnp.exp(odd_total), even_state) + odd_state
    window_total = even_total + odd_total
    if columns <= 4:
        before = chain_columns(window, window_total, column, columns)
    else:
        before = jnp.zeros_like(window)
        before_total = jnp.zeros_like(totals)
        step = 1
        while step < columns:
            pairs = [
                (y + 2 * m, y + 2 * (m + step)) for y in range(2) for m in range(columns - step)
            ]
            got, got_total = send(window, window_total, pairs)
            new_before = scale(jnp.exp(before_total), got) + before
            if 2 * step < columns:
                window = scale(jnp.exp(window_total), got) + window
                window_total = got_total + window_total
            before = new_before
            before_total = got_total + before_total
            step *= 2
    odd_entering = scale(jnp.exp(even_total), before) + even_state
    outgoing = jnp.where(row_zero, odd_entering, before)
    partner, _ = send(outgoing, totals, across)
    own_half = jnp.where(row_zero, before, odd_entering)
    first_half = jnp.where(row_zero, own_half, partner)
    second_half = jnp.where(row_zero, partner, own_half)
    return jnp.concatenate([first_half, second_half], axis=-2)


def shards(
    ssm_input,
    b_proj,
    c_proj,
    step_size,
    log_decay,
    skip_gain,
    request_of_slot,
    new_input,
    new_b,
    new_c,
    new_step,
    new_log_decay,
    out_weight,
):
    request_count = ssm_input.shape[0]
    count = lax.axis_size("ctx")
    place = lax.axis_index("ctx")
    terms = []
    for request in range(request_count):
        terms.append(
            block_terms(
                ssm_input[request],
                b_proj[request],
                c_proj[request],
                step_size[request],
                log_decay[request],
            )
        )
    totals = jnp.stack([term[1] for term in terms])
    states = jnp.stack([term[3] for term in terms])
    group_count, per_group = totals.shape[1], totals.shape[2]

    slots, steps = new_input.shape[0], new_input.shape[1]
    pieces = [totals, request_of_slot.astype(jnp.float32), new_c.astype(jnp.float32)]
    packed = jnp.concatenate([piece.reshape(-1) for piece in pieces])
    gathered = gather_ctx(packed[None])
    unpacked = []
    offset = 0
    for piece in pieces:
        size = piece.size
        unpacked.append(
            gathered[:, offset : offset + size].reshape((count,) + piece.shape)
        )
        offset += size
    all_totals, all_request, all_c = unpacked
    all_slots = count * slots
    all_request = all_request.reshape(all_slots)
    all_c = all_c.reshape(all_slots, steps, group_count, STATE)

    later = range_decay(all_totals, place + 1, count - 1)
    weighted_states = scale(later, states)
    high = weighted_states.astype(jnp.bfloat16)
    low = (weighted_states - high.astype(jnp.float32)).astype(jnp.bfloat16)
    c_rows = all_c.astype(jnp.bfloat16)
    projected = jnp.einsum(
        "rgkpn,jugn->rjugkp", high, c_rows, preferred_element_type=jnp.float32
    ) + jnp.einsum("rgkpn,jugn->rjugkp", low, c_rows, preferred_element_type=jnp.float32)
    contribution = projected[0]
    for request in range(1, request_count):
        pick = (all_request == request)[:, None, None, None, None]
        contribution = jnp.where(pick, projected[request], contribution)
    from_prompt = exchange_ctx(contribution, True)

    row_input = new_input.reshape(slots, steps, group_count, per_group, HEAD_DIM).astype(
        jnp.float32
    )
    row_b = new_b.reshape(slots, steps, group_count, STATE).astype(jnp.float32)
    row_c = new_c.reshape(slots, steps, group_count, STATE).astype(jnp.float32)
    row_step = new_step.reshape(slots, steps, group_count, per_group)
    row_logd = new_log_decay.reshape(slots, steps, group_count, per_group)
    cum_logd = jnp.cumsum(row_logd, axis=1)
    inner = jnp.einsum("jvgn,jugn->jvug", row_b, row_c, precision=HIGH)
    order_v = lax.broadcasted_iota(jnp.int32, (steps, steps), 0)
    order_u = lax.broadcasted_iota(jnp.int32, (steps, steps), 1)
    causal = (order_v <= order_u)[None, :, :, None, None]
    gap = cum_logd[:, None, :, :, :] - cum_logd[:, :, None, :, :]
    coefficient = jnp.where(
        causal, jnp.exp(jnp.where(causal, gap, 0.0)) * inner[..., None], 0.0
    ) * row_step[:, :, None, :, :]
    local_part = jnp.sum(coefficient[..., None] * row_input[:, :, None], axis=1)
    value = (
        jnp.exp(cum_logd)[..., None] * from_prompt
        + local_part
        + skip_gain.reshape(group_count, per_group, 1) * row_input
    )
    new_output = value.reshape(slots, steps, -1).astype(jnp.bfloat16)
    partial_value = jnp.einsum(
        "jup,pd->jud",
        exchange_ctx(jnp.concatenate([new_output] * count, axis=0), False),
        out_weight,
        preferred_element_type=jnp.float32,
    )
    if lax.axis_size("heads") == 2:
        other_half = lax.ppermute(partial_value, "heads", [(0, 1), (1, 0)])
        decoded = (partial_value + other_half).astype(jnp.bfloat16)
    else:
        decoded = lax.psum(partial_value, "heads").astype(jnp.bfloat16)

    entering = prefix_states(states, totals)
    prefill_out = finish(
        jnp.stack([term[2] for term in terms])
        + skip_gain.reshape(1, group_count, per_group, 1, 1)
        * ssm_input.reshape(request_count, -1, group_count, per_group, HEAD_DIM)
        .transpose(0, 2, 3, 1, 4)
        .astype(jnp.float32),
        jnp.stack([term[0] for term in terms]),
        c_proj,
        entering,
        ssm_input,
        skip_gain,
    )
    return (prefill_out, decoded)


def solution(mesh):
    in_specs = (
        P("groups", "ctx", "heads"),
        P("groups", "ctx", "heads"),
        P("groups", "ctx", "heads"),
        P("groups", "heads", "ctx"),
        P("groups", "heads", "ctx"),
        P("heads"),
        P(("groups", "ctx")),
        P(("groups", "ctx"), None, "heads"),
        P(("groups", "ctx"), None, "heads"),
        P(("groups", "ctx"), None, "heads"),
        P(("groups", "ctx"), None, "heads"),
        P(("groups", "ctx"), None, "heads"),
        P("heads", "ctx"),
    )
    out_specs = (P("groups", "ctx", "heads"), P("groups", None, "ctx"))
    return jax.shard_map(shards, mesh=mesh, in_specs=in_specs, out_specs=out_specs, check_vma=False)
```

```python
import jax
import jax.numpy as jnp
from jax import lax
from jax.sharding import PartitionSpec as P

HEADS = 128
HEAD_DIM = 64
STATE = 128
GROUPS = 4

HIGH = lax.Precision.HIGHEST


def block_terms(block_input, block_b, block_c, block_step, block_logd):
    block_size = block_input.shape[0]
    head_count = block_step.shape[0]
    per_group = HEADS // GROUPS
    group_count = head_count // per_group
    cumulative = jnp.cumsum(block_logd, axis=1)
    block_total = cumulative[:, -1]
    inputs_head = block_input.reshape(block_size, group_count, per_group, HEAD_DIM)
    b_groups = block_b.reshape(block_size, group_count, STATE)
    c_groups = block_c.reshape(block_size, group_count, STATE)
    scores = jnp.einsum("tgn,sgn->gts", c_groups, b_groups, preferred_element_type=jnp.float32)
    row_index = lax.broadcasted_iota(jnp.int32, (block_size, block_size), 0)
    col_index = lax.broadcasted_iota(jnp.int32, (block_size, block_size), 1)
    causal = row_index >= col_index
    log_gap = cumulative[:, :, None] - cumulative[:, None, :]
    decay_rate = (
        jnp.where(causal, jnp.exp(jnp.where(causal, log_gap, 0.0)), 0.0) * block_step[:, None, :]
    )
    mixing = (
        scores[:, None, :, :] * decay_rate.reshape(group_count, per_group, block_size, block_size)
    ).astype(jnp.bfloat16)
    local_out = jnp.einsum(
        "gkts,sgkp->gktp", mixing, inputs_head, preferred_element_type=jnp.float32
    )
    weighting = jnp.exp(block_total[:, None] - cumulative) * block_step
    weighted = (weighting.T.reshape(block_size, group_count, per_group, 1) * inputs_head).astype(
        jnp.bfloat16
    )
    block_state = jnp.einsum(
        "sgkp,sgn->gkpn", weighted, b_groups, preferred_element_type=jnp.float32
    )
    return (cumulative, block_total.reshape(group_count, per_group), local_out, block_state)


def finish(local_out, cumulative, c_proj, entering, ssm_input, skip_gain):
    request_count, group_count, per_group, block_size = local_out.shape[:4]
    c_groups = c_proj.reshape(request_count, block_size, group_count, STATE)
    flat = entering.reshape(request_count, group_count, per_group * HEAD_DIM, STATE)
    high = flat.astype(jnp.bfloat16)
    low = (flat - high.astype(jnp.float32)).astype(jnp.bfloat16)
    numbers = (((3,), (3,)), ((0, 2), (0, 1)))
    carried = lax.dot_general(
        jnp.concatenate([c_groups, c_groups], axis=-1),
        jnp.concatenate([high, low], axis=-1),
        numbers,
        preferred_element_type=jnp.float32,
    )
    carried = carried.reshape(request_count, group_count, block_size, per_group, HEAD_DIM)
    growth = jnp.exp(cumulative).reshape(request_count, group_count, per_group, block_size)
    carried = carried * growth.transpose(0, 1, 3, 2)[..., None]
    inputs_head = ssm_input.reshape(
        request_count, block_size, group_count, per_group, HEAD_DIM
    ).astype(jnp.float32)
    skipped = skip_gain.reshape(group_count, per_group, 1) * inputs_head
    total = carried.transpose(0, 2, 1, 3, 4) + local_out.transpose(0, 3, 1, 2, 4) + skipped
    return total.reshape(request_count, block_size, -1).astype(jnp.bfloat16)


def range_decay(all_totals, low, high):
    place = lax.broadcasted_iota(jnp.int32, all_totals.shape, 0)
    keep = (place >= low) & (place <= high)
    return jnp.exp(jnp.sum(jnp.where(keep, all_totals, 0.0), axis=0))


def scale(factor, state):
    return factor[..., None, None] * state


def send(value, total, pairs):
    state, total = lax.ppermute((value.astype(jnp.bfloat16), total), "ctx", pairs)
    return state.astype(jnp.float32), total


def gather_ctx(value):
    count = lax.axis_size("ctx")
    if count & (count - 1):
        return lax.all_gather(value, "ctx", axis=0, tiled=True)
    place = lax.axis_index("ctx")
    reach = 1
    while reach < count:
        got = lax.ppermute(value, "ctx", [(i, i ^ reach) for i in range(count)])
        upper = (place & reach) != 0
        value = jnp.where(
            upper, jnp.concatenate([got, value], axis=0), jnp.concatenate([value, got], axis=0)
        )
        reach *= 2
    return value


def reduce_scatter_ctx(value):
    count = lax.axis_size("ctx")
    if count & (count - 1):
        return lax.psum_scatter(value, "ctx", scatter_dimension=0, tiled=True)
    place = lax.axis_index("ctx")
    reach = 1
    while reach < count:
        pairs = value.reshape((value.shape[0] // 2, 2) + value.shape[1:])
        upper = (place & reach) != 0
        keep = jnp.where(upper, pairs[:, 1], pairs[:, 0])
        give = jnp.where(upper, pairs[:, 0], pairs[:, 1])
        value = keep + lax.ppermute(give, "ctx", [(i, i ^ reach) for i in range(count)])
        reach *= 2
    return value


def exchange_ctx(value, total):
    count = lax.axis_size("ctx")
    got = lax.all_to_all(value, "ctx", 0, 0, tiled=True)
    got = got.reshape((count, value.shape[0] // count) + value.shape[1:])
    return jnp.sum(got, axis=0) if total else got.reshape(value.shape)


def chain_columns(window, window_total, column, columns):
    chunks = window.shape[0]
    growth = jnp.exp(window_total)
    entering = [jnp.zeros_like(window[k]) for k in range(chunks)]
    for stage in range(columns - 1 + chunks - 1):
        senders = [m for m in range(columns - 1) if 0 <= stage - m < chunks]
        pairs = [(y + 2 * m, y + 2 * (m + 1)) for y in range(2) for m in senders]
        outgoing = jnp.zeros_like(window[0])
        for k in range(chunks):
            leaving = scale(growth[k], entering[k]) + window[k]
            outgoing = jnp.where(stage - column == k, leaving, outgoing)
        got = lax.ppermute(outgoing.astype(jnp.bfloat16), "ctx", pairs).astype(jnp.float32)
        for k in range(chunks):
            entering[k] = jnp.where(stage - column + 1 == k, got, entering[k])
    return jnp.stack(entering)


def prefix_states(states, totals):
    count = lax.axis_size("ctx")
    columns = count // 2
    place = lax.axis_index("ctx")
    row_zero = place % 2 == 0
    column = place // 2
    half = states.shape[-2] // 2
    first = states[..., :half, :]
    second = states[..., half:, :]
    mine = jnp.where(row_zero, first, second)
    other = jnp.where(row_zero, second, first)
    across = [(2 * m, 2 * m + 1) for m in range(columns)] + [
        (2 * m + 1, 2 * m) for m in range(columns)
    ]
    received, partner_total = send(other, totals, across)
    even_state = jnp.where(row_zero, mine, received)
    odd_state = jnp.where(row_zero, received, mine)
    even_total = jnp.where(row_zero, totals, partner_total)
    odd_total = jnp.where(row_zero, partner_total, totals)
    window = scale(jnp.exp(odd_total), even_state) + odd_state
    window_total = even_total + odd_total
    if columns <= 4:
        before = chain_columns(window, window_total, column, columns)
    else:
        before = jnp.zeros_like(window)
        before_total = jnp.zeros_like(totals)
        step = 1
        while step < columns:
            pairs = [
                (y + 2 * m, y + 2 * (m + step)) for y in range(2) for m in range(columns - step)
            ]
            got, got_total = send(window, window_total, pairs)
            new_before = scale(jnp.exp(before_total), got) + before
            if 2 * step < columns:
                window = scale(jnp.exp(window_total), got) + window
                window_total = got_total + window_total
            before = new_before
            before_total = got_total + before_total
            step *= 2
    odd_entering = scale(jnp.exp(even_total), before) + even_state
    outgoing = jnp.where(row_zero, odd_entering, before)
    partner, _ = send(outgoing, totals, across)
    own_half = jnp.where(row_zero, before, odd_entering)
    first_half = jnp.where(row_zero, own_half, partner)
    second_half = jnp.where(row_zero, partner, own_half)
    return jnp.concatenate([first_half, second_half], axis=-2)


def shards(
    ssm_input,
    b_proj,
    c_proj,
    step_size,
    log_decay,
    skip_gain,
    request_of_slot,
    new_input,
    new_b,
    new_c,
    new_step,
    new_log_decay,
    out_weight,
):
    request_count = ssm_input.shape[0]
    count = lax.axis_size("ctx")
    place = lax.axis_index("ctx")
    terms = []
    for request in range(request_count):
        terms.append(
            block_terms(
                ssm_input[request],
                b_proj[request],
                c_proj[request],
                step_size[request],
                log_decay[request],
            )
        )
    totals = jnp.stack([term[1] for term in terms])
    states = jnp.stack([term[3] for term in terms])
    group_count, per_group = totals.shape[1], totals.shape[2]

    slots, steps = new_input.shape[0], new_input.shape[1]
    pieces = [totals, request_of_slot.astype(jnp.float32), new_c.astype(jnp.float32)]
    packed = jnp.concatenate([piece.reshape(-1) for piece in pieces])
    gathered = gather_ctx(packed[None])
    unpacked = []
    offset = 0
    for piece in pieces:
        size = piece.size
        unpacked.append(
            gathered[:, offset : offset + size].reshape((count,) + piece.shape)
        )
        offset += size
    all_totals, all_request, all_c = unpacked
    all_slots = count * slots
    all_request = all_request.reshape(all_slots)
    all_c = all_c.reshape(all_slots, steps, group_count, STATE)

    later = range_decay(all_totals, place + 1, count - 1)
    weighted_states = scale(later, states)
    high = weighted_states.astype(jnp.bfloat16)
    low = (weighted_states - high.astype(jnp.float32)).astype(jnp.bfloat16)
    c_rows = all_c.astype(jnp.bfloat16)
    projected = jnp.einsum(
        "rgkpn,jugn->rjugkp", high, c_rows, preferred_element_type=jnp.float32
    ) + jnp.einsum("rgkpn,jugn->rjugkp", low, c_rows, preferred_element_type=jnp.float32)
    contribution = projected[0]
    for request in range(1, request_count):
        pick = (all_request == request)[:, None, None, None, None]
        contribution = jnp.where(pick, projected[request], contribution)
    from_prompt = exchange_ctx(contribution, True)

    row_input = new_input.reshape(slots, steps, group_count, per_group, HEAD_DIM).astype(
        jnp.float32
    )
    row_b = new_b.reshape(slots, steps, group_count, STATE).astype(jnp.float32)
    row_c = new_c.reshape(slots, steps, group_count, STATE).astype(jnp.float32)
    row_step = new_step.reshape(slots, steps, group_count, per_group)
    row_logd = new_log_decay.reshape(slots, steps, group_count, per_group)
    cum_logd = jnp.cumsum(row_logd, axis=1)
    inner = jnp.einsum("jvgn,jugn->jvug", row_b, row_c, precision=HIGH)
    order_v = lax.broadcasted_iota(jnp.int32, (steps, steps), 0)
    order_u = lax.broadcasted_iota(jnp.int32, (steps, steps), 1)
    causal = (order_v <= order_u)[None, :, :, None, None]
    gap = cum_logd[:, None, :, :, :] - cum_logd[:, :, None, :, :]
    coefficient = jnp.where(
        causal, jnp.exp(jnp.where(causal, gap, 0.0)) * inner[..., None], 0.0
    ) * row_step[:, :, None, :, :]
    local_part = jnp.sum(coefficient[..., None] * row_input[:, :, None], axis=1)
    value = (
        jnp.exp(cum_logd)[..., None] * from_prompt
        + local_part
        + skip_gain.reshape(group_count, per_group, 1) * row_input
    )
    new_output = value.reshape(slots, steps, -1).astype(jnp.bfloat16)
    partial_value = jnp.einsum(
        "jup,pd->jud",
        exchange_ctx(jnp.concatenate([new_output] * count, axis=0), False),
        out_weight,
        preferred_element_type=jnp.float32,
    )
    if lax.axis_size("heads") == 2:
        other_half = lax.ppermute(partial_value, "heads", [(0, 1), (1, 0)])
        decoded = (partial_value + other_half).astype(jnp.bfloat16)
    else:
        decoded = lax.psum(partial_value, "heads").astype(jnp.bfloat16)

    entering = prefix_states(states, totals)
    prefill_out = finish(
        jnp.stack([term[2] for term in terms]),
        jnp.stack([term[0] for term in terms]),
        c_proj,
        entering,
        ssm_input,
        skip_gain,
    )
    return (prefill_out, decoded)


def solution(mesh):
    in_specs = (
        P("groups", "ctx", "heads"),
        P("groups", "ctx", "heads"),
        P("groups", "ctx", "heads"),
        P("groups", "heads", "ctx"),
        P("groups", "heads", "ctx"),
        P("heads"),
        P(("groups", "ctx")),
        P(("groups", "ctx"), None, "heads"),
        P(("groups", "ctx"), None, "heads"),
        P(("groups", "ctx"), None, "heads"),
        P(("groups", "ctx"), None, "heads"),
        P(("groups", "ctx"), None, "heads"),
        P("heads", "ctx"),
    )
    out_specs = (P("groups", "ctx", "heads"), P("groups", None, "ctx"))
    return jax.shard_map(shards, mesh=mesh, in_specs=in_specs, out_specs=out_specs, check_vma=False)
```

```python
import jax
import jax.numpy as jnp
from jax import lax
from jax.sharding import PartitionSpec as P

HEADS = 128
HEAD_DIM = 64
STATE = 128
GROUPS = 4

HIGH = lax.Precision.HIGHEST


def block_terms(block_input, block_b, block_c, block_step, block_logd):
    block_size = block_input.shape[0]
    head_count = block_step.shape[0]
    per_group = HEADS // GROUPS
    group_count = head_count // per_group
    cumulative = jnp.cumsum(block_logd, axis=1)
    block_total = cumulative[:, -1]
    inputs_head = block_input.reshape(block_size, group_count, per_group, HEAD_DIM)
    b_groups = block_b.reshape(block_size, group_count, STATE)
    c_groups = block_c.reshape(block_size, group_count, STATE)
    scores = jnp.einsum("tgn,sgn->gts", c_groups, b_groups, preferred_element_type=jnp.float32)
    row_index = lax.broadcasted_iota(jnp.int32, (block_size, block_size), 0)
    col_index = lax.broadcasted_iota(jnp.int32, (block_size, block_size), 1)
    causal = row_index >= col_index
    log_gap = cumulative[:, :, None] - cumulative[:, None, :]
    decay_rate = (
        jnp.where(causal, jnp.exp(jnp.where(causal, log_gap, 0.0)), 0.0) * block_step[:, None, :]
    )
    mixing = (
        scores[:, None, :, :] * decay_rate.reshape(group_count, per_group, block_size, block_size)
    ).astype(jnp.bfloat16)
    local_out = jnp.einsum(
        "gkts,sgkp->gktp", mixing, inputs_head, preferred_element_type=jnp.float32
    )
    weighting = jnp.exp(block_total[:, None] - cumulative) * block_step
    weighted = (weighting.T.reshape(block_size, group_count, per_group, 1) * inputs_head).astype(
        jnp.bfloat16
    )
    block_state = jnp.einsum(
        "sgkp,sgn->gkpn", weighted, b_groups, preferred_element_type=jnp.float32
    )
    return (cumulative, block_total.reshape(group_count, per_group), local_out, block_state)


def finish(local_out, cumulative, c_proj, entering, ssm_input, skip_gain):
    request_count, group_count, per_group, block_size = local_out.shape[:4]
    c_groups = c_proj.reshape(request_count, block_size, group_count, STATE)
    flat = entering.reshape(request_count, group_count, per_group * HEAD_DIM, STATE)
    high = flat.astype(jnp.bfloat16)
    low = (flat - high.astype(jnp.float32)).astype(jnp.bfloat16)
    numbers = (((3,), (3,)), ((0, 2), (0, 1)))
    carried = lax.dot_general(
        jnp.concatenate([c_groups, c_groups], axis=-1),
        jnp.concatenate([high, low], axis=-1),
        numbers,
        preferred_element_type=jnp.float32,
    )
    carried = carried.reshape(request_count, group_count, block_size, per_group, HEAD_DIM)
    growth = jnp.exp(cumulative).reshape(request_count, group_count, per_group, block_size)
    carried = carried * growth.transpose(0, 1, 3, 2)[..., None]
    inputs_head = ssm_input.reshape(
        request_count, block_size, group_count, per_group, HEAD_DIM
    ).astype(jnp.float32)
    skipped = skip_gain.reshape(group_count, per_group, 1) * inputs_head
    total = carried.transpose(0, 2, 1, 3, 4) + local_out.transpose(0, 3, 1, 2, 4) + skipped
    return total.reshape(request_count, block_size, -1).astype(jnp.bfloat16)


def range_decay(all_totals, low, high):
    place = lax.broadcasted_iota(jnp.int32, all_totals.shape, 0)
    keep = (place >= low) & (place <= high)
    return jnp.exp(jnp.sum(jnp.where(keep, all_totals, 0.0), axis=0))


def scale(factor, state):
    return factor[..., None, None] * state


def send(value, total, pairs):
    state, total = lax.ppermute((value.astype(jnp.bfloat16), total), "ctx", pairs)
    return state.astype(jnp.float32), total


def gather_ctx(value):
    count = lax.axis_size("ctx")
    if count & (count - 1):
        return lax.all_gather(value, "ctx", axis=0, tiled=True)
    place = lax.axis_index("ctx")
    reach = 1
    while reach < count:
        got = lax.ppermute(value, "ctx", [(i, i ^ reach) for i in range(count)])
        upper = (place & reach) != 0
        value = jnp.where(
            upper, jnp.concatenate([got, value], axis=0), jnp.concatenate([value, got], axis=0)
        )
        reach *= 2
    return value


def reduce_scatter_ctx(value):
    count = lax.axis_size("ctx")
    if count & (count - 1):
        return lax.psum_scatter(value, "ctx", scatter_dimension=0, tiled=True)
    place = lax.axis_index("ctx")
    reach = 1
    while reach < count:
        pairs = value.reshape((value.shape[0] // 2, 2) + value.shape[1:])
        upper = (place & reach) != 0
        keep = jnp.where(upper, pairs[:, 1], pairs[:, 0])
        give = jnp.where(upper, pairs[:, 0], pairs[:, 1])
        value = keep + lax.ppermute(give, "ctx", [(i, i ^ reach) for i in range(count)])
        reach *= 2
    return value


def exchange_ctx(value, total):
    count = lax.axis_size("ctx")
    got = lax.all_to_all(value, "ctx", 0, 0, tiled=True)
    got = got.reshape((count, value.shape[0] // count) + value.shape[1:])
    return jnp.sum(got, axis=0) if total else got.reshape(value.shape)


def chain_columns(window, window_total, column, columns):
    chunks = window.shape[0]
    growth = jnp.exp(window_total)
    entering = [jnp.zeros_like(window[k]) for k in range(chunks)]
    for stage in range(columns - 1 + chunks - 1):
        senders = [m for m in range(columns - 1) if 0 <= stage - m < chunks]
        pairs = [(y + 2 * m, y + 2 * (m + 1)) for y in range(2) for m in senders]
        outgoing = jnp.zeros_like(window[0])
        for k in range(chunks):
            leaving = scale(growth[k], entering[k]) + window[k]
            outgoing = jnp.where(stage - column == k, leaving, outgoing)
        got = lax.ppermute(outgoing.astype(jnp.bfloat16), "ctx", pairs).astype(jnp.float32)
        for k in range(chunks):
            entering[k] = jnp.where(stage - column + 1 == k, got, entering[k])
    return jnp.stack(entering)


def prefix_states(states, totals):
    count = lax.axis_size("ctx")
    columns = count // 2
    place = lax.axis_index("ctx")
    row_zero = place % 2 == 0
    column = place // 2
    half = states.shape[-2] // 2
    first = states[..., :half, :]
    second = states[..., half:, :]
    mine = jnp.where(row_zero, first, second)
    other = jnp.where(row_zero, second, first)
    across = [(2 * m, 2 * m + 1) for m in range(columns)] + [
        (2 * m + 1, 2 * m) for m in range(columns)
    ]
    received, partner_total = send(other, totals, across)
    even_state = jnp.where(row_zero, mine, received)
    odd_state = jnp.where(row_zero, received, mine)
    even_total = jnp.where(row_zero, totals, partner_total)
    odd_total = jnp.where(row_zero, partner_total, totals)
    window = scale(jnp.exp(odd_total), even_state) + odd_state
    window_total = even_total + odd_total
    if columns <= 4:
        before = chain_columns(window, window_total, column, columns)
    else:
        before = jnp.zeros_like(window)
        before_total = jnp.zeros_like(totals)
        step = 1
        while step < columns:
            pairs = [
                (y + 2 * m, y + 2 * (m + step)) for y in range(2) for m in range(columns - step)
            ]
            got, got_total = send(window, window_total, pairs)
            new_before = scale(jnp.exp(before_total), got) + before
            if 2 * step < columns:
                window = scale(jnp.exp(window_total), got) + window
                window_total = got_total + window_total
            before = new_before
            before_total = got_total + before_total
            step *= 2
    odd_entering = scale(jnp.exp(even_total), before) + even_state
    outgoing = jnp.where(row_zero, odd_entering, before)
    partner, _ = send(outgoing, totals, across)
    own_half = jnp.where(row_zero, before, odd_entering)
    first_half = jnp.where(row_zero, own_half, partner)
    second_half = jnp.where(row_zero, partner, own_half)
    return jnp.concatenate([first_half, second_half], axis=-2)


def shards(
    ssm_input,
    b_proj,
    c_proj,
    step_size,
    log_decay,
    skip_gain,
    request_of_slot,
    new_input,
    new_b,
    new_c,
    new_step,
    new_log_decay,
    out_weight,
):
    request_count = ssm_input.shape[0]
    count = lax.axis_size("ctx")
    place = lax.axis_index("ctx")
    terms = []
    for request in range(request_count):
        terms.append(
            block_terms(
                ssm_input[request],
                b_proj[request],
                c_proj[request],
                step_size[request],
                log_decay[request],
            )
        )
    totals = jnp.stack([term[1] for term in terms])
    states = jnp.stack([term[3] for term in terms])
    group_count, per_group = totals.shape[1], totals.shape[2]

    slots, steps = new_input.shape[0], new_input.shape[1]
    pieces = [totals, request_of_slot.astype(jnp.float32), new_c.astype(jnp.float32)]
    packed = jnp.concatenate([piece.reshape(-1) for piece in pieces])
    gathered = gather_ctx(packed[None])
    unpacked = []
    offset = 0
    for piece in pieces:
        size = piece.size
        unpacked.append(
            gathered[:, offset : offset + size].reshape((count,) + piece.shape)
        )
        offset += size
    all_totals, all_request, all_c = unpacked
    all_slots = count * slots
    all_request = all_request.reshape(all_slots)
    all_c = all_c.reshape(all_slots, steps, group_count, STATE)

    later = range_decay(all_totals, place + 1, count - 1)
    weighted_states = scale(later, states)
    high = weighted_states.astype(jnp.bfloat16)
    low = (weighted_states - high.astype(jnp.float32)).astype(jnp.bfloat16)
    c_rows = all_c.astype(jnp.bfloat16)
    projected = jnp.einsum(
        "rgkpn,jugn->rjugkp",
        jnp.concatenate([high, low], axis=-1),
        jnp.concatenate([c_rows, c_rows], axis=-1),
        preferred_element_type=jnp.float32,
    )
    contribution = projected[0]
    for request in range(1, request_count):
        pick = (all_request == request)[:, None, None, None, None]
        contribution = jnp.where(pick, projected[request], contribution)
    from_prompt = exchange_ctx(contribution, True)

    row_input = new_input.reshape(slots, steps, group_count, per_group, HEAD_DIM).astype(
        jnp.float32
    )
    row_b = new_b.reshape(slots, steps, group_count, STATE).astype(jnp.float32)
    row_c = new_c.reshape(slots, steps, group_count, STATE).astype(jnp.float32)
    row_step = new_step.reshape(slots, steps, group_count, per_group)
    row_logd = new_log_decay.reshape(slots, steps, group_count, per_group)
    cum_logd = jnp.cumsum(row_logd, axis=1)
    inner = jnp.einsum("jvgn,jugn->jvug", row_b, row_c, precision=HIGH)
    order_v = lax.broadcasted_iota(jnp.int32, (steps, steps), 0)
    order_u = lax.broadcasted_iota(jnp.int32, (steps, steps), 1)
    causal = (order_v <= order_u)[None, :, :, None, None]
    gap = cum_logd[:, None, :, :, :] - cum_logd[:, :, None, :, :]
    coefficient = jnp.where(
        causal, jnp.exp(jnp.where(causal, gap, 0.0)) * inner[..., None], 0.0
    ) * row_step[:, :, None, :, :]
    local_part = jnp.sum(coefficient[..., None] * row_input[:, :, None], axis=1)
    value = (
        jnp.exp(cum_logd)[..., None] * from_prompt
        + local_part
        + skip_gain.reshape(group_count, per_group, 1) * row_input
    )
    new_output = value.reshape(slots, steps, -1).astype(jnp.bfloat16)
    partial_value = jnp.einsum(
        "jup,pd->jud",
        exchange_ctx(jnp.concatenate([new_output] * count, axis=0), False),
        out_weight,
        preferred_element_type=jnp.float32,
    )
    if lax.axis_size("heads") == 2:
        other_half = lax.ppermute(partial_value, "heads", [(0, 1), (1, 0)])
        decoded = (partial_value + other_half).astype(jnp.bfloat16)
    else:
        decoded = lax.psum(partial_value, "heads").astype(jnp.bfloat16)

    entering = prefix_states(states, totals)
    prefill_out = finish(
        jnp.stack([term[2] for term in terms]),
        jnp.stack([term[0] for term in terms]),
        c_proj,
        entering,
        ssm_input,
        skip_gain,
    )
    return (prefill_out, decoded)


def solution(mesh):
    in_specs = (
        P("groups", "ctx", "heads"),
        P("groups", "ctx", "heads"),
        P("groups", "ctx", "heads"),
        P("groups", "heads", "ctx"),
        P("groups", "heads", "ctx"),
        P("heads"),
        P(("groups", "ctx")),
        P(("groups", "ctx"), None, "heads"),
        P(("groups", "ctx"), None, "heads"),
        P(("groups", "ctx"), None, "heads"),
        P(("groups", "ctx"), None, "heads"),
        P(("groups", "ctx"), None, "heads"),
        P("heads", "ctx"),
    )
    out_specs = (P("groups", "ctx", "heads"), P("groups", None, "ctx"))
    return jax.shard_map(shards, mesh=mesh, in_specs=in_specs, out_specs=out_specs, check_vma=False)
```
